512 devices in a mesh: panel: 64 (over y, z), point: 8 (over x, core).
Axes of the slice: x: 4, y: 8, z: 8, core: 2. Of those that a mesh axis runs over, the one named last changes fastest.
Arguments:
- node_velocity: float32 [2, 1048576], P(None, ('panel', 'point')), may hold values from -1.5 to 1.5
- node_owner: int32 [1048576, 1], P(('panel', 'point')), may hold values from 0 to 63; in each aligned block of 2048 rows (0 to 2047, 2048 to 4095, ...) at most 64 rows name the same one
- node_panel: int32 [1048576], P(('panel', 'point')), may hold values from 0 to 127
- panel_centroid: float32 [3, 8192], P(None, 'panel'), may hold values from -1 to 1
- panel_area: float32 [8192], P('panel'), may hold values from 0.05 to 0.5
- field_points: float32 [3, 65536], P(None, ('panel', 'point')), may hold values from 1.2 to 3
Outputs:
- pressure: float32 [2, 65536], P(None, ('panel', 'point'))
The draws below stay inside these ranges and needn't reach their ends.
Inputs may be any that keep to these rules, and one draw needn't show every extreme that they name: `node_owner`: among the rows of one device at most 64 name the same owner, a bound that some block reaches.
All inputs are finite; a program needn't handle non-finite values.
Results may differ from the reference program's by a relative error of at most 0.0003.
Values sent between devices are 32-bit elements; how exact they have to be, the bound alone decides.
No kernel may reach another device: no remote copies, remote signals or barrier semaphores. Data moves between devices by JAX's collectives and lax.ppermute only.
A program may use at most 64 MiB of HBM per device.

```python
import math
import jax
import jax.numpy as jnp
import numpy as np
from jax import lax

ROW_DEV = 2048
PAN_DEV = 128
CAP = 64
ROWS = 1048576
PANELS = 8192
FIELD = 65536
N_PANEL = 64


def plant(array, key, low, largest):
    longest = array.shape.index(max(array.shape))
    spots = []
    for shift in (0, 1):
        where = [jax.random.randint(jax.random.fold_in(key, axis), (), 0, length) for axis, length in enumerate(array.shape)]
        where[longest] = (where[longest] + shift) % array.shape[longest]
        spots.append(tuple(where))
    return array.at[spots[0]].set(low).at[spots[1]].set(largest)


def block_scale(key, extent, shards, smallest, largest):
    factor_of = 1.0
    for position, blocks in shards:
        steps = jax.random.uniform(jax.random.fold_in(jax.random.fold_in(key, 6), position), (blocks,), jnp.float32, smallest / len(shards), largest / len(shards))
        factor_of = factor_of * jnp.repeat(jnp.exp(steps), extent[position] // blocks).reshape((-1,) + (1,) * (len(extent) - 1 - position))
    return factor_of


def shared_out(key, own, number, rows, count, top, limit, slope):
    order = jax.random.permutation(key, count)
    crowded, common = shares(count, rows * top, limit, slope, True), shares(count, rows * top, limit, slope, False)
    places = jnp.arange(count)

    def named(sizes, turn):
        used = int((sizes > 0).sum())
        fixed = max(1, used // 4)
        shifted = fixed + (places - fixed + turn * (used - fixed)) % max(1, count - fixed)
        return jnp.zeros((count,), jnp.int32).at[order[jnp.where(places < fixed, places, shifted)]].set(jnp.asarray(sizes, jnp.int32))

    sizes = jnp.where(number % 4 == 0, named(crowded, number // 4), named(common, number - number // 4 - 1))
    mixed = jax.random.permutation(jax.random.fold_in(own, 3), count)
    giver, sink = mixed[0:count // 2 * 2:2], mixed[1:count // 2 * 2:2]
    slack = jnp.minimum(sizes[giver] - 1, limit - sizes[sink]) // 2
    slack = jnp.where((giver == order[0]) | (sink == order[0]) | (sizes[sink] == 0), 0, jnp.maximum(slack, 0))
    shifted = jax.random.randint(jax.random.fold_in(own, 4), (count // 2,), 0, 1 << 20) % (slack + 1)
    sizes = sizes.at[giver].add(-shifted).at[sink].add(shifted)
    members = jnp.searchsorted(jnp.cumsum(sizes), jnp.arange(rows * top), side="right").astype(jnp.int32)
    listing = members.reshape(top, rows).T
    listing = listing[jax.random.permutation(jax.random.fold_in(own, 1), rows)]
    turn = jax.random.randint(jax.random.fold_in(own, 2), (rows, 1), 0, top)
    return jnp.take_along_axis(listing, (jnp.arange(top)[None, :] + turn) % top, axis=1)


def shares(count, total, reach, skew, full):
    weights = [(1 << 20) // math.isqrt(standing ** skew) + 1 for standing in range(1, count + 1)]
    largest = reach if full else min(reach, max(-(-total // count), total * weights[0] // sum(weights)))
    least = 1 if total - largest >= count - 1 else 0
    counts, surplus = [largest] + [least] * (count - 1), total - largest - least * (count - 1)
    while surplus > 0:
        candidates = [i for i in range(1, count) if counts[i] < largest] or [i for i in range(1, count) if counts[i] < reach]
        mass, left = sum([weights[i] for i in candidates]), surplus
        for i in candidates:
            extra = min(reach - counts[i], max(1, left * weights[i] // mass), surplus)
            counts[i] = counts[i] + extra
            surplus = surplus - extra
    return np.array(counts)


def noise(rng, dims, width, most, shards=(), held_as=jnp.bfloat16):
    factor_of = block_scale(rng, dims, shards, -0.22, 0.18) if shards else 1.0
    drawn = jax.random.normal(rng, dims, jnp.float32) * width * factor_of
    return jnp.minimum(jnp.maximum(drawn, -most), most).astype(held_as)


def setup_inputs(seed: int = 0) -> dict:
    keys = jax.random.split(jax.random.key(seed), 7)
    node_velocity = noise(keys[0], (2, ROWS), 0.25, 1.5, ((1, 512),), jnp.float32)
    node_owner_keys = jax.random.split(jax.random.fold_in(keys[1], 1), ROWS // ROW_DEV)
    node_owner_turns = jax.random.permutation(jax.random.fold_in(keys[1], 3), ROWS // ROW_DEV)
    node_owner = jax.vmap(lambda own, number: shared_out(jax.random.fold_in(keys[1], 2), own, number, ROW_DEV, N_PANEL, 1, CAP, 2))(node_owner_keys, node_owner_turns).reshape((ROWS, 1))
    node_panel = plant(jax.random.randint(keys[2], (ROWS,), 0, PAN_DEV), jax.random.fold_in(keys[2], 1), 0, PAN_DEV - 1).astype(jnp.int32)
    panel_centroid = jnp.clip(jax.random.uniform(keys[3], (3, PANELS), jnp.float32, -1.0, 1.0) * block_scale(keys[3], (3, PANELS), ((1, 64),), -0.4, 0.0), -1.0, 1.0)
    panel_area = jnp.clip(jnp.exp(math.log(0.5) - 2.3025851 * jax.random.uniform(keys[4], (PANELS,), jnp.float32) ** block_scale(keys[4], (PANELS,), ((0, 64),), -0.2, 0.2)), 0.05, 0.5)
    field_points = jnp.clip(1.2 + 1.8 * jax.random.uniform(keys[5], (3, FIELD), jnp.float32) ** block_scale(keys[5], (3, FIELD), ((1, 512),), -0.2, 0.2), 1.2, 3.0)
    return dict(node_velocity=node_velocity, node_owner=node_owner, node_panel=node_panel, panel_centroid=panel_centroid, panel_area=panel_area, field_points=field_points)


WAVENUMBER = 40.0
FOUR_PI = 4.0 * math.pi

def green_block(centers, strength, points):
    delta_x = points[0][None, :] - centers[0][:, None]
    delta_y = points[1][None, :] - centers[1][:, None]
    delta_z = points[2][None, :] - centers[2][:, None]
    distance = jnp.sqrt(delta_x * delta_x + delta_y * delta_y + delta_z * delta_z)
    inverse = 1.0 / (FOUR_PI * distance)
    phase_angle = WAVENUMBER * distance
    cosine_part = jnp.cos(phase_angle) * inverse
    sine_part = jnp.sin(phase_angle) * inverse
    with_cosine = jnp.dot(strength, cosine_part, precision=lax.Precision.HIGHEST, preferred_element_type=jnp.float32)
    with_sine = jnp.dot(strength, sine_part, precision=lax.Precision.HIGHEST, preferred_element_type=jnp.float32)
    return jnp.stack([with_cosine[0] - with_sine[1], with_sine[0] + with_cosine[1]])

def reference(node_velocity, node_owner, node_panel, panel_centroid, panel_area, field_points):
    panel_index = (node_owner[:, 0] * PAN_DEV + node_panel).astype(jnp.int32)
    summed = jax.ops.segment_sum(node_velocity.T, panel_index, num_segments=PANELS)
    strength = jnp.stack([-panel_area * summed[:, 1], panel_area * summed[:, 0]])
    block_size = 1024
    block_count = FIELD // block_size
    grouped = field_points.reshape(3, block_count, block_size).transpose(1, 0, 2)
    result = lax.map(lambda points: green_block(panel_centroid, strength, points), grouped)
    return result.transpose(1, 0, 2).reshape(2, FIELD)
```

```python
import math

import jax
import jax.numpy as jnp
from jax import lax
from jax.sharding import PartitionSpec as P

WAVENUMBER = 40.0
FOUR_PI = 4.0 * math.pi


def green_points(centers, strength, points):
    delta_x = points[0][None, :] - centers[0][:, None]
    delta_y = points[1][None, :] - centers[1][:, None]
    delta_z = points[2][None, :] - centers[2][:, None]
    distance = jnp.sqrt(delta_x * delta_x + delta_y * delta_y + delta_z * delta_z)
    inverse = 1.0 / (FOUR_PI * distance)
    phase_angle = WAVENUMBER * distance
    cosine_part = jnp.cos(phase_angle) * inverse
    sine_part = jnp.sin(phase_angle) * inverse
    real = strength[0][:, None] * cosine_part - strength[1][:, None] * sine_part
    imag = strength[0][:, None] * sine_part + strength[1][:, None] * cosine_part
    return jnp.stack([jnp.sum(real, axis=0), jnp.sum(imag, axis=0)])


def shards(node_velocity, node_owner, node_panel, panel_centroid, panel_area, field_points):
    slab_count = lax.axis_size("panel")
    slab_width = panel_area.shape[0]
    destination = node_owner[:, 0]
    owner_hot = (destination[None, :] == jnp.arange(slab_count, dtype=jnp.int32)[:, None]).astype(
        jnp.float32
    )
    weighted = (node_velocity[:, None, :] * owner_hot[None, :, :]).reshape(2 * slab_count, -1)
    panel_hot = (node_panel[:, None] == jnp.arange(slab_width, dtype=jnp.int32)[None, :]).astype(
        jnp.float32
    )
    partial = jnp.dot(
        weighted, panel_hot, precision=lax.Precision.HIGHEST, preferred_element_type=jnp.float32
    )
    partial = partial.reshape(2, slab_count, slab_width).transpose(1, 0, 2)
    got = lax.all_to_all(partial, "panel", split_axis=0, concat_axis=0, tiled=True)
    velocity = lax.psum(jnp.sum(got, axis=0), "point")
    strength = jnp.stack([-panel_area * velocity[1], panel_area * velocity[0]])
    packed = jnp.concatenate([strength, panel_centroid], axis=0)
    spread = jnp.broadcast_to(packed[None], (slab_count,) + packed.shape)
    gathered = lax.all_to_all(spread, "panel", split_axis=0, concat_axis=0, tiled=True)
    every = gathered.transpose(1, 0, 2).reshape(packed.shape[0], -1)
    return green_points(every[2:5], every[0:2], field_points)


def solution(mesh):
    return jax.shard_map(
        shards,
        mesh=mesh,
        in_specs=(
            P(None, ("panel", "point")),
            P(("panel", "point"), None),
            P(("panel", "point")),
            P(None, "panel"),
            P("panel"),
            P(None, ("panel", "point")),
        ),
        out_specs=P(None, ("panel", "point")),
        check_vma=False,
    )
```

```python
import math

import jax
import jax.numpy as jnp
from jax import lax
from jax.sharding import PartitionSpec as P

WAVENUMBER = 40.0
FOUR_PI = 4.0 * math.pi


def green_points(centers, strength, points):
    delta_x = points[0][None, :] - centers[0][:, None]
    delta_y = points[1][None, :] - centers[1][:, None]
    delta_z = points[2][None, :] - centers[2][:, None]
    distance = jnp.sqrt(delta_x * delta_x + delta_y * delta_y + delta_z * delta_z)
    inverse = 1.0 / (FOUR_PI * distance)
    phase_angle = WAVENUMBER * distance
    cosine_part = jnp.cos(phase_angle) * inverse
    sine_part = jnp.sin(phase_angle) * inverse
    real = strength[0][:, None] * cosine_part - strength[1][:, None] * sine_part
    imag = strength[0][:, None] * sine_part + strength[1][:, None] * cosine_part
    return jnp.stack([jnp.sum(real, axis=0), jnp.sum(imag, axis=0)])


def shards(node_velocity, node_owner, node_panel, panel_centroid, panel_area, field_points):
    slab_count = lax.axis_size("panel")
    slab_width = panel_area.shape[0]
    destination = node_owner[:, 0]
    owner_hot = (destination[None, :] == jnp.arange(slab_count, dtype=jnp.int32)[:, None]).astype(
        jnp.float32
    )
    weighted = (node_velocity[:, None, :] * owner_hot[None, :, :]).reshape(2 * slab_count, -1)
    panel_hot = (node_panel[:, None] == jnp.arange(slab_width, dtype=jnp.int32)[None, :]).astype(
        jnp.float32
    )
    partial = jnp.dot(
        weighted, panel_hot, precision=lax.Precision.HIGHEST, preferred_element_type=jnp.float32
    )
    group = ("panel", "point")
    device_count = slab_count * lax.axis_size("point")
    share = slab_count * slab_width // device_count
    partial = partial.reshape(2, device_count, share).transpose(1, 0, 2)
    got = lax.all_to_all(partial, group, split_axis=0, concat_axis=0, tiled=True)
    velocity = jnp.sum(got, axis=0)
    start = lax.axis_index("point") * share
    area = lax.dynamic_slice_in_dim(panel_area, start, share)
    centroid = lax.dynamic_slice_in_dim(panel_centroid, start, share, axis=1)
    strength = jnp.stack([-area * velocity[1], area * velocity[0]])
    packed = jnp.concatenate([strength, centroid], axis=0)
    spread = jnp.broadcast_to(packed[None], (device_count,) + packed.shape)
    gathered = lax.all_to_all(spread, group, split_axis=0, concat_axis=0, tiled=True)
    every = gathered.transpose(1, 0, 2).reshape(packed.shape[0], -1)
    return green_points(every[2:5], every[0:2], field_points)


def solution(mesh):
    return jax.shard_map(
        shards,
        mesh=mesh,
        in_specs=(
            P(None, ("panel", "point")),
            P(("panel", "point"), None),
            P(("panel", "point")),
            P(None, "panel"),
            P("panel"),
            P(None, ("panel", "point")),
        ),
        out_specs=P(None, ("panel", "point")),
        check_vma=False,
    )
```

```python
import math

import jax
import jax.numpy as jnp
from jax import lax
from jax.sharding import PartitionSpec as P

WAVENUMBER = 40.0
FOUR_PI = 4.0 * math.pi


def kernel_parts(centers, points):
    delta_x = points[0][None, :] - centers[0][:, None]
    delta_y = points[1][None, :] - centers[1][:, None]
    delta_z = points[2][None, :] - centers[2][:, None]
    distance = jnp.sqrt(delta_x * delta_x + delta_y * delta_y + delta_z * delta_z)
    inverse = 1.0 / (FOUR_PI * distance)
    phase_angle = WAVENUMBER * distance
    return jnp.cos(phase_angle) * inverse, jnp.sin(phase_angle) * inverse


def contract(strength, cosine_part, sine_part):
    real = strength[0][:, None] * cosine_part - strength[1][:, None] * sine_part
    imag = strength[0][:, None] * sine_part + strength[1][:, None] * cosine_part
    return jnp.stack([jnp.sum(real, axis=0), jnp.sum(imag, axis=0)])


def shards(node_velocity, node_owner, node_panel, panel_centroid, panel_area, field_points):
    slab_count = lax.axis_size("panel")
    slab_width = panel_area.shape[0]
    destination = node_owner[:, 0]
    owner_hot = (destination[None, :] == jnp.arange(slab_count, dtype=jnp.int32)[:, None]).astype(
        jnp.float32
    )
    weighted = (node_velocity[:, None, :] * owner_hot[None, :, :]).reshape(2 * slab_count, -1)
    panel_hot = (node_panel[:, None] == jnp.arange(slab_width, dtype=jnp.int32)[None, :]).astype(
        jnp.float32
    )
    partial = jnp.dot(
        weighted, panel_hot, precision=lax.Precision.HIGHEST, preferred_element_type=jnp.float32
    )
    partial = partial.reshape(2, slab_count, slab_width).transpose(1, 0, 2)
    centroid_copies = jnp.broadcast_to(panel_centroid[None], (slab_count,) + panel_centroid.shape)
    outgoing = jnp.concatenate([partial, centroid_copies], axis=1)
    got = lax.all_to_all(outgoing, "panel", split_axis=0, concat_axis=0, tiled=True)
    velocity = lax.psum(jnp.sum(got[:, 0:2], axis=0), "point")
    centers = got[:, 2:5].transpose(1, 0, 2).reshape(3, -1)
    cosine_part, sine_part = lax.optimization_barrier(kernel_parts(centers, field_points))
    strength = jnp.stack([-panel_area * velocity[1], panel_area * velocity[0]])
    spread = jnp.broadcast_to(strength[None], (slab_count,) + strength.shape)
    gathered = lax.all_to_all(spread, "panel", split_axis=0, concat_axis=0, tiled=True)
    every = gathered.transpose(1, 0, 2).reshape(2, -1)
    return contract(every, cosine_part, sine_part)


def solution(mesh):
    return jax.shard_map(
        shards,
        mesh=mesh,
        in_specs=(
            P(None, ("panel", "point")),
            P(("panel", "point"), None),
            P(("panel", "point")),
            P(None, "panel"),
            P("panel"),
            P(None, ("panel", "point")),
        ),
        out_specs=P(None, ("panel", "point")),
        check_vma=False,
    )
```

```python
import math

import jax
import jax.numpy as jnp
from jax import lax
from jax.sharding import PartitionSpec as P

WAVENUMBER = 40.0
FOUR_PI = 4.0 * math.pi


def green_points(centers, strength, points):
    delta_x = points[0][None, :] - centers[0][:, None]
    delta_y = points[1][None, :] - centers[1][:, None]
    delta_z = points[2][None, :] - centers[2][:, None]
    distance = jnp.sqrt(delta_x * delta_x + delta_y * delta_y + delta_z * delta_z)
    inverse = 1.0 / (FOUR_PI * distance)
    phase_angle = WAVENUMBER * distance
    cosine_part = jnp.cos(phase_angle) * inverse
    sine_part = jnp.sin(phase_angle) * inverse
    real = strength[0][:, None] * cosine_part - strength[1][:, None] * sine_part
    imag = strength[0][:, None] * sine_part + strength[1][:, None] * cosine_part
    return jnp.stack([jnp.sum(real, axis=0), jnp.sum(imag, axis=0)])


def shards(node_velocity, node_owner, node_panel, panel_centroid, panel_area, field_points):
    slab_count = lax.axis_size("panel")
    slab_width = panel_area.shape[0]
    destination = node_owner[:, 0]
    owner_hot = (destination[None, :] == jnp.arange(slab_count, dtype=jnp.int32)[:, None]).astype(
        jnp.float32
    )
    weighted = (node_velocity[:, None, :] * owner_hot[None, :, :]).reshape(2 * slab_count, -1)
    panel_hot = (node_panel[:, None] == jnp.arange(slab_width, dtype=jnp.int32)[None, :]).astype(
        jnp.float32
    )
    partial = jnp.dot(
        weighted, panel_hot, precision=lax.Precision.HIGHEST, preferred_element_type=jnp.float32
    )
    partial = partial.reshape(2, slab_count, slab_width).transpose(1, 0, 2)
    got = lax.all_to_all(partial, "panel", split_axis=0, concat_axis=0, tiled=True)
    column = jnp.sum(got, axis=0)
    point_count = lax.axis_size("point")
    copies = jnp.broadcast_to(column[None], (point_count,) + column.shape)
    velocity = jnp.sum(lax.all_to_all(copies, "point", split_axis=0, concat_axis=0, tiled=True), axis=0)
    strength = jnp.stack([-panel_area * velocity[1], panel_area * velocity[0]])
    packed = jnp.concatenate([strength, panel_centroid], axis=0)
    spread = jnp.broadcast_to(packed[None], (slab_count,) + packed.shape)
    gathered = lax.all_to_all(spread, "panel", split_axis=0, concat_axis=0, tiled=True)
    every = gathered.transpose(1, 0, 2).reshape(packed.shape[0], -1)
    return green_points(every[2:5], every[0:2], field_points)


def solution(mesh):
    return jax.shard_map(
        shards,
        mesh=mesh,
        in_specs=(
            P(None, ("panel", "point")),
            P(("panel", "point"), None),
            P(("panel", "point")),
            P(None, "panel"),
            P("panel"),
            P(None, ("panel", "point")),
        ),
        out_specs=P(None, ("panel", "point")),
        check_vma=False,
    )
```

```python
import math

import jax
import jax.numpy as jnp
from jax import lax
from jax.experimental import pallas as pl
from jax.experimental.pallas import tpu as pltpu
from jax.sharding import PartitionSpec as P

WAVENUMBER = 40.0
FOUR_PI = 4.0 * math.pi


TWO_OVER_PI = 2.0 / math.pi
HALF_PI_1 = 1.5703125
HALF_PI_2 = 4.837512969970703125e-4
HALF_PI_3 = 7.54978995489188216e-8
GROUP = 16


def sine_cosine(angle):
    turns = jnp.floor(angle * TWO_OVER_PI + 0.5)
    rest = ((angle - turns * HALF_PI_1) - turns * HALF_PI_2) - turns * HALF_PI_3
    square = rest * rest
    sine = rest + rest * square * (
        -1.6666654611e-1 + square * (8.3321608736e-3 + square * -1.9515295891e-4)
    )
    cosine = 1.0 - 0.5 * square + square * square * (
        4.166664568298827e-2 + square * (-1.388731625493765e-3 + square * 2.443315711809948e-5)
    )
    quadrant = turns.astype(jnp.int32)
    swap = (quadrant & 1) == 1
    sine_out = jnp.where(swap, cosine, sine)
    cosine_out = jnp.where(swap, sine, cosine)
    sine_out = jnp.where((quadrant & 2) == 2, -sine_out, sine_out)
    cosine_out = jnp.where(((quadrant + 1) & 2) == 2, -cosine_out, cosine_out)
    return sine_out, cosine_out


def green_kernel(panel_ref, point_ref, out_ref, total_ref):
    chunks = panel_ref.shape[0]
    points = point_ref.shape[1]
    for group in range(points // GROUP):
        rows = pl.ds(group * GROUP, GROUP)
        point_x = point_ref[0, rows, :]
        point_y = point_ref[1, rows, :]
        point_z = point_ref[2, rows, :]

        def body(chunk, carry):
            real_sum, imag_sum = carry
            block = panel_ref[chunk]
            shape = (GROUP, block.shape[1])
            strength_re = jnp.broadcast_to(block[0:1], shape)
            strength_im = jnp.broadcast_to(block[1:2], shape)
            delta_x = point_x - jnp.broadcast_to(block[2:3], shape)
            delta_y = point_y - jnp.broadcast_to(block[3:4], shape)
            delta_z = point_z - jnp.broadcast_to(block[4:5], shape)
            distance = jnp.sqrt(delta_x * delta_x + delta_y * delta_y + delta_z * delta_z)
            inverse = 1.0 / (FOUR_PI * distance)
            sine, cosine = sine_cosine(WAVENUMBER * distance)
            cosine_part = cosine * inverse
            sine_part = sine * inverse
            real_sum = real_sum + (strength_re * cosine_part - strength_im * sine_part)
            imag_sum = imag_sum + (strength_re * sine_part + strength_im * cosine_part)
            return real_sum, imag_sum

        zero = jnp.zeros((GROUP, panel_ref.shape[2]), jnp.float32)
        real_sum, imag_sum = lax.fori_loop(0, chunks, body, (zero, zero), unroll=2)
        total_ref[0, rows, :] = real_sum
        total_ref[1, rows, :] = imag_sum
    out_ref[0:1, :] = jnp.sum(total_ref[0].T, axis=0, keepdims=True)
    out_ref[1:2, :] = jnp.sum(total_ref[1].T, axis=0, keepdims=True)


def green(panels, field_points):
    points = field_points.shape[1]
    lanes = panels.shape[2]
    spread = jnp.broadcast_to(field_points[:, :, None], (3, points, lanes))
    pairs = panels.shape[0] * lanes * points
    return pl.pallas_call(
        green_kernel,
        out_shape=jax.ShapeDtypeStruct((2, points), jnp.float32),
        in_specs=[pl.BlockSpec(memory_space=pltpu.VMEM)] * 2,
        out_specs=pl.BlockSpec(memory_space=pltpu.VMEM),
        scratch_shapes=[pltpu.VMEM((2, points, lanes), jnp.float32)],
        cost_estimate=pl.CostEstimate(flops=70 * pairs, transcendentals=2 * pairs, bytes_accessed=4 * (panels.size + spread.size + 2 * points)),
    )(panels, spread)


def shards(node_velocity, node_owner, node_panel, panel_centroid, panel_area, field_points):
    slab_count = lax.axis_size("panel")
    slab_width = panel_area.shape[0]
    destination = node_owner[:, 0]
    owner_hot = (destination[None, :] == jnp.arange(slab_count, dtype=jnp.int32)[:, None]).astype(
        jnp.float32
    )
    weighted = (node_velocity[:, None, :] * owner_hot[None, :, :]).reshape(2 * slab_count, -1)
    panel_hot = (node_panel[:, None] == jnp.arange(slab_width, dtype=jnp.int32)[None, :]).astype(
        jnp.float32
    )
    partial = jnp.dot(
        weighted, panel_hot, precision=lax.Precision.HIGHEST, preferred_element_type=jnp.float32
    )
    partial = partial.reshape(2, slab_count, slab_width).transpose(1, 0, 2)
    got = lax.all_to_all(partial, "panel", split_axis=0, concat_axis=0, tiled=True)
    column = jnp.sum(got, axis=0)
    point_count = lax.axis_size("point")
    copies = jnp.broadcast_to(column[None], (point_count,) + column.shape)
    velocity = jnp.sum(lax.all_to_all(copies, "point", split_axis=0, concat_axis=0, tiled=True), axis=0)
    strength = jnp.stack([-panel_area * velocity[1], panel_area * velocity[0]])
    packed = jnp.concatenate([strength, panel_centroid], axis=0)
    spread = jnp.broadcast_to(packed[None], (slab_count,) + packed.shape)
    gathered = lax.all_to_all(spread, "panel", split_axis=0, concat_axis=0, tiled=True)
    return green(gathered, field_points)


def solution(mesh):
    return jax.shard_map(
        shards,
        mesh=mesh,
        in_specs=(
            P(None, ("panel", "point")),
            P(("panel", "point"), None),
            P(("panel", "point")),
            P(None, "panel"),
            P("panel"),
            P(None, ("panel", "point")),
        ),
        out_specs=P(None, ("panel", "point")),
        check_vma=False,
    )
```

```python
import math

import jax
import jax.numpy as jnp
from jax import lax
from jax.experimental import pallas as pl
from jax.experimental.pallas import tpu as pltpu
from jax.sharding import PartitionSpec as P

WAVENUMBER = 40.0
FOUR_PI = 4.0 * math.pi


TWO_OVER_PI = 2.0 / math.pi
HALF_PI_1 = 1.5703125
HALF_PI_2 = 4.837512969970703125e-4
HALF_PI_3 = 7.54978995489188216e-8
GROUP = 16


def sine_cosine(angle):
    turns = jnp.floor(angle * TWO_OVER_PI + 0.5)
    rest = ((angle - turns * HALF_PI_1) - turns * HALF_PI_2) - turns * HALF_PI_3
    square = rest * rest
    sine = rest + rest * square * (
        -1.6666654611e-1 + square * (8.3321608736e-3 + square * -1.9515295891e-4)
    )
    cosine = 1.0 - 0.5 * square + square * square * (
        4.166664568298827e-2 + square * (-1.388731625493765e-3 + square * 2.443315711809948e-5)
    )
    quadrant = turns.astype(jnp.int32)
    swap = (quadrant & 1) == 1
    sine_out = jnp.where(swap, cosine, sine)
    cosine_out = jnp.where(swap, sine, cosine)
    sine_out = jnp.where((quadrant & 2) == 2, -sine_out, sine_out)
    cosine_out = jnp.where(((quadrant + 1) & 2) == 2, -cosine_out, cosine_out)
    return sine_out, cosine_out


def green_kernel(panel_ref, point_ref, out_ref, total_ref):
    chunks = panel_ref.shape[0]
    points = point_ref.shape[1]
    for group in range(points // GROUP):
        rows = pl.ds(group * GROUP, GROUP)
        point_x = point_ref[0, rows, :]
        point_y = point_ref[1, rows, :]
        point_z = point_ref[2, rows, :]

        def body(chunk, carry):
            real_sum, imag_sum = carry
            block = panel_ref[chunk]
            shape = (GROUP, block.shape[1])
            strength_re = jnp.broadcast_to(block[0:1], shape)
            strength_im = jnp.broadcast_to(block[1:2], shape)
            delta_x = point_x - jnp.broadcast_to(block[2:3], shape)
            delta_y = point_y - jnp.broadcast_to(block[3:4], shape)
            delta_z = point_z - jnp.broadcast_to(block[4:5], shape)
            distance = jnp.sqrt(delta_x * delta_x + delta_y * delta_y + delta_z * delta_z)
            inverse = 1.0 / (FOUR_PI * distance)
            sine, cosine = sine_cosine(WAVENUMBER * distance)
            cosine_part = cosine * inverse
            sine_part = sine * inverse
            real_sum = real_sum + (strength_re * cosine_part - strength_im * sine_part)
            imag_sum = imag_sum + (strength_re * sine_part + strength_im * cosine_part)
            return real_sum, imag_sum

        zero = jnp.zeros((GROUP, panel_ref.shape[2]), jnp.float32)
        real_sum, imag_sum = lax.fori_loop(0, chunks, body, (zero, zero), unroll=2)
        total_ref[0, rows, :] = real_sum
        total_ref[1, rows, :] = imag_sum
    out_ref[0:1, :] = jnp.sum(total_ref[0].T, axis=0, keepdims=True)
    out_ref[1:2, :] = jnp.sum(total_ref[1].T, axis=0, keepdims=True)


def green(panels, field_points):
    points = field_points.shape[1]
    lanes = panels.shape[2]
    spread = jnp.broadcast_to(field_points[:, :, None], (3, points, lanes))
    pairs = panels.shape[0] * lanes * points
    return pl.pallas_call(
        green_kernel,
        out_shape=jax.ShapeDtypeStruct((2, points), jnp.float32),
        in_specs=[pl.BlockSpec(memory_space=pltpu.VMEM)] * 2,
        out_specs=pl.BlockSpec(memory_space=pltpu.VMEM),
        scratch_shapes=[pltpu.VMEM((2, points, lanes), jnp.float32)],
        cost_estimate=pl.CostEstimate(flops=70 * pairs, transcendentals=2 * pairs, bytes_accessed=4 * (panels.size + spread.size + 2 * points)),
    )(panels, spread)


def parts_kernel(panel_ref, point_ref, cosine_ref, sine_ref):
    block = panel_ref[0]
    points = point_ref.shape[1]
    for group in range(points // GROUP):
        rows = pl.ds(group * GROUP, GROUP)
        shape = (GROUP, block.shape[1])
        delta_x = point_ref[0, rows, :] - jnp.broadcast_to(block[2:3], shape)
        delta_y = point_ref[1, rows, :] - jnp.broadcast_to(block[3:4], shape)
        delta_z = point_ref[2, rows, :] - jnp.broadcast_to(block[4:5], shape)
        distance = jnp.sqrt(delta_x * delta_x + delta_y * delta_y + delta_z * delta_z)
        inverse = 1.0 / (FOUR_PI * distance)
        sine, cosine = sine_cosine(WAVENUMBER * distance)
        cosine_ref[0, rows, :] = cosine * inverse
        sine_ref[0, rows, :] = sine * inverse


def contract_kernel(strength_ref, cosine_ref, sine_ref, out_ref, real_ref, imag_ref):
    chunk = pl.program_id(0)

    @pl.when(chunk == 0)
    def _():
        real_ref[...] = jnp.zeros_like(real_ref)
        imag_ref[...] = jnp.zeros_like(imag_ref)

    block = strength_ref[0]
    shape = real_ref.shape
    strength_re = jnp.broadcast_to(block[0:1], shape)
    strength_im = jnp.broadcast_to(block[1:2], shape)
    cosine_part = cosine_ref[0]
    sine_part = sine_ref[0]
    real_ref[...] += strength_re * cosine_part - strength_im * sine_part
    imag_ref[...] += strength_re * sine_part + strength_im * cosine_part

    @pl.when(chunk == pl.num_programs(0) - 1)
    def _():
        out_ref[0:1, :] = jnp.sum(real_ref[...].T, axis=0, keepdims=True)
        out_ref[1:2, :] = jnp.sum(imag_ref[...].T, axis=0, keepdims=True)


def kernel_parts(panels, field_points):
    chunks, rows, lanes = panels.shape
    points = field_points.shape[1]
    spread = jnp.broadcast_to(field_points[:, :, None], (3, points, lanes))
    pairs = chunks * lanes * points
    part = jax.ShapeDtypeStruct((chunks, points, lanes), jnp.float32)
    return pl.pallas_call(
        parts_kernel,
        out_shape=(part, part),
        grid=(chunks,),
        in_specs=[
            pl.BlockSpec((1, rows, lanes), lambda c: (c, 0, 0)),
            pl.BlockSpec((3, points, lanes), lambda c: (0, 0, 0)),
        ],
        out_specs=[pl.BlockSpec((1, points, lanes), lambda c: (c, 0, 0))] * 2,
        cost_estimate=pl.CostEstimate(flops=60 * pairs, transcendentals=2 * pairs, bytes_accessed=8 * pairs),
    )(panels, spread)


def contract(strength, cosine_part, sine_part):
    chunks, points, lanes = cosine_part.shape
    return pl.pallas_call(
        contract_kernel,
        out_shape=jax.ShapeDtypeStruct((2, points), jnp.float32),
        grid=(chunks,),
        in_specs=[
            pl.BlockSpec((1, 2, lanes), lambda c: (c, 0, 0)),
            pl.BlockSpec((1, points, lanes), lambda c: (c, 0, 0)),
            pl.BlockSpec((1, points, lanes), lambda c: (c, 0, 0)),
        ],
        out_specs=pl.BlockSpec((2, points), lambda c: (0, 0)),
        scratch_shapes=[pltpu.VMEM((points, lanes), jnp.float32)] * 2,
        cost_estimate=pl.CostEstimate(flops=8 * chunks * points * lanes, transcendentals=0, bytes_accessed=8 * chunks * points * lanes),
    )(strength, cosine_part, sine_part)


def shards(node_velocity, node_owner, node_panel, panel_centroid, panel_area, field_points):
    slab_count = lax.axis_size("panel")
    slab_width = panel_area.shape[0]
    destination = node_owner[:, 0]
    owner_hot = (destination[None, :] == jnp.arange(slab_count, dtype=jnp.int32)[:, None]).astype(
        jnp.float32
    )
    weighted = (node_velocity[:, None, :] * owner_hot[None, :, :]).reshape(2 * slab_count, -1)
    panel_hot = (node_panel[:, None] == jnp.arange(slab_width, dtype=jnp.int32)[None, :]).astype(
        jnp.float32
    )
    partial = jnp.dot(
        weighted, panel_hot, precision=lax.Precision.HIGHEST, preferred_element_type=jnp.float32
    )
    partial = partial.reshape(2, slab_count, slab_width).transpose(1, 0, 2)
    centroid_copies = jnp.broadcast_to(panel_centroid[None], (slab_count,) + panel_centroid.shape)
    outgoing = jnp.concatenate([partial, centroid_copies], axis=1)
    got = lax.all_to_all(outgoing, "panel", split_axis=0, concat_axis=0, tiled=True)
    cosine_part, sine_part = kernel_parts(got, field_points)
    column = jnp.sum(got[:, 0:2], axis=0)
    point_count = lax.axis_size("point")
    copies = jnp.broadcast_to(column[None], (point_count,) + column.shape)
    velocity = jnp.sum(lax.all_to_all(copies, "point", split_axis=0, concat_axis=0, tiled=True), axis=0)
    strength = jnp.stack([-panel_area * velocity[1], panel_area * velocity[0]])
    spread = jnp.broadcast_to(strength[None], (slab_count,) + strength.shape)
    gathered = lax.all_to_all(spread, "panel", split_axis=0, concat_axis=0, tiled=True)
    return contract(gathered, cosine_part, sine_part)


def solution(mesh):
    return jax.shard_map(
        shards,
        mesh=mesh,
        in_specs=(
            P(None, ("panel", "point")),
            P(("panel", "point"), None),
            P(("panel", "point")),
            P(None, "panel"),
            P("panel"),
            P(None, ("panel", "point")),
        ),
        out_specs=P(None, ("panel", "point")),
        check_vma=False,
    )
```

```python
import math

import jax
import jax.numpy as jnp
from jax import lax
from jax.experimental import pallas as pl
from jax.experimental.pallas import tpu as pltpu
from jax.sharding import PartitionSpec as P

WAVENUMBER = 40.0
FOUR_PI = 4.0 * math.pi


TWO_OVER_PI = 2.0 / math.pi
HALF_PI_1 = 1.5703125
HALF_PI_2 = 4.837512969970703125e-4
HALF_PI_3 = 7.54978995489188216e-8
GROUP = 16
PARTS_STEP = 8
CONTRACT_STEP = 16


def sine_cosine(angle):
    turns = jnp.floor(angle * TWO_OVER_PI + 0.5)
    rest = ((angle - turns * HALF_PI_1) - turns * HALF_PI_2) - turns * HALF_PI_3
    square = rest * rest
    sine = rest + rest * square * (
        -1.6666654611e-1 + square * (8.3321608736e-3 + square * -1.9515295891e-4)
    )
    cosine = 1.0 - 0.5 * square + square * square * (
        4.166664568298827e-2 + square * (-1.388731625493765e-3 + square * 2.443315711809948e-5)
    )
    quadrant = turns.astype(jnp.int32)
    swap = (quadrant & 1) == 1
    sine_out = jnp.where(swap, cosine, sine)
    cosine_out = jnp.where(swap, sine, cosine)
    sine_out = jnp.where((quadrant & 2) == 2, -sine_out, sine_out)
    cosine_out = jnp.where(((quadrant + 1) & 2) == 2, -cosine_out, cosine_out)
    return sine_out, cosine_out


def green_kernel(panel_ref, point_ref, out_ref, total_ref):
    chunks = panel_ref.shape[0]
    points = point_ref.shape[1]
    for group in range(points // GROUP):
        rows = pl.ds(group * GROUP, GROUP)
        point_x = point_ref[0, rows, :]
        point_y = point_ref[1, rows, :]
        point_z = point_ref[2, rows, :]

        def body(chunk, carry):
            real_sum, imag_sum = carry
            block = panel_ref[chunk]
            shape = (GROUP, block.shape[1])
            strength_re = jnp.broadcast_to(block[0:1], shape)
            strength_im = jnp.broadcast_to(block[1:2], shape)
            delta_x = point_x - jnp.broadcast_to(block[2:3], shape)
            delta_y = point_y - jnp.broadcast_to(block[3:4], shape)
            delta_z = point_z - jnp.broadcast_to(block[4:5], shape)
            distance = jnp.sqrt(delta_x * delta_x + delta_y * delta_y + delta_z * delta_z)
            inverse = 1.0 / (FOUR_PI * distance)
            sine, cosine = sine_cosine(WAVENUMBER * distance)
            cosine_part = cosine * inverse
            sine_part = sine * inverse
            real_sum = real_sum + (strength_re * cosine_part - strength_im * sine_part)
            imag_sum = imag_sum + (strength_re * sine_part + strength_im * cosine_part)
            return real_sum, imag_sum

        zero = jnp.zeros((GROUP, panel_ref.shape[2]), jnp.float32)
        real_sum, imag_sum = lax.fori_loop(0, chunks, body, (zero, zero), unroll=2)
        total_ref[0, rows, :] = real_sum
        total_ref[1, rows, :] = imag_sum
    out_ref[0:1, :] = jnp.sum(total_ref[0].T, axis=0, keepdims=True)
    out_ref[1:2, :] = jnp.sum(total_ref[1].T, axis=0, keepdims=True)


def green(panels, field_points):
    points = field_points.shape[1]
    lanes = panels.shape[2]
    spread = jnp.broadcast_to(field_points[:, :, None], (3, points, lanes))
    pairs = panels.shape[0] * lanes * points
    return pl.pallas_call(
        green_kernel,
        out_shape=jax.ShapeDtypeStruct((2, points), jnp.float32),
        in_specs=[pl.BlockSpec(memory_space=pltpu.VMEM)] * 2,
        out_specs=pl.BlockSpec(memory_space=pltpu.VMEM),
        scratch_shapes=[pltpu.VMEM((2, points, lanes), jnp.float32)],
        cost_estimate=pl.CostEstimate(flops=70 * pairs, transcendentals=2 * pairs, bytes_accessed=4 * (panels.size + spread.size + 2 * points)),
    )(panels, spread)


def parts_kernel(panel_ref, point_ref, cosine_ref, sine_ref):
    points = point_ref.shape[1]

    def body(chunk, carry):
        block = panel_ref[chunk]
        shape = (GROUP, block.shape[1])
        centroid_x = jnp.broadcast_to(block[2:3], shape)
        centroid_y = jnp.broadcast_to(block[3:4], shape)
        centroid_z = jnp.broadcast_to(block[4:5], shape)
        for group in range(points // GROUP):
            rows = pl.ds(group * GROUP, GROUP)
            delta_x = point_ref[0, rows, :] - centroid_x
            delta_y = point_ref[1, rows, :] - centroid_y
            delta_z = point_ref[2, rows, :] - centroid_z
            distance = jnp.sqrt(delta_x * delta_x + delta_y * delta_y + delta_z * delta_z)
            inverse = 1.0 / (FOUR_PI * distance)
            sine, cosine = sine_cosine(WAVENUMBER * distance)
            cosine_ref[chunk, rows, :] = cosine * inverse
            sine_ref[chunk, rows, :] = sine * inverse
        return carry

    lax.fori_loop(0, panel_ref.shape[0], body, 0)


def contract_kernel(strength_ref, cosine_ref, sine_ref, out_ref, real_ref, imag_ref):
    step = pl.program_id(0)

    @pl.when(step == 0)
    def _():
        real_ref[...] = jnp.zeros_like(real_ref)
        imag_ref[...] = jnp.zeros_like(imag_ref)

    def body(chunk, carry):
        block = strength_ref[chunk]
        shape = real_ref.shape
        strength_re = jnp.broadcast_to(block[0:1], shape)
        strength_im = jnp.broadcast_to(block[1:2], shape)
        cosine_part = cosine_ref[chunk]
        sine_part = sine_ref[chunk]
        real_ref[...] += strength_re * cosine_part - strength_im * sine_part
        imag_ref[...] += strength_re * sine_part + strength_im * cosine_part
        return carry

    lax.fori_loop(0, strength_ref.shape[0], body, 0)

    @pl.when(step == pl.num_programs(0) - 1)
    def _():
        out_ref[0:1, :] = jnp.sum(real_ref[...].T, axis=0, keepdims=True)
        out_ref[1:2, :] = jnp.sum(imag_ref[...].T, axis=0, keepdims=True)


def kernel_parts(panels, field_points):
    chunks, rows, lanes = panels.shape
    points = field_points.shape[1]
    spread = jnp.broadcast_to(field_points[:, :, None], (3, points, lanes))
    pairs = chunks * lanes * points
    part = jax.ShapeDtypeStruct((chunks, points, lanes), jnp.float32)
    return pl.pallas_call(
        parts_kernel,
        out_shape=(part, part),
        grid=(chunks // PARTS_STEP,),
        in_specs=[
            pl.BlockSpec((PARTS_STEP, rows, lanes), lambda c: (c, 0, 0)),
            pl.BlockSpec((3, points, lanes), lambda c: (0, 0, 0)),
        ],
        out_specs=[pl.BlockSpec((PARTS_STEP, points, lanes), lambda c: (c, 0, 0))] * 2,
        cost_estimate=pl.CostEstimate(flops=60 * pairs, transcendentals=2 * pairs, bytes_accessed=8 * pairs),
    )(panels, spread)


def contract(strength, cosine_part, sine_part):
    chunks, points, lanes = cosine_part.shape
    return pl.pallas_call(
        contract_kernel,
        out_shape=jax.ShapeDtypeStruct((2, points), jnp.float32),
        grid=(chunks // CONTRACT_STEP,),
        in_specs=[
            pl.BlockSpec((CONTRACT_STEP, 2, lanes), lambda c: (c, 0, 0)),
            pl.BlockSpec((CONTRACT_STEP, points, lanes), lambda c: (c, 0, 0)),
            pl.BlockSpec((CONTRACT_STEP, points, lanes), lambda c: (c, 0, 0)),
        ],
        out_specs=pl.BlockSpec((2, points), lambda c: (0, 0)),
        scratch_shapes=[pltpu.VMEM((points, lanes), jnp.float32)] * 2,
        cost_estimate=pl.CostEstimate(flops=8 * chunks * points * lanes, transcendentals=0, bytes_accessed=8 * chunks * points * lanes),
    )(strength, cosine_part, sine_part)


def shards(node_velocity, node_owner, node_panel, panel_centroid, panel_area, field_points):
    slab_count = lax.axis_size("panel")
    slab_width = panel_area.shape[0]
    destination = node_owner[:, 0]
    owner_hot = (destination[None, :] == jnp.arange(slab_count, dtype=jnp.int32)[:, None]).astype(
        jnp.float32
    )
    weighted = (node_velocity[:, None, :] * owner_hot[None, :, :]).reshape(2 * slab_count, -1)
    panel_hot = (node_panel[:, None] == jnp.arange(slab_width, dtype=jnp.int32)[None, :]).astype(
        jnp.float32
    )
    partial = jnp.dot(
        weighted, panel_hot, precision=lax.Precision.HIGHEST, preferred_element_type=jnp.float32
    )
    partial = partial.reshape(2, slab_count, slab_width).transpose(1, 0, 2)
    centroid_copies = jnp.broadcast_to(panel_centroid[None], (slab_count,) + panel_centroid.shape)
    outgoing = jnp.concatenate([partial, centroid_copies], axis=1)
    got = lax.all_to_all(outgoing, "panel", split_axis=0, concat_axis=0, tiled=True)
    cosine_part, sine_part = kernel_parts(got, field_points)
    column = jnp.sum(got[:, 0:2], axis=0)
    point_count = lax.axis_size("point")
    copies = jnp.broadcast_to(column[None], (point_count,) + column.shape)
    velocity = jnp.sum(lax.all_to_all(copies, "point", split_axis=0, concat_axis=0, tiled=True), axis=0)
    strength = jnp.stack([-panel_area * velocity[1], panel_area * velocity[0]])
    spread = jnp.broadcast_to(strength[None], (slab_count,) + strength.shape)
    gathered = lax.all_to_all(spread, "panel", split_axis=0, concat_axis=0, tiled=True)
    return contract(gathered, cosine_part, sine_part)


def solution(mesh):
    return jax.shard_map(
        shards,
        mesh=mesh,
        in_specs=(
            P(None, ("panel", "point")),
            P(("panel", "point"), None),
            P(("panel", "point")),
            P(None, "panel"),
            P("panel"),
            P(None, ("panel", "point")),
        ),
        out_specs=P(None, ("panel", "point")),
        check_vma=False,
    )
```

```python
import math

import jax
import jax.numpy as jnp
from jax import lax
from jax.experimental import pallas as pl
from jax.experimental.pallas import tpu as pltpu
from jax.sharding import PartitionSpec as P

WAVENUMBER = 40.0
FOUR_PI = 4.0 * math.pi


TWO_OVER_PI = 2.0 / math.pi
HALF_PI_1 = 1.5703125
HALF_PI_2 = 4.837512969970703125e-4
HALF_PI_3 = 7.54978995489188216e-8
GROUP = 16
PARTS_STEP = 8
CONTRACT_GROUPS = 8


def sine_cosine(angle):
    turns = jnp.floor(angle * TWO_OVER_PI + 0.5)
    rest = ((angle - turns * HALF_PI_1) - turns * HALF_PI_2) - turns * HALF_PI_3
    square = rest * rest
    sine = rest + rest * square * (
        -1.6666654611e-1 + square * (8.3321608736e-3 + square * -1.9515295891e-4)
    )
    cosine = 1.0 - 0.5 * square + square * square * (
        4.166664568298827e-2 + square * (-1.388731625493765e-3 + square * 2.443315711809948e-5)
    )
    quadrant = turns.astype(jnp.int32)
    swap = (quadrant & 1) == 1
    sine_out = jnp.where(swap, cosine, sine)
    cosine_out = jnp.where(swap, sine, cosine)
    sine_out = jnp.where((quadrant & 2) == 2, -sine_out, sine_out)
    cosine_out = jnp.where(((quadrant + 1) & 2) == 2, -cosine_out, cosine_out)
    return sine_out, cosine_out


def green_kernel(panel_ref, point_ref, out_ref, total_ref):
    chunks = panel_ref.shape[0]
    points = point_ref.shape[1]
    for group in range(points // GROUP):
        rows = pl.ds(group * GROUP, GROUP)
        point_x = point_ref[0, rows, :]
        point_y = point_ref[1, rows, :]
        point_z = point_ref[2, rows, :]

        def body(chunk, carry):
            real_sum, imag_sum = carry
            block = panel_ref[chunk]
            shape = (GROUP, block.shape[1])
            strength_re = jnp.broadcast_to(block[0:1], shape)
            strength_im = jnp.broadcast_to(block[1:2], shape)
            delta_x = point_x - jnp.broadcast_to(block[2:3], shape)
            delta_y = point_y - jnp.broadcast_to(block[3:4], shape)
            delta_z = point_z - jnp.broadcast_to(block[4:5], shape)
            distance = jnp.sqrt(delta_x * delta_x + delta_y * delta_y + delta_z * delta_z)
            inverse = 1.0 / (FOUR_PI * distance)
            sine, cosine = sine_cosine(WAVENUMBER * distance)
            cosine_part = cosine * inverse
            sine_part = sine * inverse
            real_sum = real_sum + (strength_re * cosine_part - strength_im * sine_part)
            imag_sum = imag_sum + (strength_re * sine_part + strength_im * cosine_part)
            return real_sum, imag_sum

        zero = jnp.zeros((GROUP, panel_ref.shape[2]), jnp.float32)
        real_sum, imag_sum = lax.fori_loop(0, chunks, body, (zero, zero), unroll=2)
        total_ref[0, rows, :] = real_sum
        total_ref[1, rows, :] = imag_sum
    out_ref[0:1, :] = jnp.sum(total_ref[0].T, axis=0, keepdims=True)
    out_ref[1:2, :] = jnp.sum(total_ref[1].T, axis=0, keepdims=True)


def green(panels, field_points):
    points = field_points.shape[1]
    lanes = panels.shape[2]
    spread = jnp.broadcast_to(field_points[:, :, None], (3, points, lanes))
    pairs = panels.shape[0] * lanes * points
    return pl.pallas_call(
        green_kernel,
        out_shape=jax.ShapeDtypeStruct((2, points), jnp.float32),
        in_specs=[pl.BlockSpec(memory_space=pltpu.VMEM)] * 2,
        out_specs=pl.BlockSpec(memory_space=pltpu.VMEM),
        scratch_shapes=[pltpu.VMEM((2, points, lanes), jnp.float32)],
        cost_estimate=pl.CostEstimate(flops=70 * pairs, transcendentals=2 * pairs, bytes_accessed=4 * (panels.size + spread.size + 2 * points)),
    )(panels, spread)


def parts_kernel(panel_ref, point_ref, cosine_ref, sine_ref):
    points = point_ref.shape[1]

    def body(chunk, carry):
        block = panel_ref[chunk]
        shape = (GROUP, block.shape[1])
        centroid_x = jnp.broadcast_to(block[2:3], shape)
        centroid_y = jnp.broadcast_to(block[3:4], shape)
        centroid_z = jnp.broadcast_to(block[4:5], shape)
        for group in range(points // GROUP):
            rows = pl.ds(group * GROUP, GROUP)
            delta_x = point_ref[0, rows, :] - centroid_x
            delta_y = point_ref[1, rows, :] - centroid_y
            delta_z = point_ref[2, rows, :] - centroid_z
            distance = jnp.sqrt(delta_x * delta_x + delta_y * delta_y + delta_z * delta_z)
            inverse = 1.0 / (FOUR_PI * distance)
            sine, cosine = sine_cosine(WAVENUMBER * distance)
            cosine_ref[chunk, rows, :] = cosine * inverse
            sine_ref[chunk, rows, :] = sine * inverse
        return carry

    lax.fori_loop(0, panel_ref.shape[0], body, 0)


def contract_kernel(strength_ref, cosine_hbm, sine_hbm, out_ref, cosine_buf, sine_buf, real_ref, imag_ref, sems):
    chunks = cosine_hbm.shape[0]
    per_group = chunks // CONTRACT_GROUPS

    def copies(group):
        window = pl.ds(group * per_group, per_group)
        return (
            pltpu.make_async_copy(cosine_hbm.at[window], cosine_buf.at[window], sems.at[0, group]),
            pltpu.make_async_copy(sine_hbm.at[window], sine_buf.at[window], sems.at[1, group]),
        )

    for group in range(CONTRACT_GROUPS):
        for copy in copies(group):
            copy.start()
    real_ref[...] = jnp.zeros_like(real_ref)
    imag_ref[...] = jnp.zeros_like(imag_ref)

    def body(chunk, carry):
        block = strength_ref[chunk]
        shape = real_ref.shape
        strength_re = jnp.broadcast_to(block[0:1], shape)
        strength_im = jnp.broadcast_to(block[1:2], shape)
        cosine_part = cosine_buf[chunk]
        sine_part = sine_buf[chunk]
        real_ref[...] += strength_re * cosine_part - strength_im * sine_part
        imag_ref[...] += strength_re * sine_part + strength_im * cosine_part
        return carry

    for group in range(CONTRACT_GROUPS):
        for copy in copies(group):
            copy.wait()
        lax.fori_loop(group * per_group, (group + 1) * per_group, body, 0)
    out_ref[0:1, :] = jnp.sum(real_ref[...].T, axis=0, keepdims=True)
    out_ref[1:2, :] = jnp.sum(imag_ref[...].T, axis=0, keepdims=True)


def kernel_parts(panels, field_points):
    chunks, rows, lanes = panels.shape
    points = field_points.shape[1]
    spread = jnp.broadcast_to(field_points[:, :, None], (3, points, lanes))
    pairs = chunks * lanes * points
    part = jax.ShapeDtypeStruct((chunks, points, lanes), jnp.float32)
    return pl.pallas_call(
        parts_kernel,
        out_shape=(part, part),
        grid=(chunks // PARTS_STEP,),
        in_specs=[
            pl.BlockSpec((PARTS_STEP, rows, lanes), lambda c: (c, 0, 0)),
            pl.BlockSpec((3, points, lanes), lambda c: (0, 0, 0)),
        ],
        out_specs=[pl.BlockSpec((PARTS_STEP, points, lanes), lambda c: (c, 0, 0))] * 2,
        cost_estimate=pl.CostEstimate(flops=60 * pairs, transcendentals=2 * pairs, bytes_accessed=8 * pairs),
    )(panels, spread)


def contract(strength, cosine_part, sine_part):
    chunks, points, lanes = cosine_part.shape
    return pl.pallas_call(
        contract_kernel,
        out_shape=jax.ShapeDtypeStruct((2, points), jnp.float32),
        in_specs=[
            pl.BlockSpec(memory_space=pltpu.VMEM),
            pl.BlockSpec(memory_space=pl.ANY),
            pl.BlockSpec(memory_space=pl.ANY),
        ],
        out_specs=pl.BlockSpec(memory_space=pltpu.VMEM),
        scratch_shapes=[pltpu.VMEM((chunks, points, lanes), jnp.float32)] * 2
        + [pltpu.VMEM((points, lanes), jnp.float32)] * 2
        + [pltpu.SemaphoreType.DMA((2, CONTRACT_GROUPS))],
        cost_estimate=pl.CostEstimate(flops=8 * chunks * points * lanes, transcendentals=0, bytes_accessed=8 * chunks * points * lanes),
    )(strength, cosine_part, sine_part)


def shards(node_velocity, node_owner, node_panel, panel_centroid, panel_area, field_points):
    slab_count = lax.axis_size("panel")
    slab_width = panel_area.shape[0]
    destination = node_owner[:, 0]
    owner_hot = (destination[None, :] == jnp.arange(slab_count, dtype=jnp.int32)[:, None]).astype(
        jnp.float32
    )
    weighted = (node_velocity[:, None, :] * owner_hot[None, :, :]).reshape(2 * slab_count, -1)
    panel_hot = (node_panel[:, None] == jnp.arange(slab_width, dtype=jnp.int32)[None, :]).astype(
        jnp.float32
    )
    partial = jnp.dot(
        weighted, panel_hot, precision=lax.Precision.HIGHEST, preferred_element_type=jnp.float32
    )
    partial = partial.reshape(2, slab_count, slab_width).transpose(1, 0, 2)
    centroid_copies = jnp.broadcast_to(panel_centroid[None], (slab_count,) + panel_centroid.shape)
    outgoing = jnp.concatenate([partial, centroid_copies], axis=1)
    got = lax.all_to_all(outgoing, "panel", split_axis=0, concat_axis=0, tiled=True)
    cosine_part, sine_part = kernel_parts(got, field_points)
    column = jnp.sum(got[:, 0:2], axis=0)
    point_count = lax.axis_size("point")
    copies = jnp.broadcast_to(column[None], (point_count,) + column.shape)
    velocity = jnp.sum(lax.all_to_all(copies, "point", split_axis=0, concat_axis=0, tiled=True), axis=0)
    strength = jnp.stack([-panel_area * velocity[1], panel_area * velocity[0]])
    spread = jnp.broadcast_to(strength[None], (slab_count,) + strength.shape)
    gathered = lax.all_to_all(spread, "panel", split_axis=0, concat_axis=0, tiled=True)
    return contract(gathered, cosine_part, sine_part)


def solution(mesh):
    return jax.shard_map(
        shards,
        mesh=mesh,
        in_specs=(
            P(None, ("panel", "point")),
            P(("panel", "point"), None),
            P(("panel", "point")),
            P(None, "panel"),
            P("panel"),
            P(None, ("panel", "point")),
        ),
        out_specs=P(None, ("panel", "point")),
        check_vma=False,
    )
```

```python
import math

import jax
import jax.numpy as jnp
from jax import lax
from jax.experimental import pallas as pl
from jax.experimental.pallas import tpu as pltpu
from jax.sharding import PartitionSpec as P

WAVENUMBER = 40.0
FOUR_PI = 4.0 * math.pi


TWO_OVER_PI = 2.0 / math.pi
HALF_PI_1 = 1.5703125
HALF_PI_2 = 4.837512969970703125e-4
HALF_PI_3 = 7.54978995489188216e-8
GROUP = 16
PARTS_STEP = 8
CONTRACT_STEP = 16


def sine_cosine(angle):
    turns = jnp.floor(angle * TWO_OVER_PI + 0.5)
    rest = ((angle - turns * HALF_PI_1) - turns * HALF_PI_2) - turns * HALF_PI_3
    square = rest * rest
    sine = rest + rest * square * (
        -1.6666654611e-1 + square * (8.3321608736e-3 + square * -1.9515295891e-4)
    )
    cosine = 1.0 - 0.5 * square + square * square * (
        4.166664568298827e-2 + square * (-1.388731625493765e-3 + square * 2.443315711809948e-5)
    )
    quadrant = turns.astype(jnp.int32)
    swap = (quadrant & 1) == 1
    sine_out = jnp.where(swap, cosine, sine)
    cosine_out = jnp.where(swap, sine, cosine)
    sine_out = jnp.where((quadrant & 2) == 2, -sine_out, sine_out)
    cosine_out = jnp.where(((quadrant + 1) & 2) == 2, -cosine_out, cosine_out)
    return sine_out, cosine_out


def green_kernel(panel_ref, point_ref, out_ref, total_ref):
    chunks = panel_ref.shape[0]
    points = point_ref.shape[1]
    for group in range(points // GROUP):
        rows = pl.ds(group * GROUP, GROUP)
        point_x = point_ref[0, rows, :]
        point_y = point_ref[1, rows, :]
        point_z = point_ref[2, rows, :]

        def body(chunk, carry):
            real_sum, imag_sum = carry
            block = panel_ref[chunk]
            shape = (GROUP, block.shape[1])
            strength_re = jnp.broadcast_to(block[0:1], shape)
            strength_im = jnp.broadcast_to(block[1:2], shape)
            delta_x = point_x - jnp.broadcast_to(block[2:3], shape)
            delta_y = point_y - jnp.broadcast_to(block[3:4], shape)
            delta_z = point_z - jnp.broadcast_to(block[4:5], shape)
            distance = jnp.sqrt(delta_x * delta_x + delta_y * delta_y + delta_z * delta_z)
            inverse = 1.0 / (FOUR_PI * distance)
            sine, cosine = sine_cosine(WAVENUMBER * distance)
            cosine_part = cosine * inverse
            sine_part = sine * inverse
            real_sum = real_sum + (strength_re * cosine_part - strength_im * sine_part)
            imag_sum = imag_sum + (strength_re * sine_part + strength_im * cosine_part)
            return real_sum, imag_sum

        zero = jnp.zeros((GROUP, panel_ref.shape[2]), jnp.float32)
        real_sum, imag_sum = lax.fori_loop(0, chunks, body, (zero, zero), unroll=2)
        total_ref[0, rows, :] = real_sum
        total_ref[1, rows, :] = imag_sum
    out_ref[0:1, :] = jnp.sum(total_ref[0].T, axis=0, keepdims=True)
    out_ref[1:2, :] = jnp.sum(total_ref[1].T, axis=0, keepdims=True)


def green(panels, field_points):
    points = field_points.shape[1]
    lanes = panels.shape[2]
    spread = jnp.broadcast_to(field_points[:, :, None], (3, points, lanes))
    pairs = panels.shape[0] * lanes * points
    return pl.pallas_call(
        green_kernel,
        out_shape=jax.ShapeDtypeStruct((2, points), jnp.float32),
        in_specs=[pl.BlockSpec(memory_space=pltpu.VMEM)] * 2,
        out_specs=pl.BlockSpec(memory_space=pltpu.VMEM),
        scratch_shapes=[pltpu.VMEM((2, points, lanes), jnp.float32)],
        cost_estimate=pl.CostEstimate(flops=70 * pairs, transcendentals=2 * pairs, bytes_accessed=4 * (panels.size + spread.size + 2 * points)),
    )(panels, spread)


def parts_kernel(panel_ref, point_ref, cosine_ref, sine_ref):
    points = point_ref.shape[1]

    def body(chunk, carry):
        block = panel_ref[chunk]
        shape = (GROUP, block.shape[1])
        centroid_x = jnp.broadcast_to(block[2:3], shape)
        centroid_y = jnp.broadcast_to(block[3:4], shape)
        centroid_z = jnp.broadcast_to(block[4:5], shape)
        for group in range(points // GROUP):
            rows = pl.ds(group * GROUP, GROUP)
            delta_x = point_ref[0, rows, :] - centroid_x
            delta_y = point_ref[1, rows, :] - centroid_y
            delta_z = point_ref[2, rows, :] - centroid_z
            distance = jnp.sqrt(delta_x * delta_x + delta_y * delta_y + delta_z * delta_z)
            inverse = 1.0 / (FOUR_PI * distance)
            sine, cosine = sine_cosine(WAVENUMBER * distance)
            cosine_ref[chunk, rows, :] = cosine * inverse
            sine_ref[chunk, rows, :] = sine * inverse
        return carry

    lax.fori_loop(0, panel_ref.shape[0], body, 0)


def contract_kernel(strength_ref, cosine_ref, sine_ref, out_ref, real_ref, imag_ref):
    step = pl.program_id(0)

    @pl.when(step == 0)
    def _():
        real_ref[...] = jnp.zeros_like(real_ref)
        imag_ref[...] = jnp.zeros_like(imag_ref)

    def body(chunk, carry):
        block = strength_ref[chunk]
        shape = real_ref.shape
        strength_re = jnp.broadcast_to(block[0:1], shape)
        strength_im = jnp.broadcast_to(block[1:2], shape)
        cosine_part = cosine_ref[chunk]
        sine_part = sine_ref[chunk]
        real_ref[...] += strength_re * cosine_part - strength_im * sine_part
        imag_ref[...] += strength_re * sine_part + strength_im * cosine_part
        return carry

    lax.fori_loop(0, strength_ref.shape[0], body, 0)

    @pl.when(step == pl.num_programs(0) - 1)
    def _():
        out_ref[0:1, :] = jnp.sum(real_ref[...].T, axis=0, keepdims=True)
        out_ref[1:2, :] = jnp.sum(imag_ref[...].T, axis=0, keepdims=True)


def kernel_parts(panels, field_points):
    chunks, rows, lanes = panels.shape
    points = field_points.shape[1]
    spread = jnp.broadcast_to(field_points[:, :, None], (3, points, lanes))
    pairs = chunks * lanes * points
    part = jax.ShapeDtypeStruct((chunks, points, lanes), jnp.float32)
    return pl.pallas_call(
        parts_kernel,
        out_shape=(part, part),
        grid=(chunks // PARTS_STEP,),
        in_specs=[
            pl.BlockSpec((PARTS_STEP, rows, lanes), lambda c: (c, 0, 0)),
            pl.BlockSpec((3, points, lanes), lambda c: (0, 0, 0)),
        ],
        out_specs=[pl.BlockSpec((PARTS_STEP, points, lanes), lambda c: (c, 0, 0))] * 2,
        cost_estimate=pl.CostEstimate(flops=60 * pairs, transcendentals=2 * pairs, bytes_accessed=8 * pairs),
    )(panels, spread)


def contract(strength, cosine_part, sine_part):
    chunks, points, lanes = cosine_part.shape
    return pl.pallas_call(
        contract_kernel,
        out_shape=jax.ShapeDtypeStruct((2, points), jnp.float32),
        grid=(chunks // CONTRACT_STEP,),
        in_specs=[
            pl.BlockSpec((CONTRACT_STEP, 2, lanes), lambda c: (c, 0, 0)),
            pl.BlockSpec((CONTRACT_STEP, points, lanes), lambda c: (c, 0, 0)),
            pl.BlockSpec((CONTRACT_STEP, points, lanes), lambda c: (c, 0, 0)),
        ],
        out_specs=pl.BlockSpec((2, points), lambda c: (0, 0)),
        scratch_shapes=[pltpu.VMEM((points, lanes), jnp.float32)] * 2,
        cost_estimate=pl.CostEstimate(flops=8 * chunks * points * lanes, transcendentals=0, bytes_accessed=8 * chunks * points * lanes),
    )(strength, cosine_part, sine_part)


def shards(node_velocity, node_owner, node_panel, panel_centroid, panel_area, field_points):
    slab_count = lax.axis_size("panel")
    slab_width = panel_area.shape[0]
    destination = node_owner[:, 0]
    owner_hot = (destination[None, :] == jnp.arange(slab_count, dtype=jnp.int32)[:, None]).astype(
        jnp.float32
    )
    weighted = (node_velocity[:, None, :] * owner_hot[None, :, :]).reshape(2 * slab_count, -1)
    panel_hot = (node_panel[:, None] == jnp.arange(slab_width, dtype=jnp.int32)[None, :]).astype(
        jnp.float32
    )
    partial = jnp.dot(
        weighted, panel_hot, precision=lax.Precision.HIGHEST, preferred_element_type=jnp.float32
    )
    partial = partial.reshape(2, slab_count, slab_width).transpose(1, 0, 2)
    centroid_copies = jnp.broadcast_to(panel_centroid[None], (slab_count,) + panel_centroid.shape)
    outgoing = jnp.concatenate([partial, centroid_copies], axis=1)
    got = lax.all_to_all(outgoing, "panel", split_axis=0, concat_axis=0, tiled=True)
    cosine_part, sine_part = kernel_parts(got, field_points)
    column = jnp.sum(got[:, 0:2], axis=0)
    point_count = lax.axis_size("point")
    velocity = column
    distance = 1
    while distance < point_count:
        pairs = [(source, source ^ distance) for source in range(point_count)]
        velocity = velocity + lax.ppermute(velocity, "point", pairs)
        distance *= 2
    strength = jnp.stack([-panel_area * velocity[1], panel_area * velocity[0]])
    spread = jnp.broadcast_to(strength[None], (slab_count,) + strength.shape)
    gathered = lax.all_to_all(spread, "panel", split_axis=0, concat_axis=0, tiled=True)
    return contract(gathered, cosine_part, sine_part)


def solution(mesh):
    return jax.shard_map(
        shards,
        mesh=mesh,
        in_specs=(
            P(None, ("panel", "point")),
            P(("panel", "point"), None),
            P(("panel", "point")),
            P(None, "panel"),
            P("panel"),
            P(None, ("panel", "point")),
        ),
        out_specs=P(None, ("panel", "point")),
        check_vma=False,
    )
```

```python
import math

import jax
import jax.numpy as jnp
from jax import lax
from jax.experimental import pallas as pl
from jax.experimental.pallas import tpu as pltpu
from jax.sharding import PartitionSpec as P

WAVENUMBER = 40.0
FOUR_PI = 4.0 * math.pi


TWO_OVER_PI = 2.0 / math.pi
HALF_PI_1 = 1.5703125
HALF_PI_2 = 4.837512969970703125e-4
HALF_PI_3 = 7.54978995489188216e-8
GROUP = 16
PARTS_STEP = 8
CONTRACT_STEP = 16


def sine_cosine(angle):
    turns = jnp.floor(angle * TWO_OVER_PI + 0.5)
    rest = ((angle - turns * HALF_PI_1) - turns * HALF_PI_2) - turns * HALF_PI_3
    square = rest * rest
    sine = rest + rest * square * (
        -1.6666654611e-1 + square * (8.3321608736e-3 + square * -1.9515295891e-4)
    )
    cosine = 1.0 - 0.5 * square + square * square * (
        4.166664568298827e-2 + square * (-1.388731625493765e-3 + square * 2.443315711809948e-5)
    )
    quadrant = turns.astype(jnp.int32)
    swap = (quadrant & 1) == 1
    sine_out = jnp.where(swap, cosine, sine)
    cosine_out = jnp.where(swap, sine, cosine)
    sine_out = jnp.where((quadrant & 2) == 2, -sine_out, sine_out)
    cosine_out = jnp.where(((quadrant + 1) & 2) == 2, -cosine_out, cosine_out)
    return sine_out, cosine_out


def green_kernel(panel_ref, point_ref, out_ref, total_ref):
    chunks = panel_ref.shape[0]
    points = point_ref.shape[1]
    for group in range(points // GROUP):
        rows = pl.ds(group * GROUP, GROUP)
        point_x = point_ref[0, rows, :]
        point_y = point_ref[1, rows, :]
        point_z = point_ref[2, rows, :]

        def body(chunk, carry):
            real_sum, imag_sum = carry
            block = panel_ref[chunk]
            shape = (GROUP, block.shape[1])
            strength_re = jnp.broadcast_to(block[0:1], shape)
            strength_im = jnp.broadcast_to(block[1:2], shape)
            delta_x = point_x - jnp.broadcast_to(block[2:3], shape)
            delta_y = point_y - jnp.broadcast_to(block[3:4], shape)
            delta_z = point_z - jnp.broadcast_to(block[4:5], shape)
            distance = jnp.sqrt(delta_x * delta_x + delta_y * delta_y + delta_z * delta_z)
            inverse = 1.0 / (FOUR_PI * distance)
            sine, cosine = sine_cosine(WAVENUMBER * distance)
            cosine_part = cosine * inverse
            sine_part = sine * inverse
            real_sum = real_sum + (strength_re * cosine_part - strength_im * sine_part)
            imag_sum = imag_sum + (strength_re * sine_part + strength_im * cosine_part)
            return real_sum, imag_sum

        zero = jnp.zeros((GROUP, panel_ref.shape[2]), jnp.float32)
        real_sum, imag_sum = lax.fori_loop(0, chunks, body, (zero, zero), unroll=2)
        total_ref[0, rows, :] = real_sum
        total_ref[1, rows, :] = imag_sum
    out_ref[0:1, :] = jnp.sum(total_ref[0].T, axis=0, keepdims=True)
    out_ref[1:2, :] = jnp.sum(total_ref[1].T, axis=0, keepdims=True)


def green(panels, field_points):
    points = field_points.shape[1]
    lanes = panels.shape[2]
    spread = jnp.broadcast_to(field_points[:, :, None], (3, points, lanes))
    pairs = panels.shape[0] * lanes * points
    return pl.pallas_call(
        green_kernel,
        out_shape=jax.ShapeDtypeStruct((2, points), jnp.float32),
        in_specs=[pl.BlockSpec(memory_space=pltpu.VMEM)] * 2,
        out_specs=pl.BlockSpec(memory_space=pltpu.VMEM),
        scratch_shapes=[pltpu.VMEM((2, points, lanes), jnp.float32)],
        cost_estimate=pl.CostEstimate(flops=70 * pairs, transcendentals=2 * pairs, bytes_accessed=4 * (panels.size + spread.size + 2 * points)),
    )(panels, spread)


def parts_kernel(panel_ref, point_ref, cosine_ref, sine_ref):
    points = point_ref.shape[1]

    def body(chunk, carry):
        block = panel_ref[chunk]
        shape = (GROUP, block.shape[1])
        centroid_x = jnp.broadcast_to(block[2:3], shape)
        centroid_y = jnp.broadcast_to(block[3:4], shape)
        centroid_z = jnp.broadcast_to(block[4:5], shape)
        for group in range(points // GROUP):
            rows = pl.ds(group * GROUP, GROUP)
            delta_x = point_ref[0, rows, :] - centroid_x
            delta_y = point_ref[1, rows, :] - centroid_y
            delta_z = point_ref[2, rows, :] - centroid_z
            distance = jnp.sqrt(delta_x * delta_x + delta_y * delta_y + delta_z * delta_z)
            inverse = 1.0 / (FOUR_PI * distance)
            sine, cosine = sine_cosine(WAVENUMBER * distance)
            cosine_ref[chunk, rows, :] = cosine * inverse
            sine_ref[chunk, rows, :] = sine * inverse
        return carry

    lax.fori_loop(0, panel_ref.shape[0], body, 0)


def contract_kernel(velocity_ref, area_ref, cosine_ref, sine_ref, out_ref, real_ref, imag_ref):
    step = pl.program_id(0)
    per_step = cosine_ref.shape[0]

    @pl.when(step == 0)
    def _():
        real_ref[...] = jnp.zeros_like(real_ref)
        imag_ref[...] = jnp.zeros_like(imag_ref)

    def body(chunk, carry):
        panel_chunk = step * per_step + chunk
        velocity = velocity_ref[panel_chunk]
        area = area_ref[panel_chunk]
        shape = real_ref.shape
        strength_re = jnp.broadcast_to(-area[0:1] * velocity[1:2], shape)
        strength_im = jnp.broadcast_to(area[0:1] * velocity[0:1], shape)
        cosine_part = cosine_ref[chunk]
        sine_part = sine_ref[chunk]
        real_ref[...] += strength_re * cosine_part - strength_im * sine_part
        imag_ref[...] += strength_re * sine_part + strength_im * cosine_part
        return carry

    lax.fori_loop(0, per_step, body, 0)

    @pl.when(step == pl.num_programs(0) - 1)
    def _():
        out_ref[0:1, :] = jnp.sum(real_ref[...].T, axis=0, keepdims=True)
        out_ref[1:2, :] = jnp.sum(imag_ref[...].T, axis=0, keepdims=True)


def kernel_parts(panels, field_points):
    chunks, rows, lanes = panels.shape
    points = field_points.shape[1]
    spread = jnp.broadcast_to(field_points[:, :, None], (3, points, lanes))
    pairs = chunks * lanes * points
    part = jax.ShapeDtypeStruct((chunks, points, lanes), jnp.float32)
    return pl.pallas_call(
        parts_kernel,
        out_shape=(part, part),
        grid=(chunks // PARTS_STEP,),
        in_specs=[
            pl.BlockSpec((PARTS_STEP, rows, lanes), lambda c: (c, 0, 0)),
            pl.BlockSpec((3, points, lanes), lambda c: (0, 0, 0)),
        ],
        out_specs=[pl.BlockSpec((PARTS_STEP, points, lanes), lambda c: (c, 0, 0))] * 2,
        cost_estimate=pl.CostEstimate(flops=60 * pairs, transcendentals=2 * pairs, bytes_accessed=8 * pairs),
    )(panels, spread)


def contract(velocity, area, cosine_part, sine_part):
    chunks, points, lanes = cosine_part.shape
    return pl.pallas_call(
        contract_kernel,
        out_shape=jax.ShapeDtypeStruct((2, points), jnp.float32),
        grid=(chunks // CONTRACT_STEP,),
        in_specs=[
            pl.BlockSpec(memory_space=pltpu.VMEM),
            pl.BlockSpec(memory_space=pltpu.VMEM),
            pl.BlockSpec((CONTRACT_STEP, points, lanes), lambda c: (c, 0, 0)),
            pl.BlockSpec((CONTRACT_STEP, points, lanes), lambda c: (c, 0, 0)),
        ],
        out_specs=pl.BlockSpec((2, points), lambda c: (0, 0)),
        scratch_shapes=[pltpu.VMEM((points, lanes), jnp.float32)] * 2,
        cost_estimate=pl.CostEstimate(flops=8 * chunks * points * lanes, transcendentals=0, bytes_accessed=8 * chunks * points * lanes),
    )(
        pltpu.with_memory_space_constraint(velocity, pltpu.VMEM),
        pltpu.with_memory_space_constraint(area, pltpu.VMEM),
        cosine_part,
        sine_part,
    )


def shards(node_velocity, node_owner, node_panel, panel_centroid, panel_area, field_points):
    slab_count = lax.axis_size("panel")
    slab_width = panel_area.shape[0]
    destination = node_owner[:, 0]
    owner_hot = (destination[None, :] == jnp.arange(slab_count, dtype=jnp.int32)[:, None]).astype(
        jnp.float32
    )
    weighted = (node_velocity[:, None, :] * owner_hot[None, :, :]).reshape(2 * slab_count, -1)
    panel_hot = (node_panel[:, None] == jnp.arange(slab_width, dtype=jnp.int32)[None, :]).astype(
        jnp.float32
    )
    partial = jnp.dot(
        weighted, panel_hot, precision=lax.Precision.HIGHEST, preferred_element_type=jnp.float32
    )
    partial = partial.reshape(2, slab_count, slab_width).transpose(1, 0, 2)
    extra = jnp.concatenate([panel_centroid, panel_area[None]], axis=0)
    extra_copies = jnp.broadcast_to(extra[None], (slab_count,) + extra.shape)
    outgoing = jnp.concatenate([partial, extra_copies], axis=1)
    got = lax.all_to_all(outgoing, "panel", split_axis=0, concat_axis=0, tiled=True)
    cosine_part, sine_part = kernel_parts(got, field_points)
    column = jnp.sum(got[:, 0:2], axis=0)
    point_count = lax.axis_size("point")
    copies = jnp.broadcast_to(column[None], (point_count,) + column.shape)
    velocity = jnp.sum(lax.all_to_all(copies, "point", split_axis=0, concat_axis=0, tiled=True), axis=0)
    spread = jnp.broadcast_to(velocity[None], (slab_count,) + velocity.shape)
    gathered = lax.all_to_all(spread, "panel", split_axis=0, concat_axis=0, tiled=True)
    return contract(gathered, got[:, 5:6], cosine_part, sine_part)


def solution(mesh):
    return jax.shard_map(
        shards,
        mesh=mesh,
        in_specs=(
            P(None, ("panel", "point")),
            P(("panel", "point"), None),
            P(("panel", "point")),
            P(None, "panel"),
            P("panel"),
            P(None, ("panel", "point")),
        ),
        out_specs=P(None, ("panel", "point")),
        check_vma=False,
    )
```

```python
import math

import jax
import jax.numpy as jnp
from jax import lax
from jax.experimental import pallas as pl
from jax.experimental.pallas import tpu as pltpu
from jax.sharding import PartitionSpec as P

WAVENUMBER = 40.0
FOUR_PI = 4.0 * math.pi


TWO_OVER_PI = 2.0 / math.pi
HALF_PI_1 = 1.5703125
HALF_PI_2 = 4.837512969970703125e-4
HALF_PI_3 = 7.54978995489188216e-8
GROUP = 16
PARTS_STEP = 8
CONTRACT_STEP = 16


def sine_cosine(angle):
    turns = jnp.floor(angle * TWO_OVER_PI + 0.5)
    rest = ((angle - turns * HALF_PI_1) - turns * HALF_PI_2) - turns * HALF_PI_3
    square = rest * rest
    sine = rest + rest * square * (
        -1.6666654611e-1 + square * (8.3321608736e-3 + square * -1.9515295891e-4)
    )
    cosine = 1.0 - 0.5 * square + square * square * (
        4.166664568298827e-2 + square * (-1.388731625493765e-3 + square * 2.443315711809948e-5)
    )
    quadrant = turns.astype(jnp.int32)
    swap = (quadrant & 1) == 1
    sine_out = jnp.where(swap, cosine, sine)
    cosine_out = jnp.where(swap, sine, cosine)
    sine_out = jnp.where((quadrant & 2) == 2, -sine_out, sine_out)
    cosine_out = jnp.where(((quadrant + 1) & 2) == 2, -cosine_out, cosine_out)
    return sine_out, cosine_out


def green_kernel(panel_ref, point_ref, out_ref, total_ref):
    chunks = panel_ref.shape[0]
    points = point_ref.shape[1]
    for group in range(points // GROUP):
        rows = pl.ds(group * GROUP, GROUP)
        point_x = point_ref[0, rows, :]
        point_y = point_ref[1, rows, :]
        point_z = point_ref[2, rows, :]

        def body(chunk, carry):
            real_sum, imag_sum = carry
            block = panel_ref[chunk]
            shape = (GROUP, block.shape[1])
            strength_re = jnp.broadcast_to(block[0:1], shape)
            strength_im = jnp.broadcast_to(block[1:2], shape)
            delta_x = point_x - jnp.broadcast_to(block[2:3], shape)
            delta_y = point_y - jnp.broadcast_to(block[3:4], shape)
            delta_z = point_z - jnp.broadcast_to(block[4:5], shape)
            distance = jnp.sqrt(delta_x * delta_x + delta_y * delta_y + delta_z * delta_z)
            inverse = 1.0 / (FOUR_PI * distance)
            sine, cosine = sine_cosine(WAVENUMBER * distance)
            cosine_part = cosine * inverse
            sine_part = sine * inverse
            real_sum = real_sum + (strength_re * cosine_part - strength_im * sine_part)
            imag_sum = imag_sum + (strength_re * sine_part + strength_im * cosine_part)
            return real_sum, imag_sum

        zero = jnp.zeros((GROUP, panel_ref.shape[2]), jnp.float32)
        real_sum, imag_sum = lax.fori_loop(0, chunks, body, (zero, zero), unroll=2)
        total_ref[0, rows, :] = real_sum
        total_ref[1, rows, :] = imag_sum
    out_ref[0:1, :] = jnp.sum(total_ref[0].T, axis=0, keepdims=True)
    out_ref[1:2, :] = jnp.sum(total_ref[1].T, axis=0, keepdims=True)


def green(panels, field_points):
    points = field_points.shape[1]
    lanes = panels.shape[2]
    spread = jnp.broadcast_to(field_points[:, :, None], (3, points, lanes))
    pairs = panels.shape[0] * lanes * points
    return pl.pallas_call(
        green_kernel,
        out_shape=jax.ShapeDtypeStruct((2, points), jnp.float32),
        in_specs=[pl.BlockSpec(memory_space=pltpu.VMEM)] * 2,
        out_specs=pl.BlockSpec(memory_space=pltpu.VMEM),
        scratch_shapes=[pltpu.VMEM((2, points, lanes), jnp.float32)],
        cost_estimate=pl.CostEstimate(flops=70 * pairs, transcendentals=2 * pairs, bytes_accessed=4 * (panels.size + spread.size + 2 * points)),
    )(panels, spread)


def parts_kernel(panel_ref, coordinate_ref, cosine_ref, sine_ref, point_ref):
    points = point_ref.shape[1]

    @pl.when(pl.program_id(0) == 0)
    def _():
        for axis in range(3):
            row = coordinate_ref[axis:axis + 1, :]
            point_ref[axis] = jnp.broadcast_to(row, (point_ref.shape[2], points)).T

    def body(chunk, carry):
        block = panel_ref[chunk]
        shape = (GROUP, block.shape[1])
        centroid_x = jnp.broadcast_to(block[2:3], shape)
        centroid_y = jnp.broadcast_to(block[3:4], shape)
        centroid_z = jnp.broadcast_to(block[4:5], shape)
        for group in range(points // GROUP):
            rows = pl.ds(group * GROUP, GROUP)
            delta_x = point_ref[0, rows, :] - centroid_x
            delta_y = point_ref[1, rows, :] - centroid_y
            delta_z = point_ref[2, rows, :] - centroid_z
            distance = jnp.sqrt(delta_x * delta_x + delta_y * delta_y + delta_z * delta_z)
            inverse = 1.0 / (FOUR_PI * distance)
            sine, cosine = sine_cosine(WAVENUMBER * distance)
            cosine_ref[chunk, rows, :] = cosine * inverse
            sine_ref[chunk, rows, :] = sine * inverse
        return carry

    lax.fori_loop(0, panel_ref.shape[0], body, 0)


def contract_kernel(velocity_ref, area_ref, cosine_ref, sine_ref, out_ref, real_ref, imag_ref):
    step = pl.program_id(0)
    per_step = cosine_ref.shape[0]

    @pl.when(step == 0)
    def _():
        real_ref[...] = jnp.zeros_like(real_ref)
        imag_ref[...] = jnp.zeros_like(imag_ref)

    def body(chunk, carry):
        panel_chunk = step * per_step + chunk
        velocity = velocity_ref[panel_chunk]
        area = area_ref[panel_chunk]
        shape = real_ref.shape
        strength_re = jnp.broadcast_to(-area[0:1] * velocity[1:2], shape)
        strength_im = jnp.broadcast_to(area[0:1] * velocity[0:1], shape)
        cosine_part = cosine_ref[chunk]
        sine_part = sine_ref[chunk]
        real_ref[...] += strength_re * cosine_part - strength_im * sine_part
        imag_ref[...] += strength_re * sine_part + strength_im * cosine_part
        return carry

    lax.fori_loop(0, per_step, body, 0)

    @pl.when(step == pl.num_programs(0) - 1)
    def _():
        out_ref[0:1, :] = jnp.sum(real_ref[...].T, axis=0, keepdims=True)
        out_ref[1:2, :] = jnp.sum(imag_ref[...].T, axis=0, keepdims=True)


def kernel_parts(panels, field_points):
    chunks, rows, lanes = panels.shape
    points = field_points.shape[1]
    pairs = chunks * lanes * points
    part = jax.ShapeDtypeStruct((chunks, points, lanes), jnp.float32)
    return pl.pallas_call(
        parts_kernel,
        out_shape=(part, part),
        grid=(chunks // PARTS_STEP,),
        in_specs=[
            pl.BlockSpec((PARTS_STEP, rows, lanes), lambda c: (c, 0, 0)),
            pl.BlockSpec(memory_space=pltpu.VMEM),
        ],
        out_specs=[pl.BlockSpec((PARTS_STEP, points, lanes), lambda c: (c, 0, 0))] * 2,
        scratch_shapes=[pltpu.VMEM((3, points, lanes), jnp.float32)],
        compiler_params=pltpu.CompilerParams(dimension_semantics=("arbitrary",)),
        cost_estimate=pl.CostEstimate(flops=60 * pairs, transcendentals=2 * pairs, bytes_accessed=8 * pairs),
    )(panels, pltpu.with_memory_space_constraint(field_points, pltpu.VMEM))


def contract(velocity, area, cosine_part, sine_part):
    chunks, points, lanes = cosine_part.shape
    return pl.pallas_call(
        contract_kernel,
        out_shape=jax.ShapeDtypeStruct((2, points), jnp.float32),
        grid=(chunks // CONTRACT_STEP,),
        in_specs=[
            pl.BlockSpec(memory_space=pltpu.VMEM),
            pl.BlockSpec(memory_space=pltpu.VMEM),
            pl.BlockSpec((CONTRACT_STEP, points, lanes), lambda c: (c, 0, 0)),
            pl.BlockSpec((CONTRACT_STEP, points, lanes), lambda c: (c, 0, 0)),
        ],
        out_specs=pl.BlockSpec((2, points), lambda c: (0, 0)),
        scratch_shapes=[pltpu.VMEM((points, lanes), jnp.float32)] * 2,
        cost_estimate=pl.CostEstimate(flops=8 * chunks * points * lanes, transcendentals=0, bytes_accessed=8 * chunks * points * lanes),
    )(
        pltpu.with_memory_space_constraint(velocity, pltpu.VMEM),
        pltpu.with_memory_space_constraint(area, pltpu.VMEM),
        cosine_part,
        sine_part,
    )


def shards(node_velocity, node_owner, node_panel, panel_centroid, panel_area, field_points):
    slab_count = lax.axis_size("panel")
    slab_width = panel_area.shape[0]
    destination = node_owner[:, 0]
    owner_hot = (destination[None, :] == jnp.arange(slab_count, dtype=jnp.int32)[:, None]).astype(
        jnp.float32
    )
    weighted = (node_velocity[:, None, :] * owner_hot[None, :, :]).reshape(2 * slab_count, -1)
    panel_hot = (node_panel[:, None] == jnp.arange(slab_width, dtype=jnp.int32)[None, :]).astype(
        jnp.float32
    )
    partial = jnp.dot(
        weighted, panel_hot, precision=lax.Precision.HIGHEST, preferred_element_type=jnp.float32
    )
    partial = partial.reshape(2, slab_count, slab_width).transpose(1, 0, 2)
    extra = jnp.concatenate([panel_centroid, panel_area[None]], axis=0)
    extra_copies = jnp.broadcast_to(extra[None], (slab_count,) + extra.shape)
    outgoing = jnp.concatenate([partial, extra_copies], axis=1)
    got = lax.all_to_all(outgoing, "panel", split_axis=0, concat_axis=0, tiled=True)
    cosine_part, sine_part = kernel_parts(got, field_points)
    column = jnp.sum(got[:, 0:2], axis=0)
    point_count = lax.axis_size("point")
    copies = jnp.broadcast_to(column[None], (point_count,) + column.shape)
    velocity = jnp.sum(lax.all_to_all(copies, "point", split_axis=0, concat_axis=0, tiled=True), axis=0)
    spread = jnp.broadcast_to(velocity[None], (slab_count,) + velocity.shape)
    gathered = lax.all_to_all(spread, "panel", split_axis=0, concat_axis=0, tiled=True)
    return contract(gathered, got[:, 5:6], cosine_part, sine_part)


def solution(mesh):
    return jax.shard_map(
        shards,
        mesh=mesh,
        in_specs=(
            P(None, ("panel", "point")),
            P(("panel", "point"), None),
            P(("panel", "point")),
            P(None, "panel"),
            P("panel"),
            P(None, ("panel", "point")),
        ),
        out_specs=P(None, ("panel", "point")),
        check_vma=False,
    )
```

```python
import math

import jax
import jax.numpy as jnp
from jax import lax
from jax.experimental import pallas as pl
from jax.experimental.pallas import tpu as pltpu
from jax.sharding import PartitionSpec as P

WAVENUMBER = 40.0
FOUR_PI = 4.0 * math.pi


TWO_OVER_PI = 2.0 / math.pi
HALF_PI_1 = 1.5703125
HALF_PI_2 = 4.837512969970703125e-4
HALF_PI_3 = 7.54978995489188216e-8
GROUP = 16
PARTS_STEP = 8
STORED_CHUNKS = 48


def sine_cosine(angle):
    turns = jnp.floor(angle * TWO_OVER_PI + 0.5)
    rest = ((angle - turns * HALF_PI_1) - turns * HALF_PI_2) - turns * HALF_PI_3
    square = rest * rest
    sine = rest + rest * square * (
        -1.6666654611e-1 + square * (8.3321608736e-3 + square * -1.9515295891e-4)
    )
    cosine = 1.0 - 0.5 * square + square * square * (
        4.166664568298827e-2 + square * (-1.388731625493765e-3 + square * 2.443315711809948e-5)
    )
    quadrant = turns.astype(jnp.int32)
    swap = (quadrant & 1) == 1
    sine_out = jnp.where(swap, cosine, sine)
    cosine_out = jnp.where(swap, sine, cosine)
    sine_out = jnp.where((quadrant & 2) == 2, -sine_out, sine_out)
    cosine_out = jnp.where(((quadrant + 1) & 2) == 2, -cosine_out, cosine_out)
    return sine_out, cosine_out


def green_kernel(panel_ref, point_ref, out_ref, total_ref):
    chunks = panel_ref.shape[0]
    points = point_ref.shape[1]
    for group in range(points // GROUP):
        rows = pl.ds(group * GROUP, GROUP)
        point_x = point_ref[0, rows, :]
        point_y = point_ref[1, rows, :]
        point_z = point_ref[2, rows, :]

        def body(chunk, carry):
            real_sum, imag_sum = carry
            block = panel_ref[chunk]
            shape = (GROUP, block.shape[1])
            strength_re = jnp.broadcast_to(block[0:1], shape)
            strength_im = jnp.broadcast_to(block[1:2], shape)
            delta_x = point_x - jnp.broadcast_to(block[2:3], shape)
            delta_y = point_y - jnp.broadcast_to(block[3:4], shape)
            delta_z = point_z - jnp.broadcast_to(block[4:5], shape)
            distance = jnp.sqrt(delta_x * delta_x + delta_y * delta_y + delta_z * delta_z)
            inverse = 1.0 / (FOUR_PI * distance)
            sine, cosine = sine_cosine(WAVENUMBER * distance)
            cosine_part = cosine * inverse
            sine_part = sine * inverse
            real_sum = real_sum + (strength_re * cosine_part - strength_im * sine_part)
            imag_sum = imag_sum + (strength_re * sine_part + strength_im * cosine_part)
            return real_sum, imag_sum

        zero = jnp.zeros((GROUP, panel_ref.shape[2]), jnp.float32)
        real_sum, imag_sum = lax.fori_loop(0, chunks, body, (zero, zero), unroll=2)
        total_ref[0, rows, :] = real_sum
        total_ref[1, rows, :] = imag_sum
    out_ref[0:1, :] = jnp.sum(total_ref[0].T, axis=0, keepdims=True)
    out_ref[1:2, :] = jnp.sum(total_ref[1].T, axis=0, keepdims=True)


def green(panels, field_points):
    points = field_points.shape[1]
    lanes = panels.shape[2]
    spread = jnp.broadcast_to(field_points[:, :, None], (3, points, lanes))
    pairs = panels.shape[0] * lanes * points
    return pl.pallas_call(
        green_kernel,
        out_shape=jax.ShapeDtypeStruct((2, points), jnp.float32),
        in_specs=[pl.BlockSpec(memory_space=pltpu.VMEM)] * 2,
        out_specs=pl.BlockSpec(memory_space=pltpu.VMEM),
        scratch_shapes=[pltpu.VMEM((2, points, lanes), jnp.float32)],
        cost_estimate=pl.CostEstimate(flops=70 * pairs, transcendentals=2 * pairs, bytes_accessed=4 * (panels.size + spread.size + 2 * points)),
    )(panels, spread)


def parts_kernel(panel_ref, coordinate_ref, cosine_ref, sine_ref, point_ref):
    points = point_ref.shape[1]

    @pl.when(pl.program_id(0) == 0)
    def _():
        point_lanes(coordinate_ref, point_ref)

    def body(chunk, carry):
        block = panel_ref[chunk]
        shape = (GROUP, block.shape[1])
        centroid_x = jnp.broadcast_to(block[2:3], shape)
        centroid_y = jnp.broadcast_to(block[3:4], shape)
        centroid_z = jnp.broadcast_to(block[4:5], shape)
        for group in range(points // GROUP):
            rows = pl.ds(group * GROUP, GROUP)
            delta_x = point_ref[0, rows, :] - centroid_x
            delta_y = point_ref[1, rows, :] - centroid_y
            delta_z = point_ref[2, rows, :] - centroid_z
            distance = jnp.sqrt(delta_x * delta_x + delta_y * delta_y + delta_z * delta_z)
            inverse = 1.0 / (FOUR_PI * distance)
            sine, cosine = sine_cosine(WAVENUMBER * distance)
            cosine_ref[chunk, rows, :] = cosine * inverse
            sine_ref[chunk, rows, :] = sine * inverse
        return carry

    lax.fori_loop(0, panel_ref.shape[0], body, 0)


def point_lanes(coordinate_ref, point_ref):
    for axis in range(3):
        row = coordinate_ref[axis:axis + 1, :]
        point_ref[axis] = jnp.broadcast_to(row, (point_ref.shape[2], point_ref.shape[1])).T


def finish_kernel(velocity_ref, area_ref, panel_ref, coordinate_ref, cosine_hbm, sine_hbm, out_ref,
                  cosine_buf, sine_buf, point_ref, real_ref, imag_ref, sems):
    stored = cosine_hbm.shape[0]
    chunks = panel_ref.shape[0]
    points = point_ref.shape[1]
    groups = stored // PARTS_STEP

    def copies(group):
        window = pl.ds(group * PARTS_STEP, PARTS_STEP)
        return (
            pltpu.make_async_copy(cosine_hbm.at[window], cosine_buf.at[window], sems.at[0, group]),
            pltpu.make_async_copy(sine_hbm.at[window], sine_buf.at[window], sems.at[1, group]),
        )

    for group in range(groups):
        for copy in copies(group):
            copy.start()
    point_lanes(coordinate_ref, point_ref)
    real_ref[...] = jnp.zeros_like(real_ref)
    imag_ref[...] = jnp.zeros_like(imag_ref)

    def strengths(chunk, shape):
        velocity = velocity_ref[chunk]
        area = area_ref[chunk]
        strength_re = jnp.broadcast_to(-area[0:1] * velocity[1:2], shape)
        strength_im = jnp.broadcast_to(area[0:1] * velocity[0:1], shape)
        return strength_re, strength_im

    def fresh(chunk, carry):
        block = panel_ref[chunk]
        shape = (GROUP, block.shape[1])
        strength_re, strength_im = strengths(chunk, shape)
        centroid_x = jnp.broadcast_to(block[2:3], shape)
        centroid_y = jnp.broadcast_to(block[3:4], shape)
        centroid_z = jnp.broadcast_to(block[4:5], shape)
        for group in range(points // GROUP):
            rows = pl.ds(group * GROUP, GROUP)
            delta_x = point_ref[0, rows, :] - centroid_x
            delta_y = point_ref[1, rows, :] - centroid_y
            delta_z = point_ref[2, rows, :] - centroid_z
            distance = jnp.sqrt(delta_x * delta_x + delta_y * delta_y + delta_z * delta_z)
            inverse = 1.0 / (FOUR_PI * distance)
            sine, cosine = sine_cosine(WAVENUMBER * distance)
            cosine_part = cosine * inverse
            sine_part = sine * inverse
            real_ref[rows, :] += strength_re * cosine_part - strength_im * sine_part
            imag_ref[rows, :] += strength_re * sine_part + strength_im * cosine_part
        return carry

    lax.fori_loop(stored, chunks, fresh, 0)

    def saved(chunk, carry):
        strength_re, strength_im = strengths(chunk, real_ref.shape)
        cosine_part = cosine_buf[chunk]
        sine_part = sine_buf[chunk]
        real_ref[...] += strength_re * cosine_part - strength_im * sine_part
        imag_ref[...] += strength_re * sine_part + strength_im * cosine_part
        return carry

    for group in range(groups):
        for copy in copies(group):
            copy.wait()
        lax.fori_loop(group * PARTS_STEP, (group + 1) * PARTS_STEP, saved, 0)
    out_ref[0:1, :] = jnp.sum(real_ref[...].T, axis=0, keepdims=True)
    out_ref[1:2, :] = jnp.sum(imag_ref[...].T, axis=0, keepdims=True)


def kernel_parts(panels, field_points, chunks):
    rows, lanes = panels.shape[1:]
    points = field_points.shape[1]
    pairs = chunks * lanes * points
    part = jax.ShapeDtypeStruct((chunks, points, lanes), jnp.float32)
    return pl.pallas_call(
        parts_kernel,
        out_shape=(part, part),
        grid=(chunks // PARTS_STEP,),
        in_specs=[
            pl.BlockSpec((PARTS_STEP, rows, lanes), lambda c: (c, 0, 0)),
            pl.BlockSpec(memory_space=pltpu.VMEM),
        ],
        out_specs=[pl.BlockSpec((PARTS_STEP, points, lanes), lambda c: (c, 0, 0))] * 2,
        scratch_shapes=[pltpu.VMEM((3, points, lanes), jnp.float32)],
        compiler_params=pltpu.CompilerParams(dimension_semantics=("arbitrary",)),
        cost_estimate=pl.CostEstimate(flops=60 * pairs, transcendentals=2 * pairs, bytes_accessed=8 * pairs),
    )(panels, pltpu.with_memory_space_constraint(field_points, pltpu.VMEM))


def finish(velocity, area, panels, field_points, cosine_part, sine_part):
    stored, points, lanes = cosine_part.shape
    chunks = panels.shape[0]
    pairs = (chunks - stored) * points * lanes
    vmem = lambda x: pltpu.with_memory_space_constraint(x, pltpu.VMEM)
    return pl.pallas_call(
        finish_kernel,
        out_shape=jax.ShapeDtypeStruct((2, points), jnp.float32),
        in_specs=[pl.BlockSpec(memory_space=pltpu.VMEM)] * 4 + [pl.BlockSpec(memory_space=pl.ANY)] * 2,
        out_specs=pl.BlockSpec(memory_space=pltpu.VMEM),
        scratch_shapes=[pltpu.VMEM((stored, points, lanes), jnp.float32)] * 2
        + [pltpu.VMEM((3, points, lanes), jnp.float32)]
        + [pltpu.VMEM((points, lanes), jnp.float32)] * 2
        + [pltpu.SemaphoreType.DMA((2, stored // PARTS_STEP))],
        cost_estimate=pl.CostEstimate(
            flops=70 * pairs + 8 * stored * points * lanes,
            transcendentals=2 * pairs,
            bytes_accessed=8 * stored * points * lanes,
        ),
    )(vmem(velocity), vmem(area), vmem(panels), vmem(field_points), cosine_part, sine_part)


def shards(node_velocity, node_owner, node_panel, panel_centroid, panel_area, field_points):
    slab_count = lax.axis_size("panel")
    slab_width = panel_area.shape[0]
    destination = node_owner[:, 0]
    owner_hot = (destination[None, :] == jnp.arange(slab_count, dtype=jnp.int32)[:, None]).astype(
        jnp.float32
    )
    weighted = (node_velocity[:, None, :] * owner_hot[None, :, :]).reshape(2 * slab_count, -1)
    panel_hot = (node_panel[:, None] == jnp.arange(slab_width, dtype=jnp.int32)[None, :]).astype(
        jnp.float32
    )
    partial = jnp.dot(
        weighted, panel_hot, precision=lax.Precision.HIGHEST, preferred_element_type=jnp.float32
    )
    partial = partial.reshape(2, slab_count, slab_width).transpose(1, 0, 2)
    extra = jnp.concatenate([panel_centroid, panel_area[None]], axis=0)
    extra_copies = jnp.broadcast_to(extra[None], (slab_count,) + extra.shape)
    outgoing = jnp.concatenate([partial, extra_copies], axis=1)
    got = lax.all_to_all(outgoing, "panel", split_axis=0, concat_axis=0, tiled=True)
    cosine_part, sine_part = kernel_parts(got, field_points, STORED_CHUNKS)
    column = jnp.sum(got[:, 0:2], axis=0)
    point_count = lax.axis_size("point")
    copies = jnp.broadcast_to(column[None], (point_count,) + column.shape)
    velocity = jnp.sum(lax.all_to_all(copies, "point", split_axis=0, concat_axis=0, tiled=True), axis=0)
    spread = jnp.broadcast_to(velocity[None], (slab_count,) + velocity.shape)
    gathered = lax.all_to_all(spread, "panel", split_axis=0, concat_axis=0, tiled=True)
    return finish(gathered, got[:, 5:6], got, field_points, cosine_part, sine_part)


def solution(mesh):
    return jax.shard_map(
        shards,
        mesh=mesh,
        in_specs=(
            P(None, ("panel", "point")),
            P(("panel", "point"), None),
            P(("panel", "point")),
            P(None, "panel"),
            P("panel"),
            P(None, ("panel", "point")),
        ),
        out_specs=P(None, ("panel", "point")),
        check_vma=False,
    )
```

```python
import math

import jax
import jax.numpy as jnp
from jax import lax
from jax.experimental import pallas as pl
from jax.experimental.pallas import tpu as pltpu
from jax.sharding import PartitionSpec as P

WAVENUMBER = 40.0
FOUR_PI = 4.0 * math.pi


TWO_OVER_PI = 2.0 / math.pi
HALF_PI_1 = 1.5703125
HALF_PI_2 = 4.837512969970703125e-4
HALF_PI_3 = 7.54978995489188216e-8
GROUP = 16
PARTS_STEP = 8
STORED_CHUNKS = 48


def sine_cosine(angle):
    turns = jnp.floor(angle * TWO_OVER_PI + 0.5)
    rest = ((angle - turns * HALF_PI_1) - turns * HALF_PI_2) - turns * HALF_PI_3
    square = rest * rest
    sine = rest + rest * square * (
        -1.6666654611e-1 + square * (8.3321608736e-3 + square * -1.9515295891e-4)
    )
    cosine = 1.0 - 0.5 * square + square * square * (
        4.166664568298827e-2 + square * (-1.388731625493765e-3 + square * 2.443315711809948e-5)
    )
    quadrant = turns.astype(jnp.int32)
    swap = (quadrant & 1) == 1
    sine_out = jnp.where(swap, cosine, sine)
    cosine_out = jnp.where(swap, sine, cosine)
    sine_out = jnp.where((quadrant & 2) == 2, -sine_out, sine_out)
    cosine_out = jnp.where(((quadrant + 1) & 2) == 2, -cosine_out, cosine_out)
    return sine_out, cosine_out


def green_kernel(panel_ref, point_ref, out_ref, total_ref):
    chunks = panel_ref.shape[0]
    points = point_ref.shape[1]
    for group in range(points // GROUP):
        rows = pl.ds(group * GROUP, GROUP)
        point_x = point_ref[0, rows, :]
        point_y = point_ref[1, rows, :]
        point_z = point_ref[2, rows, :]

        def body(chunk, carry):
            real_sum, imag_sum = carry
            block = panel_ref[chunk]
            shape = (GROUP, block.shape[1])
            strength_re = jnp.broadcast_to(block[0:1], shape)
            strength_im = jnp.broadcast_to(block[1:2], shape)
            delta_x = point_x - jnp.broadcast_to(block[2:3], shape)
            delta_y = point_y - jnp.broadcast_to(block[3:4], shape)
            delta_z = point_z - jnp.broadcast_to(block[4:5], shape)
            distance = jnp.sqrt(delta_x * delta_x + delta_y * delta_y + delta_z * delta_z)
            inverse = 1.0 / (FOUR_PI * distance)
            sine, cosine = sine_cosine(WAVENUMBER * distance)
            cosine_part = cosine * inverse
            sine_part = sine * inverse
            real_sum = real_sum + (strength_re * cosine_part - strength_im * sine_part)
            imag_sum = imag_sum + (strength_re * sine_part + strength_im * cosine_part)
            return real_sum, imag_sum

        zero = jnp.zeros((GROUP, panel_ref.shape[2]), jnp.float32)
        real_sum, imag_sum = lax.fori_loop(0, chunks, body, (zero, zero), unroll=2)
        total_ref[0, rows, :] = real_sum
        total_ref[1, rows, :] = imag_sum
    out_ref[0:1, :] = jnp.sum(total_ref[0].T, axis=0, keepdims=True)
    out_ref[1:2, :] = jnp.sum(total_ref[1].T, axis=0, keepdims=True)


def green(panels, field_points):
    points = field_points.shape[1]
    lanes = panels.shape[2]
    spread = jnp.broadcast_to(field_points[:, :, None], (3, points, lanes))
    pairs = panels.shape[0] * lanes * points
    return pl.pallas_call(
        green_kernel,
        out_shape=jax.ShapeDtypeStruct((2, points), jnp.float32),
        in_specs=[pl.BlockSpec(memory_space=pltpu.VMEM)] * 2,
        out_specs=pl.BlockSpec(memory_space=pltpu.VMEM),
        scratch_shapes=[pltpu.VMEM((2, points, lanes), jnp.float32)],
        cost_estimate=pl.CostEstimate(flops=70 * pairs, transcendentals=2 * pairs, bytes_accessed=4 * (panels.size + spread.size + 2 * points)),
    )(panels, spread)


def parts_kernel(panel_ref, coordinate_ref, cosine_ref, sine_ref, point_ref):
    points = point_ref.shape[1]

    @pl.when(pl.program_id(0) == 0)
    def _():
        point_lanes(coordinate_ref, point_ref)

    first = pl.program_id(0) * cosine_ref.shape[0]

    def body(chunk, carry):
        block = panel_ref[first + chunk]
        shape = (GROUP, block.shape[1])
        centroid_x = jnp.broadcast_to(block[2:3], shape)
        centroid_y = jnp.broadcast_to(block[3:4], shape)
        centroid_z = jnp.broadcast_to(block[4:5], shape)
        for group in range(points // GROUP):
            rows = pl.ds(group * GROUP, GROUP)
            delta_x = point_ref[0, rows, :] - centroid_x
            delta_y = point_ref[1, rows, :] - centroid_y
            delta_z = point_ref[2, rows, :] - centroid_z
            distance = jnp.sqrt(delta_x * delta_x + delta_y * delta_y + delta_z * delta_z)
            inverse = 1.0 / (FOUR_PI * distance)
            sine, cosine = sine_cosine(WAVENUMBER * distance)
            cosine_ref[chunk, rows, :] = cosine * inverse
            sine_ref[chunk, rows, :] = sine * inverse
        return carry

    lax.fori_loop(0, cosine_ref.shape[0], body, 0)


def point_lanes(coordinate_ref, point_ref):
    for axis in range(3):
        row = coordinate_ref[axis:axis + 1, :]
        point_ref[axis] = jnp.broadcast_to(row, (point_ref.shape[2], point_ref.shape[1])).T


def finish_kernel(velocity_ref, area_ref, panel_ref, coordinate_ref, cosine_hbm, sine_hbm, out_ref,
                  cosine_buf, sine_buf, point_ref, real_ref, imag_ref, sems):
    stored = cosine_hbm.shape[0]
    chunks = panel_ref.shape[0]
    points = point_ref.shape[1]
    groups = stored // PARTS_STEP

    def copies(group):
        window = pl.ds(group * PARTS_STEP, PARTS_STEP)
        return (
            pltpu.make_async_copy(cosine_hbm.at[window], cosine_buf.at[window], sems.at[0, group]),
            pltpu.make_async_copy(sine_hbm.at[window], sine_buf.at[window], sems.at[1, group]),
        )

    for group in range(groups):
        for copy in copies(group):
            copy.start()
    point_lanes(coordinate_ref, point_ref)
    real_ref[...] = jnp.zeros_like(real_ref)
    imag_ref[...] = jnp.zeros_like(imag_ref)

    def strengths(chunk, shape):
        velocity = velocity_ref[chunk]
        area = area_ref[chunk]
        strength_re = jnp.broadcast_to(-area[0:1] * velocity[1:2], shape)
        strength_im = jnp.broadcast_to(area[0:1] * velocity[0:1], shape)
        return strength_re, strength_im

    def fresh(chunk, carry):
        block = panel_ref[chunk]
        shape = (GROUP, block.shape[1])
        strength_re, strength_im = strengths(chunk, shape)
        centroid_x = jnp.broadcast_to(block[2:3], shape)
        centroid_y = jnp.broadcast_to(block[3:4], shape)
        centroid_z = jnp.broadcast_to(block[4:5], shape)
        for group in range(points // GROUP):
            rows = pl.ds(group * GROUP, GROUP)
            delta_x = point_ref[0, rows, :] - centroid_x
            delta_y = point_ref[1, rows, :] - centroid_y
            delta_z = point_ref[2, rows, :] - centroid_z
            distance = jnp.sqrt(delta_x * delta_x + delta_y * delta_y + delta_z * delta_z)
            inverse = 1.0 / (FOUR_PI * distance)
            sine, cosine = sine_cosine(WAVENUMBER * distance)
            cosine_part = cosine * inverse
            sine_part = sine * inverse
            real_ref[rows, :] += strength_re * cosine_part - strength_im * sine_part
            imag_ref[rows, :] += strength_re * sine_part + strength_im * cosine_part
        return carry

    lax.fori_loop(stored, chunks, fresh, 0)

    def saved(chunk, carry):
        strength_re, strength_im = strengths(chunk, real_ref.shape)
        cosine_part = cosine_buf[chunk]
        sine_part = sine_buf[chunk]
        real_ref[...] += strength_re * cosine_part - strength_im * sine_part
        imag_ref[...] += strength_re * sine_part + strength_im * cosine_part
        return carry

    for group in range(groups):
        for copy in copies(group):
            copy.wait()
        lax.fori_loop(group * PARTS_STEP, (group + 1) * PARTS_STEP, saved, 0)
    out_ref[0:1, :] = jnp.sum(real_ref[...].T, axis=0, keepdims=True)
    out_ref[1:2, :] = jnp.sum(imag_ref[...].T, axis=0, keepdims=True)


def kernel_parts(panels, field_points, chunks):
    rows, lanes = panels.shape[1:]
    points = field_points.shape[1]
    pairs = chunks * lanes * points
    part = jax.ShapeDtypeStruct((chunks, points, lanes), jnp.float32)
    return pl.pallas_call(
        parts_kernel,
        out_shape=(part, part),
        grid=(chunks // PARTS_STEP,),
        in_specs=[pl.BlockSpec(memory_space=pltpu.VMEM)] * 2,
        out_specs=[pl.BlockSpec((PARTS_STEP, points, lanes), lambda c: (c, 0, 0))] * 2,
        scratch_shapes=[pltpu.VMEM((3, points, lanes), jnp.float32)],
        compiler_params=pltpu.CompilerParams(dimension_semantics=("arbitrary",)),
        cost_estimate=pl.CostEstimate(flops=60 * pairs, transcendentals=2 * pairs, bytes_accessed=8 * pairs),
    )(
        pltpu.with_memory_space_constraint(panels, pltpu.VMEM),
        pltpu.with_memory_space_constraint(field_points, pltpu.VMEM),
    )


def finish(velocity, area, panels, field_points, cosine_part, sine_part):
    stored, points, lanes = cosine_part.shape
    chunks = panels.shape[0]
    pairs = (chunks - stored) * points * lanes
    vmem = lambda x: pltpu.with_memory_space_constraint(x, pltpu.VMEM)
    return pl.pallas_call(
        finish_kernel,
        out_shape=jax.ShapeDtypeStruct((2, points), jnp.float32),
        in_specs=[pl.BlockSpec(memory_space=pltpu.VMEM)] * 4 + [pl.BlockSpec(memory_space=pl.ANY)] * 2,
        out_specs=pl.BlockSpec(memory_space=pltpu.VMEM),
        scratch_shapes=[pltpu.VMEM((stored, points, lanes), jnp.float32)] * 2
        + [pltpu.VMEM((3, points, lanes), jnp.float32)]
        + [pltpu.VMEM((points, lanes), jnp.float32)] * 2
        + [pltpu.SemaphoreType.DMA((2, stored // PARTS_STEP))],
        cost_estimate=pl.CostEstimate(
            flops=70 * pairs + 8 * stored * points * lanes,
            transcendentals=2 * pairs,
            bytes_accessed=8 * stored * points * lanes,
        ),
    )(vmem(velocity), vmem(area), vmem(panels), vmem(field_points), cosine_part, sine_part)


def shards(node_velocity, node_owner, node_panel, panel_centroid, panel_area, field_points):
    slab_count = lax.axis_size("panel")
    slab_width = panel_area.shape[0]
    destination = node_owner[:, 0]
    owner_hot = (destination[None, :] == jnp.arange(slab_count, dtype=jnp.int32)[:, None]).astype(
        jnp.float32
    )
    weighted = (node_velocity[:, None, :] * owner_hot[None, :, :]).reshape(2 * slab_count, -1)
    panel_hot = (node_panel[:, None] == jnp.arange(slab_width, dtype=jnp.int32)[None, :]).astype(
        jnp.float32
    )
    partial = jnp.dot(
        weighted, panel_hot, precision=lax.Precision.HIGHEST, preferred_element_type=jnp.float32
    )
    partial = partial.reshape(2, slab_count, slab_width).transpose(1, 0, 2)
    extra = jnp.concatenate([panel_centroid, panel_area[None]], axis=0)
    extra_copies = jnp.broadcast_to(extra[None], (slab_count,) + extra.shape)
    outgoing = jnp.concatenate([partial, extra_copies], axis=1)
    got = lax.all_to_all(outgoing, "panel", split_axis=0, concat_axis=0, tiled=True)
    cosine_part, sine_part = kernel_parts(got, field_points, STORED_CHUNKS)
    column = jnp.sum(got[:, 0:2], axis=0)
    point_count = lax.axis_size("point")
    copies = jnp.broadcast_to(column[None], (point_count,) + column.shape)
    velocity = jnp.sum(lax.all_to_all(copies, "point", split_axis=0, concat_axis=0, tiled=True), axis=0)
    spread = jnp.broadcast_to(velocity[None], (slab_count,) + velocity.shape)
    gathered = lax.all_to_all(spread, "panel", split_axis=0, concat_axis=0, tiled=True)
    return finish(gathered, got[:, 5:6], got, field_points, cosine_part, sine_part)


def solution(mesh):
    return jax.shard_map(
        shards,
        mesh=mesh,
        in_specs=(
            P(None, ("panel", "point")),
            P(("panel", "point"), None),
            P(("panel", "point")),
            P(None, "panel"),
            P("panel"),
            P(None, ("panel", "point")),
        ),
        out_specs=P(None, ("panel", "point")),
        check_vma=False,
    )
```

```python
import functools
import math

import jax
import jax.numpy as jnp
from jax import lax
from jax.experimental import pallas as pl
from jax.experimental.pallas import tpu as pltpu
from jax.sharding import PartitionSpec as P

WAVENUMBER = 40.0
FOUR_PI = 4.0 * math.pi


TWO_OVER_PI = 2.0 / math.pi
HALF_PI_1 = 1.5703125
HALF_PI_2 = 4.837512969970703125e-4
HALF_PI_3 = 7.54978995489188216e-8
GROUP = 16
PARTS_STEP = 8
NEAR_CHUNKS = 8
FAR_CHUNKS = 48


def sine_cosine(angle):
    turns = jnp.floor(angle * TWO_OVER_PI + 0.5)
    rest = ((angle - turns * HALF_PI_1) - turns * HALF_PI_2) - turns * HALF_PI_3
    square = rest * rest
    sine = rest + rest * square * (
        -1.6666654611e-1 + square * (8.3321608736e-3 + square * -1.9515295891e-4)
    )
    cosine = 1.0 - 0.5 * square + square * square * (
        4.166664568298827e-2 + square * (-1.388731625493765e-3 + square * 2.443315711809948e-5)
    )
    quadrant = turns.astype(jnp.int32)
    swap = (quadrant & 1) == 1
    sine_out = jnp.where(swap, cosine, sine)
    cosine_out = jnp.where(swap, sine, cosine)
    sine_out = jnp.where((quadrant & 2) == 2, -sine_out, sine_out)
    cosine_out = jnp.where(((quadrant + 1) & 2) == 2, -cosine_out, cosine_out)
    return sine_out, cosine_out


def green_kernel(panel_ref, point_ref, out_ref, total_ref):
    chunks = panel_ref.shape[0]
    points = point_ref.shape[1]
    for group in range(points // GROUP):
        rows = pl.ds(group * GROUP, GROUP)
        point_x = point_ref[0, rows, :]
        point_y = point_ref[1, rows, :]
        point_z = point_ref[2, rows, :]

        def body(chunk, carry):
            real_sum, imag_sum = carry
            block = panel_ref[chunk]
            shape = (GROUP, block.shape[1])
            strength_re = jnp.broadcast_to(block[0:1], shape)
            strength_im = jnp.broadcast_to(block[1:2], shape)
            delta_x = point_x - jnp.broadcast_to(block[2:3], shape)
            delta_y = point_y - jnp.broadcast_to(block[3:4], shape)
            delta_z = point_z - jnp.broadcast_to(block[4:5], shape)
            distance = jnp.sqrt(delta_x * delta_x + delta_y * delta_y + delta_z * delta_z)
            inverse = 1.0 / (FOUR_PI * distance)
            sine, cosine = sine_cosine(WAVENUMBER * distance)
            cosine_part = cosine * inverse
            sine_part = sine * inverse
            real_sum = real_sum + (strength_re * cosine_part - strength_im * sine_part)
            imag_sum = imag_sum + (strength_re * sine_part + strength_im * cosine_part)
            return real_sum, imag_sum

        zero = jnp.zeros((GROUP, panel_ref.shape[2]), jnp.float32)
        real_sum, imag_sum = lax.fori_loop(0, chunks, body, (zero, zero), unroll=2)
        total_ref[0, rows, :] = real_sum
        total_ref[1, rows, :] = imag_sum
    out_ref[0:1, :] = jnp.sum(total_ref[0].T, axis=0, keepdims=True)
    out_ref[1:2, :] = jnp.sum(total_ref[1].T, axis=0, keepdims=True)


def green(panels, field_points):
    points = field_points.shape[1]
    lanes = panels.shape[2]
    spread = jnp.broadcast_to(field_points[:, :, None], (3, points, lanes))
    pairs = panels.shape[0] * lanes * points
    return pl.pallas_call(
        green_kernel,
        out_shape=jax.ShapeDtypeStruct((2, points), jnp.float32),
        in_specs=[pl.BlockSpec(memory_space=pltpu.VMEM)] * 2,
        out_specs=pl.BlockSpec(memory_space=pltpu.VMEM),
        scratch_shapes=[pltpu.VMEM((2, points, lanes), jnp.float32)],
        cost_estimate=pl.CostEstimate(flops=70 * pairs, transcendentals=2 * pairs, bytes_accessed=4 * (panels.size + spread.size + 2 * points)),
    )(panels, spread)


def parts_kernel(offset, panel_ref, coordinate_ref, cosine_ref, sine_ref, point_ref):
    points = point_ref.shape[1]

    @pl.when(pl.program_id(0) == 0)
    def _():
        point_lanes(coordinate_ref, point_ref)

    first = offset + pl.program_id(0) * cosine_ref.shape[0]

    def body(chunk, carry):
        block = panel_ref[first + chunk]
        shape = (GROUP, block.shape[1])
        centroid_x = jnp.broadcast_to(block[2:3], shape)
        centroid_y = jnp.broadcast_to(block[3:4], shape)
        centroid_z = jnp.broadcast_to(block[4:5], shape)
        for group in range(points // GROUP):
            rows = pl.ds(group * GROUP, GROUP)
            delta_x = point_ref[0, rows, :] - centroid_x
            delta_y = point_ref[1, rows, :] - centroid_y
            delta_z = point_ref[2, rows, :] - centroid_z
            distance = jnp.sqrt(delta_x * delta_x + delta_y * delta_y + delta_z * delta_z)
            inverse = 1.0 / (FOUR_PI * distance)
            sine, cosine = sine_cosine(WAVENUMBER * distance)
            cosine_ref[chunk, rows, :] = cosine * inverse
            sine_ref[chunk, rows, :] = sine * inverse
        return carry

    lax.fori_loop(0, cosine_ref.shape[0], body, 0)


def point_lanes(coordinate_ref, point_ref):
    for axis in range(3):
        row = coordinate_ref[axis:axis + 1, :]
        point_ref[axis] = jnp.broadcast_to(row, (point_ref.shape[2], point_ref.shape[1])).T


def finish_kernel(velocity_ref, area_ref, panel_ref, coordinate_ref, cosine_near, sine_near, cosine_hbm, sine_hbm,
                  out_ref, cosine_buf, sine_buf, point_ref, real_ref, imag_ref, sems):
    near = cosine_near.shape[0]
    far = cosine_hbm.shape[0]
    chunks = panel_ref.shape[0]
    points = point_ref.shape[1]
    groups = far // PARTS_STEP

    def copies(group):
        window = pl.ds(group * PARTS_STEP, PARTS_STEP)
        return (
            pltpu.make_async_copy(cosine_hbm.at[window], cosine_buf.at[window], sems.at[0, group]),
            pltpu.make_async_copy(sine_hbm.at[window], sine_buf.at[window], sems.at[1, group]),
        )

    for group in range(groups):
        for copy in copies(group):
            copy.start()
    point_lanes(coordinate_ref, point_ref)
    real_ref[...] = jnp.zeros_like(real_ref)
    imag_ref[...] = jnp.zeros_like(imag_ref)

    def strengths(chunk, shape):
        velocity = velocity_ref[chunk]
        area = area_ref[chunk]
        strength_re = jnp.broadcast_to(-area[0:1] * velocity[1:2], shape)
        strength_im = jnp.broadcast_to(area[0:1] * velocity[0:1], shape)
        return strength_re, strength_im

    def fresh(chunk, carry):
        block = panel_ref[chunk]
        shape = (GROUP, block.shape[1])
        strength_re, strength_im = strengths(chunk, shape)
        centroid_x = jnp.broadcast_to(block[2:3], shape)
        centroid_y = jnp.broadcast_to(block[3:4], shape)
        centroid_z = jnp.broadcast_to(block[4:5], shape)
        for group in range(points // GROUP):
            rows = pl.ds(group * GROUP, GROUP)
            delta_x = point_ref[0, rows, :] - centroid_x
            delta_y = point_ref[1, rows, :] - centroid_y
            delta_z = point_ref[2, rows, :] - centroid_z
            distance = jnp.sqrt(delta_x * delta_x + delta_y * delta_y + delta_z * delta_z)
            inverse = 1.0 / (FOUR_PI * distance)
            sine, cosine = sine_cosine(WAVENUMBER * distance)
            cosine_part = cosine * inverse
            sine_part = sine * inverse
            real_ref[rows, :] += strength_re * cosine_part - strength_im * sine_part
            imag_ref[rows, :] += strength_re * sine_part + strength_im * cosine_part
        return carry

    lax.fori_loop(near + far, chunks, fresh, 0)

    def saved(cosine_src, sine_src, base):
        def body(chunk, carry):
            strength_re, strength_im = strengths(chunk, real_ref.shape)
            cosine_part = cosine_src[chunk - base]
            sine_part = sine_src[chunk - base]
            real_ref[...] += strength_re * cosine_part - strength_im * sine_part
            imag_ref[...] += strength_re * sine_part + strength_im * cosine_part
            return carry

        return body

    lax.fori_loop(0, near, saved(cosine_near, sine_near, 0), 0)
    for group in range(groups):
        for copy in copies(group):
            copy.wait()
        start = near + group * PARTS_STEP
        lax.fori_loop(start, start + PARTS_STEP, saved(cosine_buf, sine_buf, near), 0)
    out_ref[0:1, :] = jnp.sum(real_ref[...].T, axis=0, keepdims=True)
    out_ref[1:2, :] = jnp.sum(imag_ref[...].T, axis=0, keepdims=True)


def kernel_parts(panels, field_points, offset, chunks):
    rows, lanes = panels.shape[1:]
    points = field_points.shape[1]
    pairs = chunks * lanes * points
    part = jax.ShapeDtypeStruct((chunks, points, lanes), jnp.float32)
    return pl.pallas_call(
        functools.partial(parts_kernel, offset),
        out_shape=(part, part),
        grid=(chunks // PARTS_STEP,),
        in_specs=[pl.BlockSpec(memory_space=pltpu.VMEM)] * 2,
        out_specs=[pl.BlockSpec((PARTS_STEP, points, lanes), lambda c: (c, 0, 0))] * 2,
        scratch_shapes=[pltpu.VMEM((3, points, lanes), jnp.float32)],
        compiler_params=pltpu.CompilerParams(dimension_semantics=("arbitrary",)),
        cost_estimate=pl.CostEstimate(flops=60 * pairs, transcendentals=2 * pairs, bytes_accessed=8 * pairs),
    )(
        pltpu.with_memory_space_constraint(panels, pltpu.VMEM),
        pltpu.with_memory_space_constraint(field_points, pltpu.VMEM),
    )


def finish(velocity, area, panels, field_points, near_parts, far_parts):
    (cosine_near, sine_near), (cosine_far, sine_far) = near_parts, far_parts
    far, points, lanes = cosine_far.shape
    chunks = panels.shape[0]
    stored = far + cosine_near.shape[0]
    pairs = (chunks - stored) * points * lanes
    vmem = lambda x: pltpu.with_memory_space_constraint(x, pltpu.VMEM)
    return pl.pallas_call(
        finish_kernel,
        out_shape=jax.ShapeDtypeStruct((2, points), jnp.float32),
        in_specs=[pl.BlockSpec(memory_space=pltpu.VMEM)] * 6 + [pl.BlockSpec(memory_space=pl.ANY)] * 2,
        out_specs=pl.BlockSpec(memory_space=pltpu.VMEM),
        scratch_shapes=[pltpu.VMEM((far, points, lanes), jnp.float32)] * 2
        + [pltpu.VMEM((3, points, lanes), jnp.float32)]
        + [pltpu.VMEM((points, lanes), jnp.float32)] * 2
        + [pltpu.SemaphoreType.DMA((2, far // PARTS_STEP))],
        cost_estimate=pl.CostEstimate(
            flops=70 * pairs + 8 * stored * points * lanes,
            transcendentals=2 * pairs,
            bytes_accessed=8 * far * points * lanes,
        ),
    )(
        vmem(velocity), vmem(area), vmem(panels), vmem(field_points),
        vmem(cosine_near), vmem(sine_near), cosine_far, sine_far,
    )


def shards(node_velocity, node_owner, node_panel, panel_centroid, panel_area, field_points):
    slab_count = lax.axis_size("panel")
    slab_width = panel_area.shape[0]
    destination = node_owner[:, 0]
    owner_hot = (destination[None, :] == jnp.arange(slab_count, dtype=jnp.int32)[:, None]).astype(
        jnp.float32
    )
    weighted = (node_velocity[:, None, :] * owner_hot[None, :, :]).reshape(2 * slab_count, -1)
    panel_hot = (node_panel[:, None] == jnp.arange(slab_width, dtype=jnp.int32)[None, :]).astype(
        jnp.float32
    )
    partial = jnp.dot(
        weighted, panel_hot, precision=lax.Precision.HIGHEST, preferred_element_type=jnp.float32
    )
    partial = partial.reshape(2, slab_count, slab_width).transpose(1, 0, 2)
    extra = jnp.concatenate([panel_centroid, panel_area[None]], axis=0)
    extra_copies = jnp.broadcast_to(extra[None], (slab_count,) + extra.shape)
    outgoing = jnp.concatenate([partial, extra_copies], axis=1)
    got = lax.all_to_all(outgoing, "panel", split_axis=0, concat_axis=0, tiled=True)
    near_parts = kernel_parts(got, field_points, 0, NEAR_CHUNKS)
    far_parts = kernel_parts(got, field_points, NEAR_CHUNKS, FAR_CHUNKS)
    column = jnp.sum(got[:, 0:2], axis=0)
    point_count = lax.axis_size("point")
    copies = jnp.broadcast_to(column[None], (point_count,) + column.shape)
    velocity = jnp.sum(lax.all_to_all(copies, "point", split_axis=0, concat_axis=0, tiled=True), axis=0)
    spread = jnp.broadcast_to(velocity[None], (slab_count,) + velocity.shape)
    gathered = lax.all_to_all(spread, "panel", split_axis=0, concat_axis=0, tiled=True)
    return finish(gathered, got[:, 5:6], got, field_points, near_parts, far_parts)


def solution(mesh):
    return jax.shard_map(
        shards,
        mesh=mesh,
        in_specs=(
            P(None, ("panel", "point")),
            P(("panel", "point"), None),
            P(("panel", "point")),
            P(None, "panel"),
            P("panel"),
            P(None, ("panel", "point")),
        ),
        out_specs=P(None, ("panel", "point")),
        check_vma=False,
    )
```

```python
import functools
import math

import jax
import jax.numpy as jnp
from jax import lax
from jax.experimental import pallas as pl
from jax.experimental.pallas import tpu as pltpu
from jax.sharding import PartitionSpec as P

WAVENUMBER = 40.0
FOUR_PI = 4.0 * math.pi


TWO_OVER_PI = 2.0 / math.pi
HALF_PI_1 = 1.5703125
HALF_PI_2 = 4.837512969970703125e-4
HALF_PI_3 = 7.54978995489188216e-8
GROUP = 16
PARTS_STEP = 8
NEAR_CHUNKS = 16
FAR_CHUNKS = 40


def sine_cosine(angle):
    turns = jnp.floor(angle * TWO_OVER_PI + 0.5)
    rest = ((angle - turns * HALF_PI_1) - turns * HALF_PI_2) - turns * HALF_PI_3
    square = rest * rest
    sine = rest + rest * square * (
        -1.6666654611e-1 + square * (8.3321608736e-3 + square * -1.9515295891e-4)
    )
    cosine = 1.0 - 0.5 * square + square * square * (
        4.166664568298827e-2 + square * (-1.388731625493765e-3 + square * 2.443315711809948e-5)
    )
    quadrant = turns.astype(jnp.int32)
    swap = (quadrant & 1) == 1
    sine_out = jnp.where(swap, cosine, sine)
    cosine_out = jnp.where(swap, sine, cosine)
    sine_out = jnp.where((quadrant & 2) == 2, -sine_out, sine_out)
    cosine_out = jnp.where(((quadrant + 1) & 2) == 2, -cosine_out, cosine_out)
    return sine_out, cosine_out


def green_kernel(panel_ref, point_ref, out_ref, total_ref):
    chunks = panel_ref.shape[0]
    points = point_ref.shape[1]
    for group in range(points // GROUP):
        rows = pl.ds(group * GROUP, GROUP)
        point_x = point_ref[0, rows, :]
        point_y = point_ref[1, rows, :]
        point_z = point_ref[2, rows, :]

        def body(chunk, carry):
            real_sum, imag_sum = carry
            block = panel_ref[chunk]
            shape = (GROUP, block.shape[1])
            strength_re = jnp.broadcast_to(block[0:1], shape)
            strength_im = jnp.broadcast_to(block[1:2], shape)
            delta_x = point_x - jnp.broadcast_to(block[2:3], shape)
            delta_y = point_y - jnp.broadcast_to(block[3:4], shape)
            delta_z = point_z - jnp.broadcast_to(block[4:5], shape)
            distance = jnp.sqrt(delta_x * delta_x + delta_y * delta_y + delta_z * delta_z)
            inverse = 1.0 / (FOUR_PI * distance)
            sine, cosine = sine_cosine(WAVENUMBER * distance)
            cosine_part = cosine * inverse
            sine_part = sine * inverse
            real_sum = real_sum + (strength_re * cosine_part - strength_im * sine_part)
            imag_sum = imag_sum + (strength_re * sine_part + strength_im * cosine_part)
            return real_sum, imag_sum

        zero = jnp.zeros((GROUP, panel_ref.shape[2]), jnp.float32)
        real_sum, imag_sum = lax.fori_loop(0, chunks, body, (zero, zero), unroll=2)
        total_ref[0, rows, :] = real_sum
        total_ref[1, rows, :] = imag_sum
    out_ref[0:1, :] = jnp.sum(total_ref[0].T, axis=0, keepdims=True)
    out_ref[1:2, :] = jnp.sum(total_ref[1].T, axis=0, keepdims=True)


def green(panels, field_points):
    points = field_points.shape[1]
    lanes = panels.shape[2]
    spread = jnp.broadcast_to(field_points[:, :, None], (3, points, lanes))
    pairs = panels.shape[0] * lanes * points
    return pl.pallas_call(
        green_kernel,
        out_shape=jax.ShapeDtypeStruct((2, points), jnp.float32),
        in_specs=[pl.BlockSpec(memory_space=pltpu.VMEM)] * 2,
        out_specs=pl.BlockSpec(memory_space=pltpu.VMEM),
        scratch_shapes=[pltpu.VMEM((2, points, lanes), jnp.float32)],
        cost_estimate=pl.CostEstimate(flops=70 * pairs, transcendentals=2 * pairs, bytes_accessed=4 * (panels.size + spread.size + 2 * points)),
    )(panels, spread)


def parts_kernel(offset, panel_ref, coordinate_ref, cosine_ref, sine_ref, point_ref):
    points = point_ref.shape[1]

    @pl.when(pl.program_id(0) == 0)
    def _():
        point_lanes(coordinate_ref, point_ref)

    first = offset + pl.program_id(0) * cosine_ref.shape[0]

    def body(chunk, carry):
        block = panel_ref[first + chunk]
        shape = (GROUP, block.shape[1])
        centroid_x = jnp.broadcast_to(block[2:3], shape)
        centroid_y = jnp.broadcast_to(block[3:4], shape)
        centroid_z = jnp.broadcast_to(block[4:5], shape)
        for group in range(points // GROUP):
            rows = pl.ds(group * GROUP, GROUP)
            delta_x = point_ref[0, rows, :] - centroid_x
            delta_y = point_ref[1, rows, :] - centroid_y
            delta_z = point_ref[2, rows, :] - centroid_z
            distance = jnp.sqrt(delta_x * delta_x + delta_y * delta_y + delta_z * delta_z)
            inverse = 1.0 / (FOUR_PI * distance)
            sine, cosine = sine_cosine(WAVENUMBER * distance)
            cosine_ref[chunk, rows, :] = cosine * inverse
            sine_ref[chunk, rows, :] = sine * inverse
        return carry

    lax.fori_loop(0, cosine_ref.shape[0], body, 0)


def point_lanes(coordinate_ref, point_ref):
    for axis in range(3):
        row = coordinate_ref[axis:axis + 1, :]
        point_ref[axis] = jnp.broadcast_to(row, (point_ref.shape[2], point_ref.shape[1])).T


def finish_kernel(velocity_ref, area_ref, panel_ref, coordinate_ref, cosine_near, sine_near, cosine_hbm, sine_hbm,
                  out_ref, cosine_buf, sine_buf, point_ref, real_ref, imag_ref, sems):
    near = cosine_near.shape[0]
    far = cosine_hbm.shape[0]
    chunks = panel_ref.shape[0]
    points = point_ref.shape[1]
    groups = far // PARTS_STEP

    def copies(group):
        window = pl.ds(group * PARTS_STEP, PARTS_STEP)
        return (
            pltpu.make_async_copy(cosine_hbm.at[window], cosine_buf.at[window], sems.at[0, group]),
            pltpu.make_async_copy(sine_hbm.at[window], sine_buf.at[window], sems.at[1, group]),
        )

    for group in range(groups):
        for copy in copies(group):
            copy.start()
    point_lanes(coordinate_ref, point_ref)
    real_ref[...] = jnp.zeros_like(real_ref)
    imag_ref[...] = jnp.zeros_like(imag_ref)

    def strengths(chunk, shape):
        velocity = velocity_ref[chunk]
        area = area_ref[chunk]
        strength_re = jnp.broadcast_to(-area[0:1] * velocity[1:2], shape)
        strength_im = jnp.broadcast_to(area[0:1] * velocity[0:1], shape)
        return strength_re, strength_im

    def fresh(chunk, carry):
        block = panel_ref[chunk]
        shape = (GROUP, block.shape[1])
        strength_re, strength_im = strengths(chunk, shape)
        centroid_x = jnp.broadcast_to(block[2:3], shape)
        centroid_y = jnp.broadcast_to(block[3:4], shape)
        centroid_z = jnp.broadcast_to(block[4:5], shape)
        for group in range(points // GROUP):
            rows = pl.ds(group * GROUP, GROUP)
            delta_x = point_ref[0, rows, :] - centroid_x
            delta_y = point_ref[1, rows, :] - centroid_y
            delta_z = point_ref[2, rows, :] - centroid_z
            distance = jnp.sqrt(delta_x * delta_x + delta_y * delta_y + delta_z * delta_z)
            inverse = 1.0 / (FOUR_PI * distance)
            sine, cosine = sine_cosine(WAVENUMBER * distance)
            cosine_part = cosine * inverse
            sine_part = sine * inverse
            real_ref[rows, :] += strength_re * cosine_part - strength_im * sine_part
            imag_ref[rows, :] += strength_re * sine_part + strength_im * cosine_part
        return carry

    lax.fori_loop(near + far, chunks, fresh, 0)

    def saved(cosine_src, sine_src, base):
        def body(chunk, carry):
            strength_re, strength_im = strengths(chunk, real_ref.shape)
            cosine_part = cosine_src[chunk - base]
            sine_part = sine_src[chunk - base]
            real_ref[...] += strength_re * cosine_part - strength_im * sine_part
            imag_ref[...] += strength_re * sine_part + strength_im * cosine_part
            return carry

        return body

    lax.fori_loop(0, near, saved(cosine_near, sine_near, 0), 0)
    for group in range(groups):
        for copy in copies(group):
            copy.wait()
        start = near + group * PARTS_STEP
        lax.fori_loop(start, start + PARTS_STEP, saved(cosine_buf, sine_buf, near), 0)
    out_ref[0:1, :] = jnp.sum(real_ref[...].T, axis=0, keepdims=True)
    out_ref[1:2, :] = jnp.sum(imag_ref[...].T, axis=0, keepdims=True)


def kernel_parts(panels, field_points, offset, chunks):
    rows, lanes = panels.shape[1:]
    points = field_points.shape[1]
    pairs = chunks * lanes * points
    part = jax.ShapeDtypeStruct((chunks, points, lanes), jnp.float32)
    return pl.pallas_call(
        functools.partial(parts_kernel, offset),
        out_shape=(part, part),
        grid=(chunks // PARTS_STEP,),
        in_specs=[pl.BlockSpec(memory_space=pltpu.VMEM)] * 2,
        out_specs=[pl.BlockSpec((PARTS_STEP, points, lanes), lambda c: (c, 0, 0))] * 2,
        scratch_shapes=[pltpu.VMEM((3, points, lanes), jnp.float32)],
        compiler_params=pltpu.CompilerParams(dimension_semantics=("arbitrary",)),
        cost_estimate=pl.CostEstimate(flops=60 * pairs, transcendentals=2 * pairs, bytes_accessed=8 * pairs),
    )(
        pltpu.with_memory_space_constraint(panels, pltpu.VMEM),
        pltpu.with_memory_space_constraint(field_points, pltpu.VMEM),
    )


def finish(velocity, area, panels, field_points, near_parts, far_parts):
    (cosine_near, sine_near), (cosine_far, sine_far) = near_parts, far_parts
    far, points, lanes = cosine_far.shape
    chunks = panels.shape[0]
    stored = far + cosine_near.shape[0]
    pairs = (chunks - stored) * points * lanes
    vmem = lambda x: pltpu.with_memory_space_constraint(x, pltpu.VMEM)
    return pl.pallas_call(
        finish_kernel,
        out_shape=jax.ShapeDtypeStruct((2, points), jnp.float32),
        in_specs=[pl.BlockSpec(memory_space=pltpu.VMEM)] * 6 + [pl.BlockSpec(memory_space=pl.ANY)] * 2,
        out_specs=pl.BlockSpec(memory_space=pltpu.VMEM),
        scratch_shapes=[pltpu.VMEM((far, points, lanes), jnp.float32)] * 2
        + [pltpu.VMEM((3, points, lanes), jnp.float32)]
        + [pltpu.VMEM((points, lanes), jnp.float32)] * 2
        + [pltpu.SemaphoreType.DMA((2, far // PARTS_STEP))],
        cost_estimate=pl.CostEstimate(
            flops=70 * pairs + 8 * stored * points * lanes,
            transcendentals=2 * pairs,
            bytes_accessed=8 * far * points * lanes,
        ),
    )(
        vmem(velocity), vmem(area), vmem(panels), vmem(field_points),
        vmem(cosine_near), vmem(sine_near), cosine_far, sine_far,
    )


def shards(node_velocity, node_owner, node_panel, panel_centroid, panel_area, field_points):
    slab_count = lax.axis_size("panel")
    slab_width = panel_area.shape[0]
    destination = node_owner[:, 0]
    owner_hot = (destination[None, :] == jnp.arange(slab_count, dtype=jnp.int32)[:, None]).astype(
        jnp.float32
    )
    weighted = (node_velocity[:, None, :] * owner_hot[None, :, :]).reshape(2 * slab_count, -1)
    panel_hot = (node_panel[:, None] == jnp.arange(slab_width, dtype=jnp.int32)[None, :]).astype(
        jnp.float32
    )
    partial = jnp.dot(
        weighted, panel_hot, precision=lax.Precision.HIGHEST, preferred_element_type=jnp.float32
    )
    partial = partial.reshape(2, slab_count, slab_width).transpose(1, 0, 2)
    extra = jnp.concatenate([panel_centroid, panel_area[None]], axis=0)
    extra_copies = jnp.broadcast_to(extra[None], (slab_count,) + extra.shape)
    outgoing = jnp.concatenate([partial, extra_copies], axis=1)
    got = lax.all_to_all(outgoing, "panel", split_axis=0, concat_axis=0, tiled=True)
    near_parts = kernel_parts(got, field_points, 0, NEAR_CHUNKS)
    far_parts = kernel_parts(got, field_points, NEAR_CHUNKS, FAR_CHUNKS)
    column = jnp.sum(got[:, 0:2], axis=0)
    point_count = lax.axis_size("point")
    copies = jnp.broadcast_to(column[None], (point_count,) + column.shape)
    velocity = jnp.sum(lax.all_to_all(copies, "point", split_axis=0, concat_axis=0, tiled=True), axis=0)
    spread = jnp.broadcast_to(velocity[None], (slab_count,) + velocity.shape)
    gathered = lax.all_to_all(spread, "panel", split_axis=0, concat_axis=0, tiled=True)
    return finish(gathered, got[:, 5:6], got, field_points, near_parts, far_parts)


def solution(mesh):
    return jax.shard_map(
        shards,
        mesh=mesh,
        in_specs=(
            P(None, ("panel", "point")),
            P(("panel", "point"), None),
            P(("panel", "point")),
            P(None, "panel"),
            P("panel"),
            P(None, ("panel", "point")),
        ),
        out_specs=P(None, ("panel", "point")),
        check_vma=False,
    )
```

```python
import functools
import math

import jax
import jax.numpy as jnp
from jax import lax
from jax.experimental import pallas as pl
from jax.experimental.pallas import tpu as pltpu
from jax.sharding import PartitionSpec as P

WAVENUMBER = 40.0
FOUR_PI = 4.0 * math.pi


TWO_OVER_PI = 2.0 / math.pi
HALF_PI_1 = 1.5703125
HALF_PI_2 = 4.837512969970703125e-4
HALF_PI_3 = 7.54978995489188216e-8
GROUP = 16
PARTS_STEP = 8
NEAR_CHUNKS = 16
FAR_CHUNKS = 40


def sine_cosine(angle):
    turns = jnp.floor(angle * TWO_OVER_PI + 0.5)
    rest = ((angle - turns * HALF_PI_1) - turns * HALF_PI_2) - turns * HALF_PI_3
    square = rest * rest
    sine = rest + rest * square * (
        -1.6666654611e-1 + square * (8.3321608736e-3 + square * -1.9515295891e-4)
    )
    cosine = 1.0 - 0.5 * square + square * square * (
        4.166664568298827e-2 + square * (-1.388731625493765e-3 + square * 2.443315711809948e-5)
    )
    quadrant = turns.astype(jnp.int32)
    swap = (quadrant & 1) == 1
    sine_out = jnp.where(swap, cosine, sine)
    cosine_out = jnp.where(swap, sine, cosine)
    sine_out = jnp.where((quadrant & 2) == 2, -sine_out, sine_out)
    cosine_out = jnp.where(((quadrant + 1) & 2) == 2, -cosine_out, cosine_out)
    return sine_out, cosine_out


def green_kernel(panel_ref, point_ref, out_ref, total_ref):
    chunks = panel_ref.shape[0]
    points = point_ref.shape[1]
    for group in range(points // GROUP):
        rows = pl.ds(group * GROUP, GROUP)
        point_x = point_ref[0, rows, :]
        point_y = point_ref[1, rows, :]
        point_z = point_ref[2, rows, :]

        def body(chunk, carry):
            real_sum, imag_sum = carry
            block = panel_ref[chunk]
            shape = (GROUP, block.shape[1])
            strength_re = jnp.broadcast_to(block[0:1], shape)
            strength_im = jnp.broadcast_to(block[1:2], shape)
            delta_x = point_x - jnp.broadcast_to(block[2:3], shape)
            delta_y = point_y - jnp.broadcast_to(block[3:4], shape)
            delta_z = point_z - jnp.broadcast_to(block[4:5], shape)
            distance = jnp.sqrt(delta_x * delta_x + delta_y * delta_y + delta_z * delta_z)
            inverse = 1.0 / (FOUR_PI * distance)
            sine, cosine = sine_cosine(WAVENUMBER * distance)
            cosine_part = cosine * inverse
            sine_part = sine * inverse
            real_sum = real_sum + (strength_re * cosine_part - strength_im * sine_part)
            imag_sum = imag_sum + (strength_re * sine_part + strength_im * cosine_part)
            return real_sum, imag_sum

        zero = jnp.zeros((GROUP, panel_ref.shape[2]), jnp.float32)
        real_sum, imag_sum = lax.fori_loop(0, chunks, body, (zero, zero), unroll=2)
        total_ref[0, rows, :] = real_sum
        total_ref[1, rows, :] = imag_sum
    out_ref[0:1, :] = jnp.sum(total_ref[0].T, axis=0, keepdims=True)
    out_ref[1:2, :] = jnp.sum(total_ref[1].T, axis=0, keepdims=True)


def green(panels, field_points):
    points = field_points.shape[1]
    lanes = panels.shape[2]
    spread = jnp.broadcast_to(field_points[:, :, None], (3, points, lanes))
    pairs = panels.shape[0] * lanes * points
    return pl.pallas_call(
        green_kernel,
        out_shape=jax.ShapeDtypeStruct((2, points), jnp.float32),
        in_specs=[pl.BlockSpec(memory_space=pltpu.VMEM)] * 2,
        out_specs=pl.BlockSpec(memory_space=pltpu.VMEM),
        scratch_shapes=[pltpu.VMEM((2, points, lanes), jnp.float32)],
        cost_estimate=pl.CostEstimate(flops=70 * pairs, transcendentals=2 * pairs, bytes_accessed=4 * (panels.size + spread.size + 2 * points)),
    )(panels, spread)


def parts_kernel(offset, panel_ref, coordinate_ref, cosine_ref, sine_ref, point_ref):
    points = point_ref.shape[1]

    @pl.when(pl.program_id(0) == 0)
    def _():
        point_lanes(coordinate_ref, point_ref)

    first = offset + pl.program_id(0) * cosine_ref.shape[0]

    def body(chunk, carry):
        block = panel_ref[first + chunk]
        shape = (GROUP, block.shape[1])
        centroid_x = jnp.broadcast_to(block[2:3], shape)
        centroid_y = jnp.broadcast_to(block[3:4], shape)
        centroid_z = jnp.broadcast_to(block[4:5], shape)
        for group in range(points // GROUP):
            rows = pl.ds(group * GROUP, GROUP)
            delta_x = point_ref[0, rows, :] - centroid_x
            delta_y = point_ref[1, rows, :] - centroid_y
            delta_z = point_ref[2, rows, :] - centroid_z
            distance = jnp.sqrt(delta_x * delta_x + delta_y * delta_y + delta_z * delta_z)
            inverse = 1.0 / (FOUR_PI * distance)
            sine, cosine = sine_cosine(WAVENUMBER * distance)
            cosine_ref[chunk, rows, :] = cosine * inverse
            sine_ref[chunk, rows, :] = sine * inverse
        return carry

    lax.fori_loop(0, cosine_ref.shape[0], body, 0)


def point_lanes(coordinate_ref, point_ref):
    for axis in range(3):
        row = coordinate_ref[axis:axis + 1, :]
        point_ref[axis] = jnp.broadcast_to(row, (point_ref.shape[2], point_ref.shape[1])).T


def finish_kernel(velocity_ref, area_ref, panel_ref, coordinate_ref, cosine_near, sine_near, cosine_hbm, sine_hbm,
                  out_ref, cosine_buf, sine_buf, point_ref, real_ref, imag_ref, sems):
    near = cosine_near.shape[0]
    far = cosine_hbm.shape[0]
    chunks = panel_ref.shape[0]
    points = point_ref.shape[1]
    groups = far // PARTS_STEP

    def copies(group):
        window = pl.ds(group * PARTS_STEP, PARTS_STEP)
        return (
            pltpu.make_async_copy(cosine_hbm.at[window], cosine_buf.at[window], sems.at[0, group]),
            pltpu.make_async_copy(sine_hbm.at[window], sine_buf.at[window], sems.at[1, group]),
        )

    for group in range(groups):
        for copy in copies(group):
            copy.start()
    point_lanes(coordinate_ref, point_ref)
    real_ref[...] = jnp.zeros_like(real_ref)
    imag_ref[...] = jnp.zeros_like(imag_ref)

    def strengths(chunk, shape):
        velocity = velocity_ref[chunk]
        area = area_ref[chunk]
        strength_re = jnp.broadcast_to(-area[0:1] * velocity[1:2], shape)
        strength_im = jnp.broadcast_to(area[0:1] * velocity[0:1], shape)
        return strength_re, strength_im

    def fresh(chunk, carry):
        block = panel_ref[chunk]
        shape = (GROUP, block.shape[1])
        strength_re, strength_im = strengths(chunk, shape)
        centroid_x = jnp.broadcast_to(block[2:3], shape)
        centroid_y = jnp.broadcast_to(block[3:4], shape)
        centroid_z = jnp.broadcast_to(block[4:5], shape)
        for group in range(points // GROUP):
            rows = pl.ds(group * GROUP, GROUP)
            delta_x = point_ref[0, rows, :] - centroid_x
            delta_y = point_ref[1, rows, :] - centroid_y
            delta_z = point_ref[2, rows, :] - centroid_z
            distance = jnp.sqrt(delta_x * delta_x + delta_y * delta_y + delta_z * delta_z)
            inverse = 1.0 / (FOUR_PI * distance)
            sine, cosine = sine_cosine(WAVENUMBER * distance)
            cosine_part = cosine * inverse
            sine_part = sine * inverse
            real_ref[rows, :] += strength_re * cosine_part - strength_im * sine_part
            imag_ref[rows, :] += strength_re * sine_part + strength_im * cosine_part
        return carry

    lax.fori_loop(near + far, chunks, fresh, 0)

    def saved(cosine_src, sine_src, base):
        def body(chunk, carry):
            strength_re, strength_im = strengths(chunk, real_ref.shape)
            cosine_part = cosine_src[chunk - base]
            sine_part = sine_src[chunk - base]
            real_ref[...] += strength_re * cosine_part - strength_im * sine_part
            imag_ref[...] += strength_re * sine_part + strength_im * cosine_part
            return carry

        return body

    lax.fori_loop(0, near, saved(cosine_near, sine_near, 0), 0)
    for group in range(groups):
        for copy in copies(group):
            copy.wait()
        start = near + group * PARTS_STEP
        lax.fori_loop(start, start + PARTS_STEP, saved(cosine_buf, sine_buf, near), 0)
    out_ref[0:1, :] = jnp.sum(real_ref[...].T, axis=0, keepdims=True)
    out_ref[1:2, :] = jnp.sum(imag_ref[...].T, axis=0, keepdims=True)


def kernel_parts(panels, field_points, offset, chunks):
    rows, lanes = panels.shape[1:]
    points = field_points.shape[1]
    pairs = chunks * lanes * points
    part = jax.ShapeDtypeStruct((chunks, points, lanes), jnp.float32)
    return pl.pallas_call(
        functools.partial(parts_kernel, offset),
        out_shape=(part, part),
        grid=(chunks // PARTS_STEP,),
        in_specs=[pl.BlockSpec(memory_space=pltpu.VMEM)] * 2,
        out_specs=[pl.BlockSpec((PARTS_STEP, points, lanes), lambda c: (c, 0, 0))] * 2,
        scratch_shapes=[pltpu.VMEM((3, points, lanes), jnp.float32)],
        compiler_params=pltpu.CompilerParams(dimension_semantics=("arbitrary",)),
        cost_estimate=pl.CostEstimate(flops=60 * pairs, transcendentals=2 * pairs, bytes_accessed=8 * pairs),
    )(
        pltpu.with_memory_space_constraint(panels, pltpu.VMEM),
        pltpu.with_memory_space_constraint(field_points, pltpu.VMEM),
    )


def finish(velocity, area, panels, field_points, near_parts, far_parts):
    (cosine_near, sine_near), (cosine_far, sine_far) = near_parts, far_parts
    far, points, lanes = cosine_far.shape
    chunks = panels.shape[0]
    stored = far + cosine_near.shape[0]
    pairs = (chunks - stored) * points * lanes
    vmem = lambda x: pltpu.with_memory_space_constraint(x, pltpu.VMEM)
    return pl.pallas_call(
        finish_kernel,
        out_shape=jax.ShapeDtypeStruct((2, points), jnp.float32),
        in_specs=[pl.BlockSpec(memory_space=pltpu.VMEM)] * 6 + [pl.BlockSpec(memory_space=pl.ANY)] * 2,
        out_specs=pl.BlockSpec(memory_space=pltpu.VMEM),
        scratch_shapes=[pltpu.VMEM((far, points, lanes), jnp.float32)] * 2
        + [pltpu.VMEM((3, points, lanes), jnp.float32)]
        + [pltpu.VMEM((points, lanes), jnp.float32)] * 2
        + [pltpu.SemaphoreType.DMA((2, far // PARTS_STEP))],
        cost_estimate=pl.CostEstimate(
            flops=70 * pairs + 8 * stored * points * lanes,
            transcendentals=2 * pairs,
            bytes_accessed=8 * far * points * lanes,
        ),
    )(
        vmem(velocity), vmem(area), vmem(panels), vmem(field_points),
        vmem(cosine_near), vmem(sine_near), cosine_far, sine_far,
    )


def shards(node_velocity, node_owner, node_panel, panel_centroid, panel_area, field_points):
    slab_count = lax.axis_size("panel")
    slab_width = panel_area.shape[0]
    destination = node_owner[:, 0]
    owner_hot = (destination[None, :] == jnp.arange(slab_count, dtype=jnp.int32)[:, None]).astype(
        jnp.float32
    )
    weighted = (node_velocity[:, None, :] * owner_hot[None, :, :]).reshape(2 * slab_count, -1)
    panel_hot = (node_panel[:, None] == jnp.arange(slab_width, dtype=jnp.int32)[None, :]).astype(
        jnp.float32
    )
    partial = jnp.dot(
        weighted, panel_hot, precision=lax.Precision.HIGHEST, preferred_element_type=jnp.float32
    )
    partial = partial.reshape(2, slab_count, slab_width).transpose(1, 0, 2)
    centroid_copies = jnp.broadcast_to(panel_centroid[None], (slab_count,) + panel_centroid.shape)
    area_copies = jnp.broadcast_to(panel_area[None, None], (slab_count, 1, slab_width))
    outgoing = jnp.concatenate([partial, centroid_copies, area_copies], axis=1)
    got = lax.all_to_all(outgoing, "panel", split_axis=0, concat_axis=0, tiled=True)
    near_parts = kernel_parts(got, field_points, 0, NEAR_CHUNKS)
    far_parts = kernel_parts(got, field_points, NEAR_CHUNKS, FAR_CHUNKS)
    column = jnp.sum(got[:, 0:2], axis=0)
    point_count = lax.axis_size("point")
    copies = jnp.broadcast_to(column[None], (point_count,) + column.shape)
    velocity = jnp.sum(lax.all_to_all(copies, "point", split_axis=0, concat_axis=0, tiled=True), axis=0)
    spread = jnp.broadcast_to(velocity[None], (slab_count,) + velocity.shape)
    gathered = lax.all_to_all(spread, "panel", split_axis=0, concat_axis=0, tiled=True)
    return finish(gathered, got[:, 5:6], got, field_points, near_parts, far_parts)


def solution(mesh):
    return jax.shard_map(
        shards,
        mesh=mesh,
        in_specs=(
            P(None, ("panel", "point")),
            P(("panel", "point"), None),
            P(("panel", "point")),
            P(None, "panel"),
            P("panel"),
            P(None, ("panel", "point")),
        ),
        out_specs=P(None, ("panel", "point")),
        check_vma=False,
    )
```

```python
import functools
import math

import jax
import jax.numpy as jnp
from jax import lax
from jax.experimental import pallas as pl
from jax.experimental.pallas import tpu as pltpu
from jax.sharding import PartitionSpec as P

WAVENUMBER = 40.0
FOUR_PI = 4.0 * math.pi


TWO_OVER_PI = 2.0 / math.pi
HALF_PI_1 = 1.5703125
HALF_PI_2 = 4.837512969970703125e-4
HALF_PI_3 = 7.54978995489188216e-8
GROUP = 16
PARTS_STEP = 8
NEAR_CHUNKS = 16
FAR_CHUNKS = 40
FAR_COPY = 40


def sine_cosine(angle):
    turns = jnp.floor(angle * TWO_OVER_PI + 0.5)
    rest = ((angle - turns * HALF_PI_1) - turns * HALF_PI_2) - turns * HALF_PI_3
    square = rest * rest
    sine = rest + rest * square * (
        -1.6666654611e-1 + square * (8.3321608736e-3 + square * -1.9515295891e-4)
    )
    cosine = 1.0 - 0.5 * square + square * square * (
        4.166664568298827e-2 + square * (-1.388731625493765e-3 + square * 2.443315711809948e-5)
    )
    quadrant = turns.astype(jnp.int32)
    swap = (quadrant & 1) == 1
    sine_out = jnp.where(swap, cosine, sine)
    cosine_out = jnp.where(swap, sine, cosine)
    sine_out = jnp.where((quadrant & 2) == 2, -sine_out, sine_out)
    cosine_out = jnp.where(((quadrant + 1) & 2) == 2, -cosine_out, cosine_out)
    return sine_out, cosine_out


def green_kernel(panel_ref, point_ref, out_ref, total_ref):
    chunks = panel_ref.shape[0]
    points = point_ref.shape[1]
    for group in range(points // GROUP):
        rows = pl.ds(group * GROUP, GROUP)
        point_x = point_ref[0, rows, :]
        point_y = point_ref[1, rows, :]
        point_z = point_ref[2, rows, :]

        def body(chunk, carry):
            real_sum, imag_sum = carry
            block = panel_ref[chunk]
            shape = (GROUP, block.shape[1])
            strength_re = jnp.broadcast_to(block[0:1], shape)
            strength_im = jnp.broadcast_to(block[1:2], shape)
            delta_x = point_x - jnp.broadcast_to(block[2:3], shape)
            delta_y = point_y - jnp.broadcast_to(block[3:4], shape)
            delta_z = point_z - jnp.broadcast_to(block[4:5], shape)
            distance = jnp.sqrt(delta_x * delta_x + delta_y * delta_y + delta_z * delta_z)
            inverse = 1.0 / (FOUR_PI * distance)
            sine, cosine = sine_cosine(WAVENUMBER * distance)
            cosine_part = cosine * inverse
            sine_part = sine * inverse
            real_sum = real_sum + (strength_re * cosine_part - strength_im * sine_part)
            imag_sum = imag_sum + (strength_re * sine_part + strength_im * cosine_part)
            return real_sum, imag_sum

        zero = jnp.zeros((GROUP, panel_ref.shape[2]), jnp.float32)
        real_sum, imag_sum = lax.fori_loop(0, chunks, body, (zero, zero), unroll=2)
        total_ref[0, rows, :] = real_sum
        total_ref[1, rows, :] = imag_sum
    out_ref[0:1, :] = jnp.sum(total_ref[0].T, axis=0, keepdims=True)
    out_ref[1:2, :] = jnp.sum(total_ref[1].T, axis=0, keepdims=True)


def green(panels, field_points):
    points = field_points.shape[1]
    lanes = panels.shape[2]
    spread = jnp.broadcast_to(field_points[:, :, None], (3, points, lanes))
    pairs = panels.shape[0] * lanes * points
    return pl.pallas_call(
        green_kernel,
        out_shape=jax.ShapeDtypeStruct((2, points), jnp.float32),
        in_specs=[pl.BlockSpec(memory_space=pltpu.VMEM)] * 2,
        out_specs=pl.BlockSpec(memory_space=pltpu.VMEM),
        scratch_shapes=[pltpu.VMEM((2, points, lanes), jnp.float32)],
        cost_estimate=pl.CostEstimate(flops=70 * pairs, transcendentals=2 * pairs, bytes_accessed=4 * (panels.size + spread.size + 2 * points)),
    )(panels, spread)


def parts_kernel(offset, panel_ref, coordinate_ref, cosine_ref, sine_ref, point_ref):
    points = point_ref.shape[1]

    @pl.when(pl.program_id(0) == 0)
    def _():
        point_lanes(coordinate_ref, point_ref)

    first = offset + pl.program_id(0) * cosine_ref.shape[0]

    def body(chunk, carry):
        block = panel_ref[first + chunk]
        shape = (GROUP, block.shape[1])
        centroid_x = jnp.broadcast_to(block[2:3], shape)
        centroid_y = jnp.broadcast_to(block[3:4], shape)
        centroid_z = jnp.broadcast_to(block[4:5], shape)
        for group in range(points // GROUP):
            rows = pl.ds(group * GROUP, GROUP)
            delta_x = point_ref[0, rows, :] - centroid_x
            delta_y = point_ref[1, rows, :] - centroid_y
            delta_z = point_ref[2, rows, :] - centroid_z
            distance = jnp.sqrt(delta_x * delta_x + delta_y * delta_y + delta_z * delta_z)
            inverse = 1.0 / (FOUR_PI * distance)
            sine, cosine = sine_cosine(WAVENUMBER * distance)
            cosine_ref[chunk, rows, :] = cosine * inverse
            sine_ref[chunk, rows, :] = sine * inverse
        return carry

    lax.fori_loop(0, cosine_ref.shape[0], body, 0)


def point_lanes(coordinate_ref, point_ref):
    for axis in range(3):
        row = coordinate_ref[axis:axis + 1, :]
        point_ref[axis] = jnp.broadcast_to(row, (point_ref.shape[2], point_ref.shape[1])).T


def finish_kernel(velocity_ref, area_ref, panel_ref, coordinate_ref, cosine_near, sine_near, cosine_hbm, sine_hbm,
                  out_ref, cosine_buf, sine_buf, point_ref, real_ref, imag_ref, sems):
    near = cosine_near.shape[0]
    far = cosine_hbm.shape[0]
    chunks = panel_ref.shape[0]
    points = point_ref.shape[1]
    groups = far // FAR_COPY

    def copies(group):
        window = pl.ds(group * FAR_COPY, FAR_COPY)
        return (
            pltpu.make_async_copy(cosine_hbm.at[window], cosine_buf.at[window], sems.at[0, group]),
            pltpu.make_async_copy(sine_hbm.at[window], sine_buf.at[window], sems.at[1, group]),
        )

    for group in range(groups):
        for copy in copies(group):
            copy.start()
    point_lanes(coordinate_ref, point_ref)
    real_ref[...] = jnp.zeros_like(real_ref)
    imag_ref[...] = jnp.zeros_like(imag_ref)

    def strengths(chunk, shape):
        velocity = velocity_ref[chunk]
        area = area_ref[chunk]
        strength_re = jnp.broadcast_to(-area[0:1] * velocity[1:2], shape)
        strength_im = jnp.broadcast_to(area[0:1] * velocity[0:1], shape)
        return strength_re, strength_im

    def fresh(chunk, carry):
        block = panel_ref[chunk]
        shape = (GROUP, block.shape[1])
        strength_re, strength_im = strengths(chunk, shape)
        centroid_x = jnp.broadcast_to(block[2:3], shape)
        centroid_y = jnp.broadcast_to(block[3:4], shape)
        centroid_z = jnp.broadcast_to(block[4:5], shape)
        for group in range(points // GROUP):
            rows = pl.ds(group * GROUP, GROUP)
            delta_x = point_ref[0, rows, :] - centroid_x
            delta_y = point_ref[1, rows, :] - centroid_y
            delta_z = point_ref[2, rows, :] - centroid_z
            distance = jnp.sqrt(delta_x * delta_x + delta_y * delta_y + delta_z * delta_z)
            inverse = 1.0 / (FOUR_PI * distance)
            sine, cosine = sine_cosine(WAVENUMBER * distance)
            cosine_part = cosine * inverse
            sine_part = sine * inverse
            real_ref[rows, :] += strength_re * cosine_part - strength_im * sine_part
            imag_ref[rows, :] += strength_re * sine_part + strength_im * cosine_part
        return carry

    lax.fori_loop(near + far, chunks, fresh, 0)

    def saved(cosine_src, sine_src, base):
        def body(chunk, carry):
            strength_re, strength_im = strengths(chunk, real_ref.shape)
            cosine_part = cosine_src[chunk - base]
            sine_part = sine_src[chunk - base]
            real_ref[...] += strength_re * cosine_part - strength_im * sine_part
            imag_ref[...] += strength_re * sine_part + strength_im * cosine_part
            return carry

        return body

    lax.fori_loop(0, near, saved(cosine_near, sine_near, 0), 0)
    for group in range(groups):
        for copy in copies(group):
            copy.wait()
        start = near + group * FAR_COPY
        lax.fori_loop(start, start + FAR_COPY, saved(cosine_buf, sine_buf, near), 0)
    out_ref[0:1, :] = jnp.sum(real_ref[...].T, axis=0, keepdims=True)
    out_ref[1:2, :] = jnp.sum(imag_ref[...].T, axis=0, keepdims=True)


def kernel_parts(panels, field_points, offset, chunks):
    rows, lanes = panels.shape[1:]
    points = field_points.shape[1]
    pairs = chunks * lanes * points
    part = jax.ShapeDtypeStruct((chunks, points, lanes), jnp.float32)
    return pl.pallas_call(
        functools.partial(parts_kernel, offset),
        out_shape=(part, part),
        grid=(chunks // PARTS_STEP,),
        in_specs=[pl.BlockSpec(memory_space=pltpu.VMEM)] * 2,
        out_specs=[pl.BlockSpec((PARTS_STEP, points, lanes), lambda c: (c, 0, 0))] * 2,
        scratch_shapes=[pltpu.VMEM((3, points, lanes), jnp.float32)],
        compiler_params=pltpu.CompilerParams(dimension_semantics=("arbitrary",)),
        cost_estimate=pl.CostEstimate(flops=60 * pairs, transcendentals=2 * pairs, bytes_accessed=8 * pairs),
    )(
        pltpu.with_memory_space_constraint(panels, pltpu.VMEM),
        pltpu.with_memory_space_constraint(field_points, pltpu.VMEM),
    )


def finish(velocity, area, panels, field_points, near_parts, far_parts):
    (cosine_near, sine_near), (cosine_far, sine_far) = near_parts, far_parts
    far, points, lanes = cosine_far.shape
    chunks = panels.shape[0]
    stored = far + cosine_near.shape[0]
    pairs = (chunks - stored) * points * lanes
    vmem = lambda x: pltpu.with_memory_space_constraint(x, pltpu.VMEM)
    return pl.pallas_call(
        finish_kernel,
        out_shape=jax.ShapeDtypeStruct((2, points), jnp.float32),
        in_specs=[pl.BlockSpec(memory_space=pltpu.VMEM)] * 6 + [pl.BlockSpec(memory_space=pl.ANY)] * 2,
        out_specs=pl.BlockSpec(memory_space=pltpu.VMEM),
        scratch_shapes=[pltpu.VMEM((far, points, lanes), jnp.float32)] * 2
        + [pltpu.VMEM((3, points, lanes), jnp.float32)]
        + [pltpu.VMEM((points, lanes), jnp.float32)] * 2
        + [pltpu.SemaphoreType.DMA((2, far // FAR_COPY))],
        cost_estimate=pl.CostEstimate(
            flops=70 * pairs + 8 * stored * points * lanes,
            transcendentals=2 * pairs,
            bytes_accessed=8 * far * points * lanes,
        ),
    )(
        vmem(velocity), vmem(area), vmem(panels), vmem(field_points),
        vmem(cosine_near), vmem(sine_near), cosine_far, sine_far,
    )


def shards(node_velocity, node_owner, node_panel, panel_centroid, panel_area, field_points):
    slab_count = lax.axis_size("panel")
    slab_width = panel_area.shape[0]
    destination = node_owner[:, 0]
    owner_hot = (destination[None, :] == jnp.arange(slab_count, dtype=jnp.int32)[:, None]).astype(
        jnp.float32
    )
    weighted = (node_velocity[:, None, :] * owner_hot[None, :, :]).reshape(2 * slab_count, -1)
    panel_hot = (node_panel[:, None] == jnp.arange(slab_width, dtype=jnp.int32)[None, :]).astype(
        jnp.float32
    )
    partial = jnp.dot(
        weighted, panel_hot, precision=lax.Precision.HIGHEST, preferred_element_type=jnp.float32
    )
    partial = partial.reshape(2, slab_count, slab_width).transpose(1, 0, 2)
    extra = jnp.concatenate([panel_centroid, panel_area[None]], axis=0)
    extra_copies = jnp.broadcast_to(extra[None], (slab_count,) + extra.shape)
    outgoing = jnp.concatenate([partial, extra_copies], axis=1)
    got = lax.all_to_all(outgoing, "panel", split_axis=0, concat_axis=0, tiled=True)
    near_parts = kernel_parts(got, field_points, 0, NEAR_CHUNKS)
    far_parts = kernel_parts(got, field_points, NEAR_CHUNKS, FAR_CHUNKS)
    column = jnp.sum(got[:, 0:2], axis=0)
    point_count = lax.axis_size("point")
    copies = jnp.broadcast_to(column[None], (point_count,) + column.shape)
    velocity = jnp.sum(lax.all_to_all(copies, "point", split_axis=0, concat_axis=0, tiled=True), axis=0)
    spread = jnp.broadcast_to(velocity[None], (slab_count,) + velocity.shape)
    gathered = lax.all_to_all(spread, "panel", split_axis=0, concat_axis=0, tiled=True)
    return finish(gathered, got[:, 5:6], got, field_points, near_parts, far_parts)


def solution(mesh):
    return jax.shard_map(
        shards,
        mesh=mesh,
        in_specs=(
            P(None, ("panel", "point")),
            P(("panel", "point"), None),
            P(("panel", "point")),
            P(None, "panel"),
            P("panel"),
            P(None, ("panel", "point")),
        ),
        out_specs=P(None, ("panel", "point")),
        check_vma=False,
    )
```

```python
import functools
import math

import jax
import jax.numpy as jnp
from jax import lax
from jax.experimental import pallas as pl
from jax.experimental.pallas import tpu as pltpu
from jax.sharding import PartitionSpec as P

WAVENUMBER = 40.0
FOUR_PI = 4.0 * math.pi


TWO_OVER_PI = 2.0 / math.pi
HALF_PI_1 = 1.5703125
HALF_PI_2 = 4.837512969970703125e-4
HALF_PI_3 = 7.54978995489188216e-8
GROUP = 16
PARTS_STEP = 8
NEAR_CHUNKS = 16
FAR_CHUNKS = 40


def sine_cosine(angle):
    turns = jnp.floor(angle * TWO_OVER_PI + 0.5)
    rest = ((angle - turns * HALF_PI_1) - turns * HALF_PI_2) - turns * HALF_PI_3
    square = rest * rest
    sine = rest + rest * square * (
        -1.6666654611e-1 + square * (8.3321608736e-3 + square * -1.9515295891e-4)
    )
    cosine = 1.0 - 0.5 * square + square * square * (
        4.166664568298827e-2 + square * (-1.388731625493765e-3 + square * 2.443315711809948e-5)
    )
    quadrant = turns.astype(jnp.int32)
    swap = (quadrant & 1) == 1
    sine_out = jnp.where(swap, cosine, sine)
    cosine_out = jnp.where(swap, sine, cosine)
    sine_out = jnp.where((quadrant & 2) == 2, -sine_out, sine_out)
    cosine_out = jnp.where(((quadrant + 1) & 2) == 2, -cosine_out, cosine_out)
    return sine_out, cosine_out


def green_kernel(panel_ref, point_ref, out_ref, total_ref):
    chunks = panel_ref.shape[0]
    points = point_ref.shape[1]
    for group in range(points // GROUP):
        rows = pl.ds(group * GROUP, GROUP)
        point_x = point_ref[0, rows, :]
        point_y = point_ref[1, rows, :]
        point_z = point_ref[2, rows, :]

        def body(chunk, carry):
            real_sum, imag_sum = carry
            block = panel_ref[chunk]
            shape = (GROUP, block.shape[1])
            strength_re = jnp.broadcast_to(block[0:1], shape)
            strength_im = jnp.broadcast_to(block[1:2], shape)
            delta_x = point_x - jnp.broadcast_to(block[2:3], shape)
            delta_y = point_y - jnp.broadcast_to(block[3:4], shape)
            delta_z = point_z - jnp.broadcast_to(block[4:5], shape)
            distance = jnp.sqrt(delta_x * delta_x + delta_y * delta_y + delta_z * delta_z)
            inverse = 1.0 / (FOUR_PI * distance)
            sine, cosine = sine_cosine(WAVENUMBER * distance)
            cosine_part = cosine * inverse
            sine_part = sine * inverse
            real_sum = real_sum + (strength_re * cosine_part - strength_im * sine_part)
            imag_sum = imag_sum + (strength_re * sine_part + strength_im * cosine_part)
            return real_sum, imag_sum

        zero = jnp.zeros((GROUP, panel_ref.shape[2]), jnp.float32)
        real_sum, imag_sum = lax.fori_loop(0, chunks, body, (zero, zero), unroll=2)
        total_ref[0, rows, :] = real_sum
        total_ref[1, rows, :] = imag_sum
    out_ref[0:1, :] = jnp.sum(total_ref[0].T, axis=0, keepdims=True)
    out_ref[1:2, :] = jnp.sum(total_ref[1].T, axis=0, keepdims=True)


def green(panels, field_points):
    points = field_points.shape[1]
    lanes = panels.shape[2]
    spread = jnp.broadcast_to(field_points[:, :, None], (3, points, lanes))
    pairs = panels.shape[0] * lanes * points
    return pl.pallas_call(
        green_kernel,
        out_shape=jax.ShapeDtypeStruct((2, points), jnp.float32),
        in_specs=[pl.BlockSpec(memory_space=pltpu.VMEM)] * 2,
        out_specs=pl.BlockSpec(memory_space=pltpu.VMEM),
        scratch_shapes=[pltpu.VMEM((2, points, lanes), jnp.float32)],
        cost_estimate=pl.CostEstimate(flops=70 * pairs, transcendentals=2 * pairs, bytes_accessed=4 * (panels.size + spread.size + 2 * points)),
    )(panels, spread)


def parts_kernel(offset, panel_ref, coordinate_ref, cosine_ref, sine_ref, point_ref):
    points = point_ref.shape[1]

    @pl.when(pl.program_id(0) == 0)
    def _():
        point_lanes(coordinate_ref, point_ref)

    first = offset + pl.program_id(0) * cosine_ref.shape[0]

    def body(chunk, carry):
        block = panel_ref[first + chunk]
        shape = (GROUP, block.shape[1])
        centroid_x = jnp.broadcast_to(block[2:3], shape)
        centroid_y = jnp.broadcast_to(block[3:4], shape)
        centroid_z = jnp.broadcast_to(block[4:5], shape)
        for group in range(points // GROUP):
            rows = pl.ds(group * GROUP, GROUP)
            delta_x = point_ref[0, rows, :] - centroid_x
            delta_y = point_ref[1, rows, :] - centroid_y
            delta_z = point_ref[2, rows, :] - centroid_z
            distance = jnp.sqrt(delta_x * delta_x + delta_y * delta_y + delta_z * delta_z)
            inverse = 1.0 / (FOUR_PI * distance)
            sine, cosine = sine_cosine(WAVENUMBER * distance)
            cosine_ref[chunk, rows, :] = cosine * inverse
            sine_ref[chunk, rows, :] = sine * inverse
        return carry

    lax.fori_loop(0, cosine_ref.shape[0], body, 0)


def point_lanes(coordinate_ref, point_ref):
    for axis in range(3):
        row = coordinate_ref[axis:axis + 1, :]
        point_ref[axis] = jnp.broadcast_to(row, (point_ref.shape[2], point_ref.shape[1])).T


def finish_kernel(velocity_ref, area_ref, panel_ref, coordinate_ref, cosine_near, sine_near, cosine_hbm, sine_hbm,
                  out_ref, cosine_buf, sine_buf, point_ref, real_ref, imag_ref, sems):
    near = cosine_near.shape[0]
    far = cosine_hbm.shape[0]
    chunks = panel_ref.shape[0]
    points = point_ref.shape[1]
    groups = far // PARTS_STEP

    def copies(group):
        window = pl.ds(group * PARTS_STEP, PARTS_STEP)
        return (
            pltpu.make_async_copy(cosine_hbm.at[window], cosine_buf.at[window], sems.at[0, group]),
            pltpu.make_async_copy(sine_hbm.at[window], sine_buf.at[window], sems.at[1, group]),
        )

    for group in range(groups):
        for copy in copies(group):
            copy.start()
    point_lanes(coordinate_ref, point_ref)
    real_ref[...] = jnp.zeros_like(real_ref)
    imag_ref[...] = jnp.zeros_like(imag_ref)

    def strengths(chunk, shape):
        velocity = velocity_ref[chunk]
        area = area_ref[chunk]
        strength_re = jnp.broadcast_to(-area[0:1] * velocity[1:2], shape)
        strength_im = jnp.broadcast_to(area[0:1] * velocity[0:1], shape)
        return strength_re, strength_im

    def fresh(chunk, carry):
        block = panel_ref[chunk]
        shape = (GROUP, block.shape[1])
        strength_re, strength_im = strengths(chunk, shape)
        centroid_x = jnp.broadcast_to(block[2:3], shape)
        centroid_y = jnp.broadcast_to(block[3:4], shape)
        centroid_z = jnp.broadcast_to(block[4:5], shape)
        for group in range(points // GROUP):
            rows = pl.ds(group * GROUP, GROUP)
            delta_x = point_ref[0, rows, :] - centroid_x
            delta_y = point_ref[1, rows, :] - centroid_y
            delta_z = point_ref[2, rows, :] - centroid_z
            distance = jnp.sqrt(delta_x * delta_x + delta_y * delta_y + delta_z * delta_z)
            inverse = 1.0 / (FOUR_PI * distance)
            sine, cosine = sine_cosine(WAVENUMBER * distance)
            cosine_part = cosine * inverse
            sine_part = sine * inverse
            real_ref[rows, :] += strength_re * cosine_part - strength_im * sine_part
            imag_ref[rows, :] += strength_re * sine_part + strength_im * cosine_part
        return carry

    lax.fori_loop(near + far, chunks, fresh, 0)

    def saved(cosine_src, sine_src, base):
        def body(chunk, carry):
            strength_re, strength_im = strengths(chunk, real_ref.shape)
            cosine_part = cosine_src[chunk - base]
            sine_part = sine_src[chunk - base]
            real_ref[...] += strength_re * cosine_part - strength_im * sine_part
            imag_ref[...] += strength_re * sine_part + strength_im * cosine_part
            return carry

        return body

    lax.fori_loop(0, near, saved(cosine_near, sine_near, 0), 0)
    for group in range(groups):
        for copy in copies(group):
            copy.wait()
        start = near + group * PARTS_STEP
        lax.fori_loop(start, start + PARTS_STEP, saved(cosine_buf, sine_buf, near), 0)
    out_ref[0:1, :] = jnp.sum(real_ref[...].T, axis=0, keepdims=True)
    out_ref[1:2, :] = jnp.sum(imag_ref[...].T, axis=0, keepdims=True)


def kernel_parts(panels, field_points, offset, chunks):
    rows, lanes = panels.shape[1:]
    points = field_points.shape[1]
    pairs = chunks * lanes * points
    part = jax.ShapeDtypeStruct((chunks, points, lanes), jnp.float32)
    return pl.pallas_call(
        functools.partial(parts_kernel, offset),
        out_shape=(part, part),
        grid=(chunks // PARTS_STEP,),
        in_specs=[pl.BlockSpec(memory_space=pltpu.VMEM)] * 2,
        out_specs=[pl.BlockSpec((PARTS_STEP, points, lanes), lambda c: (c, 0, 0))] * 2,
        scratch_shapes=[pltpu.VMEM((3, points, lanes), jnp.float32)],
        compiler_params=pltpu.CompilerParams(dimension_semantics=("arbitrary",)),
        cost_estimate=pl.CostEstimate(flops=60 * pairs, transcendentals=2 * pairs, bytes_accessed=8 * pairs),
    )(
        pltpu.with_memory_space_constraint(panels, pltpu.VMEM),
        pltpu.with_memory_space_constraint(field_points, pltpu.VMEM),
    )


def finish(velocity, area, panels, field_points, near_parts, far_parts):
    (cosine_near, sine_near), (cosine_far, sine_far) = near_parts, far_parts
    far, points, lanes = cosine_far.shape
    chunks = panels.shape[0]
    stored = far + cosine_near.shape[0]
    pairs = (chunks - stored) * points * lanes
    vmem = lambda x: pltpu.with_memory_space_constraint(x, pltpu.VMEM)
    return pl.pallas_call(
        finish_kernel,
        out_shape=jax.ShapeDtypeStruct((2, points), jnp.float32),
        in_specs=[pl.BlockSpec(memory_space=pltpu.VMEM)] * 6 + [pl.BlockSpec(memory_space=pl.ANY)] * 2,
        out_specs=pl.BlockSpec(memory_space=pltpu.VMEM),
        scratch_shapes=[pltpu.VMEM((far, points, lanes), jnp.float32)] * 2
        + [pltpu.VMEM((3, points, lanes), jnp.float32)]
        + [pltpu.VMEM((points, lanes), jnp.float32)] * 2
        + [pltpu.SemaphoreType.DMA((2, far // PARTS_STEP))],
        cost_estimate=pl.CostEstimate(
            flops=70 * pairs + 8 * stored * points * lanes,
            transcendentals=2 * pairs,
            bytes_accessed=8 * far * points * lanes,
        ),
    )(
        vmem(velocity), vmem(area), vmem(panels), vmem(field_points),
        vmem(cosine_near), vmem(sine_near), cosine_far, sine_far,
    )


def shards(node_velocity, node_owner, node_panel, panel_centroid, panel_area, field_points):
    slab_count = lax.axis_size("panel")
    slab_width = panel_area.shape[0]
    destination = node_owner[:, 0]
    owner_hot = (destination[None, :] == jnp.arange(slab_count, dtype=jnp.int32)[:, None]).astype(
        jnp.float32
    )
    weighted = (node_velocity[:, None, :] * owner_hot[None, :, :]).reshape(2 * slab_count, -1)
    panel_hot = (node_panel[:, None] == jnp.arange(slab_width, dtype=jnp.int32)[None, :]).astype(
        jnp.float32
    )
    partial = jnp.dot(
        weighted, panel_hot, precision=lax.Precision.HIGH, preferred_element_type=jnp.float32
    )
    partial = partial.reshape(2, slab_count, slab_width).transpose(1, 0, 2)
    extra = jnp.concatenate([panel_centroid, panel_area[None]], axis=0)
    extra_copies = jnp.broadcast_to(extra[None], (slab_count,) + extra.shape)
    outgoing = jnp.concatenate([partial, extra_copies], axis=1)
    got = lax.all_to_all(outgoing, "panel", split_axis=0, concat_axis=0, tiled=True)
    near_parts = kernel_parts(got, field_points, 0, NEAR_CHUNKS)
    far_parts = kernel_parts(got, field_points, NEAR_CHUNKS, FAR_CHUNKS)
    column = jnp.sum(got[:, 0:2], axis=0)
    point_count = lax.axis_size("point")
    copies = jnp.broadcast_to(column[None], (point_count,) + column.shape)
    velocity = jnp.sum(lax.all_to_all(copies, "point", split_axis=0, concat_axis=0, tiled=True), axis=0)
    spread = jnp.broadcast_to(velocity[None], (slab_count,) + velocity.shape)
    gathered = lax.all_to_all(spread, "panel", split_axis=0, concat_axis=0, tiled=True)
    return finish(gathered, got[:, 5:6], got, field_points, near_parts, far_parts)


def solution(mesh):
    return jax.shard_map(
        shards,
        mesh=mesh,
        in_specs=(
            P(None, ("panel", "point")),
            P(("panel", "point"), None),
            P(("panel", "point")),
            P(None, "panel"),
            P("panel"),
            P(None, ("panel", "point")),
        ),
        out_specs=P(None, ("panel", "point")),
        check_vma=False,
    )
```

```python
import functools
import math

import jax
import jax.numpy as jnp
from jax import lax
from jax.experimental import pallas as pl
from jax.experimental.pallas import tpu as pltpu
from jax.sharding import PartitionSpec as P

WAVENUMBER = 40.0
FOUR_PI = 4.0 * math.pi


TWO_OVER_PI = 2.0 / math.pi
HALF_PI_1 = 1.5703125
HALF_PI_2 = 4.837512969970703125e-4
HALF_PI_3 = 7.54978995489188216e-8
GROUP = 16
PARTS_STEP = 8
NEAR_CHUNKS = 16
FAR_CHUNKS = 40


def sine_cosine(angle):
    turns = jnp.floor(angle * TWO_OVER_PI + 0.5)
    rest = ((angle - turns * HALF_PI_1) - turns * HALF_PI_2) - turns * HALF_PI_3
    square = rest * rest
    sine = rest + rest * square * (
        -1.6666654611e-1 + square * (8.3321608736e-3 + square * -1.9515295891e-4)
    )
    cosine = 1.0 - 0.5 * square + square * square * (
        4.166664568298827e-2 + square * (-1.388731625493765e-3 + square * 2.443315711809948e-5)
    )
    quadrant = turns.astype(jnp.int32)
    swap = (quadrant & 1) == 1
    sine_out = jnp.where(swap, cosine, sine)
    cosine_out = jnp.where(swap, sine, cosine)
    sine_out = jnp.where((quadrant & 2) == 2, -sine_out, sine_out)
    cosine_out = jnp.where(((quadrant + 1) & 2) == 2, -cosine_out, cosine_out)
    return sine_out, cosine_out


def green_kernel(panel_ref, point_ref, out_ref, total_ref):
    chunks = panel_ref.shape[0]
    points = point_ref.shape[1]
    for group in range(points // GROUP):
        rows = pl.ds(group * GROUP, GROUP)
        point_x = point_ref[0, rows, :]
        point_y = point_ref[1, rows, :]
        point_z = point_ref[2, rows, :]

        def body(chunk, carry):
            real_sum, imag_sum = carry
            block = panel_ref[chunk]
            shape = (GROUP, block.shape[1])
            strength_re = jnp.broadcast_to(block[0:1], shape)
            strength_im = jnp.broadcast_to(block[1:2], shape)
            delta_x = point_x - jnp.broadcast_to(block[2:3], shape)
            delta_y = point_y - jnp.broadcast_to(block[3:4], shape)
            delta_z = point_z - jnp.broadcast_to(block[4:5], shape)
            distance = jnp.sqrt(delta_x * delta_x + delta_y * delta_y + delta_z * delta_z)
            inverse = 1.0 / (FOUR_PI * distance)
            sine, cosine = sine_cosine(WAVENUMBER * distance)
            cosine_part = cosine * inverse
            sine_part = sine * inverse
            real_sum = real_sum + (strength_re * cosine_part - strength_im * sine_part)
            imag_sum = imag_sum + (strength_re * sine_part + strength_im * cosine_part)
            return real_sum, imag_sum

        zero = jnp.zeros((GROUP, panel_ref.shape[2]), jnp.float32)
        real_sum, imag_sum = lax.fori_loop(0, chunks, body, (zero, zero), unroll=2)
        total_ref[0, rows, :] = real_sum
        total_ref[1, rows, :] = imag_sum
    out_ref[0:1, :] = jnp.sum(total_ref[0].T, axis=0, keepdims=True)
    out_ref[1:2, :] = jnp.sum(total_ref[1].T, axis=0, keepdims=True)


def green(panels, field_points):
    points = field_points.shape[1]
    lanes = panels.shape[2]
    spread = jnp.broadcast_to(field_points[:, :, None], (3, points, lanes))
    pairs = panels.shape[0] * lanes * points
    return pl.pallas_call(
        green_kernel,
        out_shape=jax.ShapeDtypeStruct((2, points), jnp.float32),
        in_specs=[pl.BlockSpec(memory_space=pltpu.VMEM)] * 2,
        out_specs=pl.BlockSpec(memory_space=pltpu.VMEM),
        scratch_shapes=[pltpu.VMEM((2, points, lanes), jnp.float32)],
        cost_estimate=pl.CostEstimate(flops=70 * pairs, transcendentals=2 * pairs, bytes_accessed=4 * (panels.size + spread.size + 2 * points)),
    )(panels, spread)


def parts_kernel(offset, panel_ref, coordinate_ref, cosine_ref, sine_ref, point_ref):
    points = point_ref.shape[1]

    @pl.when(pl.program_id(0) == 0)
    def _():
        point_lanes(coordinate_ref, point_ref)

    first = offset + pl.program_id(0) * cosine_ref.shape[0]

    def body(chunk, carry):
        block = panel_ref[first + chunk]
        shape = (GROUP, block.shape[1])
        centroid_x = jnp.broadcast_to(block[2:3], shape)
        centroid_y = jnp.broadcast_to(block[3:4], shape)
        centroid_z = jnp.broadcast_to(block[4:5], shape)
        for group in range(points // GROUP):
            rows = pl.ds(group * GROUP, GROUP)
            delta_x = point_ref[0, rows, :] - centroid_x
            delta_y = point_ref[1, rows, :] - centroid_y
            delta_z = point_ref[2, rows, :] - centroid_z
            distance = jnp.sqrt(delta_x * delta_x + delta_y * delta_y + delta_z * delta_z)
            inverse = 1.0 / (FOUR_PI * distance)
            sine, cosine = sine_cosine(WAVENUMBER * distance)
            cosine_ref[chunk, rows, :] = cosine * inverse
            sine_ref[chunk, rows, :] = sine * inverse
        return carry

    lax.fori_loop(0, cosine_ref.shape[0], body, 0)


def point_lanes(coordinate_ref, point_ref):
    for axis in range(3):
        row = coordinate_ref[axis:axis + 1, :]
        point_ref[axis] = jnp.broadcast_to(row, (point_ref.shape[2], point_ref.shape[1])).T


def finish_kernel(velocity_ref, area_ref, panel_ref, coordinate_ref, cosine_near, sine_near, cosine_hbm, sine_hbm,
                  out_ref, cosine_buf, sine_buf, point_ref, real_ref, imag_ref, sems):
    near = cosine_near.shape[0]
    far = cosine_hbm.shape[0]
    chunks = panel_ref.shape[0]
    points = point_ref.shape[1]
    groups = far // PARTS_STEP

    def copies(group):
        window = pl.ds(group * PARTS_STEP, PARTS_STEP)
        return (
            pltpu.make_async_copy(cosine_hbm.at[window], cosine_buf.at[window], sems.at[0, group]),
            pltpu.make_async_copy(sine_hbm.at[window], sine_buf.at[window], sems.at[1, group]),
        )

    for group in range(groups):
        for copy in copies(group):
            copy.start()
    point_lanes(coordinate_ref, point_ref)
    real_ref[...] = jnp.zeros_like(real_ref)
    imag_ref[...] = jnp.zeros_like(imag_ref)

    def strengths(chunk, shape):
        velocity = velocity_ref[chunk]
        area = area_ref[chunk]
        strength_re = jnp.broadcast_to(-area[0:1] * velocity[1:2], shape)
        strength_im = jnp.broadcast_to(area[0:1] * velocity[0:1], shape)
        return strength_re, strength_im

    def fresh(chunk, carry):
        block = panel_ref[chunk]
        shape = (GROUP, block.shape[1])
        strength_re, strength_im = strengths(chunk, shape)
        centroid_x = jnp.broadcast_to(block[2:3], shape)
        centroid_y = jnp.broadcast_to(block[3:4], shape)
        centroid_z = jnp.broadcast_to(block[4:5], shape)
        for group in range(points // GROUP):
            rows = pl.ds(group * GROUP, GROUP)
            delta_x = point_ref[0, rows, :] - centroid_x
            delta_y = point_ref[1, rows, :] - centroid_y
            delta_z = point_ref[2, rows, :] - centroid_z
            distance = jnp.sqrt(delta_x * delta_x + delta_y * delta_y + delta_z * delta_z)
            inverse = 1.0 / (FOUR_PI * distance)
            sine, cosine = sine_cosine(WAVENUMBER * distance)
            cosine_part = cosine * inverse
            sine_part = sine * inverse
            real_ref[rows, :] += strength_re * cosine_part - strength_im * sine_part
            imag_ref[rows, :] += strength_re * sine_part + strength_im * cosine_part
        return carry

    lax.fori_loop(near + far, chunks, fresh, 0)

    def saved(cosine_src, sine_src, base):
        def body(chunk, carry):
            strength_re, strength_im = strengths(chunk, real_ref.shape)
            cosine_part = cosine_src[chunk - base]
            sine_part = sine_src[chunk - base]
            real_ref[...] += strength_re * cosine_part - strength_im * sine_part
            imag_ref[...] += strength_re * sine_part + strength_im * cosine_part
            return carry

        return body

    lax.fori_loop(0, near, saved(cosine_near, sine_near, 0), 0, unroll=2)
    for group in range(groups):
        for copy in copies(group):
            copy.wait()
        start = near + group * PARTS_STEP
        lax.fori_loop(start, start + PARTS_STEP, saved(cosine_buf, sine_buf, near), 0, unroll=2)
    out_ref[0:1, :] = jnp.sum(real_ref[...].T, axis=0, keepdims=True)
    out_ref[1:2, :] = jnp.sum(imag_ref[...].T, axis=0, keepdims=True)


def kernel_parts(panels, field_points, offset, chunks):
    rows, lanes = panels.shape[1:]
    points = field_points.shape[1]
    pairs = chunks * lanes * points
    part = jax.ShapeDtypeStruct((chunks, points, lanes), jnp.float32)
    return pl.pallas_call(
        functools.partial(parts_kernel, offset),
        out_shape=(part, part),
        grid=(chunks // PARTS_STEP,),
        in_specs=[pl.BlockSpec(memory_space=pltpu.VMEM)] * 2,
        out_specs=[pl.BlockSpec((PARTS_STEP, points, lanes), lambda c: (c, 0, 0))] * 2,
        scratch_shapes=[pltpu.VMEM((3, points, lanes), jnp.float32)],
        compiler_params=pltpu.CompilerParams(dimension_semantics=("arbitrary",)),
        cost_estimate=pl.CostEstimate(flops=60 * pairs, transcendentals=2 * pairs, bytes_accessed=8 * pairs),
    )(
        pltpu.with_memory_space_constraint(panels, pltpu.VMEM),
        pltpu.with_memory_space_constraint(field_points, pltpu.VMEM),
    )


def finish(velocity, area, panels, field_points, near_parts, far_parts):
    (cosine_near, sine_near), (cosine_far, sine_far) = near_parts, far_parts
    far, points, lanes = cosine_far.shape
    chunks = panels.shape[0]
    stored = far + cosine_near.shape[0]
    pairs = (chunks - stored) * points * lanes
    vmem = lambda x: pltpu.with_memory_space_constraint(x, pltpu.VMEM)
    return pl.pallas_call(
        finish_kernel,
        out_shape=jax.ShapeDtypeStruct((2, points), jnp.float32),
        in_specs=[pl.BlockSpec(memory_space=pltpu.VMEM)] * 6 + [pl.BlockSpec(memory_space=pl.ANY)] * 2,
        out_specs=pl.BlockSpec(memory_space=pltpu.VMEM),
        scratch_shapes=[pltpu.VMEM((far, points, lanes), jnp.float32)] * 2
        + [pltpu.VMEM((3, points, lanes), jnp.float32)]
        + [pltpu.VMEM((points, lanes), jnp.float32)] * 2
        + [pltpu.SemaphoreType.DMA((2, far // PARTS_STEP))],
        cost_estimate=pl.CostEstimate(
            flops=70 * pairs + 8 * stored * points * lanes,
            transcendentals=2 * pairs,
            bytes_accessed=8 * far * points * lanes,
        ),
    )(
        vmem(velocity), vmem(area), vmem(panels), vmem(field_points),
        vmem(cosine_near), vmem(sine_near), cosine_far, sine_far,
    )


def shards(node_velocity, node_owner, node_panel, panel_centroid, panel_area, field_points):
    slab_count = lax.axis_size("panel")
    slab_width = panel_area.shape[0]
    destination = node_owner[:, 0]
    owner_hot = (destination[None, :] == jnp.arange(slab_count, dtype=jnp.int32)[:, None]).astype(
        jnp.float32
    )
    weighted = (node_velocity[:, None, :] * owner_hot[None, :, :]).reshape(2 * slab_count, -1)
    panel_hot = (node_panel[:, None] == jnp.arange(slab_width, dtype=jnp.int32)[None, :]).astype(
        jnp.float32
    )
    partial = jnp.dot(
        weighted, panel_hot, precision=lax.Precision.HIGHEST, preferred_element_type=jnp.float32
    )
    partial = partial.reshape(2, slab_count, slab_width).transpose(1, 0, 2)
    extra = jnp.concatenate([panel_centroid, panel_area[None]], axis=0)
    extra_copies = jnp.broadcast_to(extra[None], (slab_count,) + extra.shape)
    outgoing = jnp.concatenate([partial, extra_copies], axis=1)
    got = lax.all_to_all(outgoing, "panel", split_axis=0, concat_axis=0, tiled=True)
    near_parts = kernel_parts(got, field_points, 0, NEAR_CHUNKS)
    far_parts = kernel_parts(got, field_points, NEAR_CHUNKS, FAR_CHUNKS)
    column = jnp.sum(got[:, 0:2], axis=0)
    point_count = lax.axis_size("point")
    copies = jnp.broadcast_to(column[None], (point_count,) + column.shape)
    velocity = jnp.sum(lax.all_to_all(copies, "point", split_axis=0, concat_axis=0, tiled=True), axis=0)
    spread = jnp.broadcast_to(velocity[None], (slab_count,) + velocity.shape)
    gathered = lax.all_to_all(spread, "panel", split_axis=0, concat_axis=0, tiled=True)
    return finish(gathered, got[:, 5:6], got, field_points, near_parts, far_parts)


def solution(mesh):
    return jax.shard_map(
        shards,
        mesh=mesh,
        in_specs=(
            P(None, ("panel", "point")),
            P(("panel", "point"), None),
            P(("panel", "point")),
            P(None, "panel"),
            P("panel"),
            P(None, ("panel", "point")),
        ),
        out_specs=P(None, ("panel", "point")),
        check_vma=False,
    )
```
